512 devices in a mesh: head: 16 (over y, core), seq: 32 (over z, x).
Axes of the slice: x: 4, y: 8, z: 8, core: 2. Of those that a mesh axis runs over, the one named last changes fastest.
Arguments:
- queries: bfloat16 [32768, 2048], P(('seq', 'head'))
- keys: bfloat16 [32768, 2048], P(('seq', 'head'))
- values: bfloat16 [32768, 2048], P(('seq', 'head')), may hold values from -6 to 6
- grad_out: bfloat16 [32768, 2048], P(('seq', 'head')), may hold values from -6 to 6
- random_blocks: int32 [256, 3], P('seq'), may hold values from 0 to 255, as said below
Outputs:
- attended: bfloat16 [32768, 2048], P(('seq', 'head'))
- grad_queries: bfloat16 [32768, 2048], P(('seq', 'head'))
- grad_keys: bfloat16 [32768, 2048], P(('seq', 'head'))
- grad_values: bfloat16 [32768, 2048], P(('seq', 'head'))
The draws below stay inside these ranges and needn't reach their ends.
Inputs may be any that keep to these rules, and one draw needn't show every extreme that they name: `random_blocks`: within the rows of one sequence group (8 consecutive query blocks), at most 2 entries name blocks of any one group's range of 8 blocks, and in every group's rows one group's range is named exactly 2 times.
All inputs are finite; a program needn't handle non-finite values.
Results may differ from the reference program's by a relative error of at most 0.022.
Values may be sent and summed in bfloat16 or wider, within the bound.
No kernel may reach another device: no remote copies, remote signals or barrier semaphores. Data moves between devices by JAX's collectives and lax.ppermute only.
A program may use at most 192 MiB of HBM per device.

```python
import jax
import jax.numpy as jnp
from jax import lax

HD = 128
BLK = 128
RAND = 3
HEADS = 16
TOKENS = 32768
QBG = 8
NBLK = 256
CAP = 2


def draw_queries(key, part):
    result = jnp.clip(jax.random.normal(jax.random.fold_in(key, 11), (TOKENS, HEADS * HD), jnp.float32), -6.0, 6.0)
    return result.astype(jnp.bfloat16)


def draw_keys(key, part):
    result = jnp.clip(jax.random.normal(jax.random.fold_in(key, 21), (TOKENS, HEADS * HD), jnp.float32), -6.0, 6.0)
    return result.astype(jnp.bfloat16)


def draw_random_blocks(key, part):
    groups = NBLK // QBG
    slot_count = QBG * RAND

    def one_group(group_index):
        group_key = jax.random.fold_in(key, group_index)
        order = jax.random.permutation(jax.random.fold_in(group_key, 1), slot_count)
        busiest = jax.random.randint(jax.random.fold_in(group_key, 2), (), 0, groups)
        remainder = jnp.arange(slot_count, dtype=jnp.int32) - CAP
        others = (busiest + 1 + jnp.maximum(remainder, 0) % (groups - 1)) % groups
        owner_sorted = jnp.where(remainder < 0, busiest, others).astype(jnp.int32)
        owners = jnp.zeros((slot_count,), jnp.int32).at[order].set(owner_sorted)
        local_ids = jax.random.randint(jax.random.fold_in(group_key, 3), (slot_count,), 0, QBG)
        return (owners * QBG + local_ids).astype(jnp.int32).reshape(QBG, RAND)
    return jax.vmap(one_group)(jnp.arange(groups, dtype=jnp.int32)).reshape(NBLK, RAND)


def steps_of(key, dims, shards, low, high):
    factor_of = 1.0
    for position, parts in shards:
        draws = jax.random.uniform(jax.random.fold_in(jax.random.fold_in(key, 6), position), (parts,), jnp.float32, low / len(shards), high / len(shards))
        factor_of = factor_of * jnp.repeat(jnp.exp(draws), dims[position] // parts).reshape((-1,) + (1,) * (len(dims) - 1 - position))
    return factor_of


def centred(own_key, dims, width, reach, split=(), kind=jnp.bfloat16):
    level = steps_of(own_key, dims, split, -0.22, 0.18) if split else 1.0
    values = jax.random.normal(own_key, dims, jnp.float32) * width * level
    return jnp.minimum(jnp.maximum(values, -reach), reach).astype(kind)


def setup_inputs(seed: int = 0) -> dict:
    streams_of = jax.random.split(jax.random.key(seed), 6)
    queries = draw_queries(jax.random.fold_in(streams_of[5], 71), 0)
    keys = draw_keys(jax.random.fold_in(streams_of[5], 71), 0)
    values = centred(streams_of[2], (TOKENS, HEADS * HD), 1.0, 6.0, ((0, 512),))
    grad_out = centred(streams_of[3], (TOKENS, HEADS * HD), 1.0, 6.0, ((0, 512),))
    random_blocks = draw_random_blocks(jax.random.fold_in(streams_of[5], 71), 0)
    return {"queries": queries, "keys": keys, "values": values, "grad_out": grad_out, "random_blocks": random_blocks}


def reference(queries, keys, values, grad_out, random_blocks):
    block_count = TOKENS // BLK
    score_scale = HD ** -0.5
    block_ids = jnp.arange(block_count, dtype=jnp.int32)
    window_ids = jnp.clip(block_ids[:, None] + jnp.arange(-1, 2, dtype=jnp.int32)[None, :], 0, block_count - 1)
    global_ids = jnp.zeros((block_count, 2), jnp.int32) + jnp.arange(2, dtype=jnp.int32)[None, :]
    random_ids = random_blocks.astype(jnp.int32)
    listed = jnp.concatenate([global_ids, window_ids, random_ids], axis=1)
    all_true = jnp.ones((block_count, 1), dtype=bool)
    slot_ok = jnp.concatenate([all_true, all_true, (block_ids > 0)[:, None], all_true,
                               (block_ids < block_count - 1)[:, None],
                               jnp.ones((block_count, RAND), dtype=bool)], axis=1)
    valid = jnp.repeat(slot_ok, BLK, axis=1)

    def one_head(head):
        def columns(table):
            return lax.dynamic_slice_in_dim(table, head * HD, HD, 1).reshape(block_count, BLK, HD).astype(jnp.float32)

        query_blocks = columns(queries)
        key_blocks = columns(keys)
        value_blocks = columns(values)
        grad_blocks = columns(grad_out)
        key_rows = key_blocks[listed].reshape(block_count, (5 + RAND) * BLK, HD)
        value_rows = value_blocks[listed].reshape(block_count, (5 + RAND) * BLK, HD)
        scores = score_scale * jnp.einsum("bid,bjd->bij", query_blocks, key_rows)
        scores = jnp.where(valid[:, None, :], scores, -jnp.inf)
        row_max = jnp.max(scores, axis=-1, keepdims=True)
        exponent = jnp.exp(scores - row_max)
        attention_probs = exponent / jnp.sum(exponent, axis=-1, keepdims=True)
        weights = lax.optimization_barrier(attention_probs.astype(jnp.bfloat16)).astype(jnp.float32)
        attended = jnp.einsum("bij,bjd->bid", weights, value_rows).astype(jnp.bfloat16)
        grad_prob = jnp.einsum("bid,bjd->bij", grad_blocks, value_rows)
        row_delta = jnp.sum(attention_probs * grad_prob, axis=-1, keepdims=True)
        grad_score = (score_scale * attention_probs * (grad_prob - row_delta)).astype(jnp.bfloat16)
        grad_score = lax.optimization_barrier(grad_score).astype(jnp.float32)
        grad_q = jnp.einsum("bij,bjd->bid", grad_score, key_rows).astype(jnp.bfloat16)
        key_slots = jnp.einsum("bij,bid->bjd", grad_score, query_blocks).reshape(block_count, 5 + RAND, BLK, HD)
        value_slots = jnp.einsum("bij,bid->bjd", weights, grad_blocks).reshape(block_count, 5 + RAND, BLK, HD)

        def collect(slots):
            total = jnp.zeros((block_count, BLK, HD), jnp.float32)
            total = total.at[0:2].add(jnp.sum(slots[:, 0:2], axis=0))
            total = total.at[window_ids.reshape(-1)].add(slots[:, 2:5].reshape(-1, BLK, HD))
            rounded = lax.optimization_barrier(slots[:, 5:].astype(jnp.bfloat16)).astype(jnp.float32)
            total = total.at[random_ids.reshape(-1)].add(rounded.reshape(-1, BLK, HD))
            return total.astype(jnp.bfloat16).reshape(TOKENS, HD)

        return (attended.reshape(TOKENS, HD), grad_q.reshape(TOKENS, HD),
                collect(key_slots), collect(value_slots))

    results = lax.map(one_head, jnp.arange(HEADS, dtype=jnp.int32))

    def regroup(stacked):
        return jnp.transpose(stacked, (1, 0, 2)).reshape(TOKENS, HEADS * HD)

    return (regroup(results[0]), regroup(results[1]), regroup(results[2]), regroup(results[3]))
```

```python
import jax
import jax.numpy as jnp
from jax import lax
from jax.sharding import PartitionSpec as P

HD = 128
BLK = 128
RAND = 3


def with_halo(cells, sides, width):
    for axis, dim in sides:
        count = lax.axis_size(axis)
        ends = count - 1
        head = lax.slice_in_dim(cells, 0, width, axis=dim)
        tail = lax.slice_in_dim(cells, cells.shape[dim] - width, cells.shape[dim], axis=dim)
        cells = jnp.concatenate(
            [
                lax.ppermute(tail, axis, [(i, (i + 1) % count) for i in range(ends)]),
                cells,
                lax.ppermute(head, axis, [((i + 1) % count, i) for i in range(ends)]),
            ],
            axis=dim,
        )
    return cells


def broadcast(value, axis):
    count = lax.axis_size(axis)
    me = lax.axis_index(axis)
    step = 1
    while step < count:
        pairs = [(i, i + step) for i in range(step) if i + step < count]
        got = lax.ppermute(value, axis, pairs)
        value = jnp.where((me >= step) & (me < 2 * step), got, value)
        step *= 2
    return value


def reduce_to_first(value, axis):
    count = lax.axis_size(axis)
    step = 1
    while step * 2 < count:
        step *= 2
    while step >= 1:
        pairs = [(i + step, i) for i in range(step) if i + step < count]
        value = value + lax.ppermute(value, axis, pairs)
        step //= 2
    return value


def slot_places(owners, groups, capacity):
    owner_hits = (owners[:, None] == jnp.arange(groups, dtype=jnp.int32)[None, :]).astype(jnp.int32)
    earlier = jnp.cumsum(owner_hits, axis=0) - owner_hits
    return owners * capacity + jnp.sum(earlier * owner_hits, axis=1)


def request_table(list_rows, query_count, groups, capacity):
    flat_rows = list_rows.reshape(-1)
    places = slot_places(flat_rows // query_count, groups, capacity)
    matches = places[None, :] == jnp.arange(groups * capacity, dtype=jnp.int32)[:, None]
    table = jnp.sum(jnp.where(matches, (flat_rows % query_count)[None, :], 0), axis=1)
    return table.reshape(groups, capacity)


def window_valid(my_group, query_count, groups):
    block_ids = jnp.arange(query_count, dtype=jnp.int32)
    left_ok = jnp.logical_not(jnp.logical_and(my_group == 0, block_ids == 0))
    right_ok = jnp.logical_not(
        jnp.logical_and(my_group == groups - 1, block_ids == query_count - 1)
    )
    all_true = jnp.ones((query_count, BLK), dtype=bool)
    return jnp.concatenate(
        [
            all_true,
            all_true,
            left_ok[:, None] & all_true,
            all_true,
            right_ok[:, None] & all_true,
            jnp.ones((query_count, RAND * BLK), dtype=bool),
        ],
        axis=1,
    )


def against_keys(rows, global_part, window_part, remote_part):
    return jnp.concatenate(
        [
            jnp.einsum("qihd,jhd->qhij", rows, global_part, preferred_element_type=jnp.float32),
            jnp.einsum("qihd,qjhd->qhij", rows, window_part, preferred_element_type=jnp.float32),
            jnp.einsum("qihd,qjhd->qhij", rows, remote_part, preferred_element_type=jnp.float32),
        ],
        axis=-1,
    )


def split_keys(table):
    return (table[..., : 2 * BLK], table[..., 2 * BLK : 5 * BLK], table[..., 5 * BLK :])


def weigh_keys(table, global_part, window_part, remote_part):
    global_w, window_w, random_w = split_keys(table)
    return (
        jnp.einsum("qhij,jhd->qihd", global_w, global_part, preferred_element_type=jnp.float32)
        + jnp.einsum("qhij,qjhd->qihd", window_w, window_part, preferred_element_type=jnp.float32)
        + jnp.einsum("qhij,qjhd->qihd", random_w, remote_part, preferred_element_type=jnp.float32)
    )


def key_terms(table, rows):
    global_w, window_w, random_w = split_keys(table)
    return (
        jnp.einsum("qhij,qihd->jhd", global_w, rows, preferred_element_type=jnp.float32),
        jnp.einsum("qhij,qihd->qjhd", window_w, rows, preferred_element_type=jnp.float32),
        jnp.einsum("qhij,qihd->qjhd", random_w, rows, preferred_element_type=jnp.float32),
    )


def shards(queries, keys, values, grad_out, random_blocks):
    groups = lax.axis_size("seq")
    my_group = lax.axis_index("seq")
    head_q, head_k, head_v, head_g = (
        lax.all_to_all(queries, "head", split_axis=1, concat_axis=0, tiled=True),
        lax.all_to_all(keys, "head", split_axis=1, concat_axis=0, tiled=True),
        lax.all_to_all(values, "head", split_axis=1, concat_axis=0, tiled=True),
        lax.all_to_all(grad_out, "head", split_axis=1, concat_axis=0, tiled=True),
    )
    group_tokens = head_q.shape[0]
    head_count = head_q.shape[1] // HD
    query_count = group_tokens // BLK
    capacity = max(2, 3 * query_count * RAND // (2 * groups))
    score_scale = HD ** (-0.5)
    key_value = jnp.stack([head_k, head_v])
    kv_blocks = key_value.reshape(2, query_count, BLK, head_count, HD)
    edged = with_halo(key_value, (("seq", 1),), BLK)
    edged = edged.reshape(2, query_count + 2, BLK, head_count, HD)
    window_kv = jnp.concatenate(
        [edged[:, 0:query_count], edged[:, 1 : query_count + 1], edged[:, 2 : query_count + 2]],
        axis=2,
    )
    global_kv = broadcast(kv_blocks[:, 0:2].reshape(2, 2 * BLK, head_count, HD), "seq")
    flat_ids = random_blocks.reshape(-1)
    places = slot_places(flat_ids // query_count, groups, capacity)
    wanted = lax.all_to_all(
        request_table(random_blocks, query_count, groups, capacity),
        "seq",
        split_axis=0,
        concat_axis=0,
        tiled=True,
    )
    served = jnp.take(kv_blocks, wanted.reshape(-1), axis=1)
    served = served.reshape(2, groups, capacity, BLK, head_count, HD)
    fetched = lax.all_to_all(served, "seq", split_axis=1, concat_axis=1, tiled=True)
    chosen = jnp.take(fetched.reshape(2, groups * capacity, BLK, head_count, HD), places, axis=1)
    remote_kv = chosen.reshape(2, query_count, RAND * BLK, head_count, HD)
    query_blocks = head_q.reshape(query_count, BLK, head_count, HD)
    grad_blocks = head_g.reshape(query_count, BLK, head_count, HD)
    scores = score_scale * against_keys(query_blocks, global_kv[0], window_kv[0], remote_kv[0])
    valid = window_valid(my_group, query_count, groups)
    scores = jnp.where(valid[:, None, None, :], scores, -jnp.inf)
    row_max = jnp.max(scores, axis=-1, keepdims=True)
    exponent = jnp.exp(scores - row_max)
    attention_probs = exponent / jnp.sum(exponent, axis=-1, keepdims=True)
    weights = attention_probs.astype(jnp.bfloat16)
    attended = weigh_keys(weights, global_kv[1], window_kv[1], remote_kv[1]).astype(jnp.bfloat16)
    grad_prob = against_keys(grad_blocks, global_kv[1], window_kv[1], remote_kv[1])
    row_delta = jnp.sum(attention_probs * grad_prob, axis=-1, keepdims=True)
    grad_score = (score_scale * attention_probs * (grad_prob - row_delta)).astype(jnp.bfloat16)
    grad_q = weigh_keys(grad_score, global_kv[0], window_kv[0], remote_kv[0]).astype(jnp.bfloat16)
    key_global, key_window, key_random = key_terms(grad_score, query_blocks)
    value_global, value_window, value_random = key_terms(weights, grad_blocks)
    global_sum = reduce_to_first(jnp.stack([key_global, value_global]), "seq")
    window_grad = jnp.stack([key_window, value_window]).reshape(
        2, query_count, 3, BLK, head_count, HD
    )
    no_pad = (0, 0)
    extended = (
        jnp.pad(window_grad[:, :, 0], (no_pad, (0, 2), no_pad, no_pad, no_pad))
        + jnp.pad(window_grad[:, :, 1], (no_pad, (1, 1), no_pad, no_pad, no_pad))
        + jnp.pad(window_grad[:, :, 2], (no_pad, (2, 0), no_pad, no_pad, no_pad))
    )
    outward = jnp.concatenate([extended[:, 0], extended[:, query_count + 1]], axis=1)
    inward = with_halo(outward.astype(jnp.bfloat16), (("seq", 1),), BLK).astype(outward.dtype)
    own_grad = extended[:, 1 : query_count + 1]
    own_grad = own_grad.at[:, 0].add(inward[:, :BLK])
    own_grad = own_grad.at[:, query_count - 1].add(inward[:, 3 * BLK :])
    random_terms = (
        jnp.stack([key_random, value_random])
        .reshape(2, query_count * RAND, BLK, head_count, HD)
        .astype(jnp.bfloat16)
    )
    send_pick = (places[None, :] == jnp.arange(groups * capacity, dtype=jnp.int32)[:, None]).astype(
        jnp.bfloat16
    )
    outgoing = jnp.einsum(
        "pj,xjihd->xpihd", send_pick, random_terms, preferred_element_type=jnp.float32
    ).astype(jnp.bfloat16)
    incoming = lax.all_to_all(
        outgoing.reshape(2, groups, capacity, BLK, head_count, HD),
        "seq",
        split_axis=1,
        concat_axis=1,
        tiled=True,
    )
    take_pick = (
        wanted.reshape(-1)[None, :] == jnp.arange(query_count, dtype=jnp.int32)[:, None]
    ).astype(jnp.bfloat16)
    random_sum = jnp.einsum(
        "qp,xpihd->xqihd",
        take_pick,
        incoming.reshape(2, groups * capacity, BLK, head_count, HD),
        preferred_element_type=jnp.float32,
    )
    global_sum = global_sum.reshape(2, 2, BLK, head_count, HD)
    own_grad = own_grad.at[:, 0:2].add(jnp.where(my_group == 0, global_sum, 0.0))
    total_grad = own_grad + random_sum
    grad_k = total_grad[0].reshape(group_tokens, head_count * HD).astype(jnp.bfloat16)
    grad_v = total_grad[1].reshape(group_tokens, head_count * HD).astype(jnp.bfloat16)
    return (
        lax.all_to_all(
            attended.reshape(group_tokens, head_count * HD),
            "head",
            split_axis=0,
            concat_axis=1,
            tiled=True,
        ),
        lax.all_to_all(
            grad_q.reshape(group_tokens, head_count * HD),
            "head",
            split_axis=0,
            concat_axis=1,
            tiled=True,
        ),
        lax.all_to_all(grad_k, "head", split_axis=0, concat_axis=1, tiled=True),
        lax.all_to_all(grad_v, "head", split_axis=0, concat_axis=1, tiled=True),
    )


def solution(mesh):
    placed = (
        P(("seq", "head"), None),
        P(("seq", "head"), None),
        P(("seq", "head"), None),
        P(("seq", "head"), None),
        P("seq", None),
    )
    return jax.shard_map(
        shards,
        mesh=mesh,
        in_specs=placed,
        out_specs=(
            P(("seq", "head"), None),
            P(("seq", "head"), None),
            P(("seq", "head"), None),
            P(("seq", "head"), None),
        ),
        check_vma=False,
    )
```

```python
import jax
import jax.numpy as jnp
from jax import lax
from jax.sharding import PartitionSpec as P

HD = 128
BLK = 128
RAND = 3


def with_halo(cells, sides, width):
    for axis, dim in sides:
        count = lax.axis_size(axis)
        ends = count - 1
        head = lax.slice_in_dim(cells, 0, width, axis=dim)
        tail = lax.slice_in_dim(cells, cells.shape[dim] - width, cells.shape[dim], axis=dim)
        cells = jnp.concatenate(
            [
                lax.ppermute(tail, axis, [(i, (i + 1) % count) for i in range(ends)]),
                cells,
                lax.ppermute(head, axis, [((i + 1) % count, i) for i in range(ends)]),
            ],
            axis=dim,
        )
    return cells


def broadcast(value, axis):
    count = lax.axis_size(axis)
    me = lax.axis_index(axis)
    step = 1
    while step < count:
        pairs = [(i, i + step) for i in range(step) if i + step < count]
        got = lax.ppermute(value, axis, pairs)
        value = jnp.where((me >= step) & (me < 2 * step), got, value)
        step *= 2
    return value


def reduce_to_first(value, axis):
    count = lax.axis_size(axis)
    step = 1
    while step * 2 < count:
        step *= 2
    while step >= 1:
        pairs = [(i + step, i) for i in range(step) if i + step < count]
        value = value + lax.ppermute(value, axis, pairs)
        step //= 2
    return value


def slot_places(owners, groups, capacity):
    owner_hits = (owners[:, None] == jnp.arange(groups, dtype=jnp.int32)[None, :]).astype(jnp.int32)
    earlier = jnp.cumsum(owner_hits, axis=0) - owner_hits
    return owners * capacity + jnp.sum(earlier * owner_hits, axis=1)


def request_table(list_rows, query_count, groups, capacity):
    flat_rows = list_rows.reshape(-1)
    places = slot_places(flat_rows // query_count, groups, capacity)
    matches = places[None, :] == jnp.arange(groups * capacity, dtype=jnp.int32)[:, None]
    table = jnp.sum(jnp.where(matches, (flat_rows % query_count)[None, :], 0), axis=1)
    return table.reshape(groups, capacity)


def window_valid(my_group, query_count, groups):
    block_ids = jnp.arange(query_count, dtype=jnp.int32)
    left_ok = jnp.logical_not(jnp.logical_and(my_group == 0, block_ids == 0))
    right_ok = jnp.logical_not(
        jnp.logical_and(my_group == groups - 1, block_ids == query_count - 1)
    )
    all_true = jnp.ones((query_count, BLK), dtype=bool)
    return jnp.concatenate(
        [
            all_true,
            all_true,
            left_ok[:, None] & all_true,
            all_true,
            right_ok[:, None] & all_true,
            jnp.ones((query_count, RAND * BLK), dtype=bool),
        ],
        axis=1,
    )


def against_keys(rows, global_part, window_part, remote_part):
    return jnp.concatenate(
        [
            jnp.einsum("qihd,jhd->qhij", rows, global_part, preferred_element_type=jnp.float32),
            jnp.einsum("qihd,qjhd->qhij", rows, window_part, preferred_element_type=jnp.float32),
            jnp.einsum("qihd,qjhd->qhij", rows, remote_part, preferred_element_type=jnp.float32),
        ],
        axis=-1,
    )


def split_keys(table):
    return (table[..., : 2 * BLK], table[..., 2 * BLK : 5 * BLK], table[..., 5 * BLK :])


def weigh_keys(table, global_part, window_part, remote_part):
    global_w, window_w, random_w = split_keys(table)
    return (
        jnp.einsum("qhij,jhd->qihd", global_w, global_part, preferred_element_type=jnp.float32)
        + jnp.einsum("qhij,qjhd->qihd", window_w, window_part, preferred_element_type=jnp.float32)
        + jnp.einsum("qhij,qjhd->qihd", random_w, remote_part, preferred_element_type=jnp.float32)
    )


def key_terms(table, rows):
    global_w, window_w, random_w = split_keys(table)
    return (
        jnp.einsum("qhij,qihd->jhd", global_w, rows, preferred_element_type=jnp.float32),
        jnp.einsum("qhij,qihd->qjhd", window_w, rows, preferred_element_type=jnp.float32),
        jnp.einsum("qhij,qihd->qjhd", random_w, rows, preferred_element_type=jnp.float32),
    )


def shards(queries, keys, values, grad_out, random_blocks):
    groups = lax.axis_size("seq")
    my_group = lax.axis_index("seq")
    head_q, head_k, head_v, head_g = lax.all_to_all(
        jnp.stack([queries, keys, values, grad_out]), "head", split_axis=2, concat_axis=1, tiled=True
    )
    group_tokens = head_q.shape[0]
    head_count = head_q.shape[1] // HD
    query_count = group_tokens // BLK
    capacity = max(2, 3 * query_count * RAND // (2 * groups))
    score_scale = HD ** (-0.5)
    key_value = jnp.stack([head_k, head_v])
    kv_blocks = key_value.reshape(2, query_count, BLK, head_count, HD)
    edged = with_halo(key_value, (("seq", 1),), BLK)
    edged = edged.reshape(2, query_count + 2, BLK, head_count, HD)
    window_kv = jnp.concatenate(
        [edged[:, 0:query_count], edged[:, 1 : query_count + 1], edged[:, 2 : query_count + 2]],
        axis=2,
    )
    global_kv = broadcast(kv_blocks[:, 0:2].reshape(2, 2 * BLK, head_count, HD), "seq")
    flat_ids = random_blocks.reshape(-1)
    places = slot_places(flat_ids // query_count, groups, capacity)
    wanted = lax.all_to_all(
        request_table(random_blocks, query_count, groups, capacity),
        "seq",
        split_axis=0,
        concat_axis=0,
        tiled=True,
    )
    served = jnp.take(kv_blocks, wanted.reshape(-1), axis=1)
    served = served.reshape(2, groups, capacity, BLK, head_count, HD)
    fetched = lax.all_to_all(served, "seq", split_axis=1, concat_axis=1, tiled=True)
    chosen = jnp.take(fetched.reshape(2, groups * capacity, BLK, head_count, HD), places, axis=1)
    remote_kv = chosen.reshape(2, query_count, RAND * BLK, head_count, HD)
    query_blocks = head_q.reshape(query_count, BLK, head_count, HD)
    grad_blocks = head_g.reshape(query_count, BLK, head_count, HD)
    scores = score_scale * against_keys(query_blocks, global_kv[0], window_kv[0], remote_kv[0])
    valid = window_valid(my_group, query_count, groups)
    scores = jnp.where(valid[:, None, None, :], scores, -jnp.inf)
    row_max = jnp.max(scores, axis=-1, keepdims=True)
    exponent = jnp.exp(scores - row_max)
    attention_probs = exponent / jnp.sum(exponent, axis=-1, keepdims=True)
    weights = attention_probs.astype(jnp.bfloat16)
    attended = weigh_keys(weights, global_kv[1], window_kv[1], remote_kv[1]).astype(jnp.bfloat16)
    grad_prob = against_keys(grad_blocks, global_kv[1], window_kv[1], remote_kv[1])
    row_delta = jnp.sum(attention_probs * grad_prob, axis=-1, keepdims=True)
    grad_score = (score_scale * attention_probs * (grad_prob - row_delta)).astype(jnp.bfloat16)
    grad_q = weigh_keys(grad_score, global_kv[0], window_kv[0], remote_kv[0]).astype(jnp.bfloat16)
    key_global, key_window, key_random = key_terms(grad_score, query_blocks)
    value_global, value_window, value_random = key_terms(weights, grad_blocks)
    global_sum = reduce_to_first(jnp.stack([key_global, value_global]), "seq")
    window_grad = jnp.stack([key_window, value_window]).reshape(
        2, query_count, 3, BLK, head_count, HD
    )
    no_pad = (0, 0)
    extended = (
        jnp.pad(window_grad[:, :, 0], (no_pad, (0, 2), no_pad, no_pad, no_pad))
        + jnp.pad(window_grad[:, :, 1], (no_pad, (1, 1), no_pad, no_pad, no_pad))
        + jnp.pad(window_grad[:, :, 2], (no_pad, (2, 0), no_pad, no_pad, no_pad))
    )
    outward = jnp.concatenate([extended[:, 0], extended[:, query_count + 1]], axis=1)
    inward = with_halo(outward.astype(jnp.bfloat16), (("seq", 1),), BLK).astype(outward.dtype)
    own_grad = extended[:, 1 : query_count + 1]
    own_grad = own_grad.at[:, 0].add(inward[:, :BLK])
    own_grad = own_grad.at[:, query_count - 1].add(inward[:, 3 * BLK :])
    random_terms = (
        jnp.stack([key_random, value_random])
        .reshape(2, query_count * RAND, BLK, head_count, HD)
        .astype(jnp.bfloat16)
    )
    send_pick = (places[None, :] == jnp.arange(groups * capacity, dtype=jnp.int32)[:, None]).astype(
        jnp.bfloat16
    )
    outgoing = jnp.einsum(
        "pj,xjihd->xpihd", send_pick, random_terms, preferred_element_type=jnp.float32
    ).astype(jnp.bfloat16)
    incoming = lax.all_to_all(
        outgoing.reshape(2, groups, capacity, BLK, head_count, HD),
        "seq",
        split_axis=1,
        concat_axis=1,
        tiled=True,
    )
    take_pick = (
        wanted.reshape(-1)[None, :] == jnp.arange(query_count, dtype=jnp.int32)[:, None]
    ).astype(jnp.bfloat16)
    random_sum = jnp.einsum(
        "qp,xpihd->xqihd",
        take_pick,
        incoming.reshape(2, groups * capacity, BLK, head_count, HD),
        preferred_element_type=jnp.float32,
    )
    global_sum = global_sum.reshape(2, 2, BLK, head_count, HD)
    own_grad = own_grad.at[:, 0:2].add(jnp.where(my_group == 0, global_sum, 0.0))
    total_grad = own_grad + random_sum
    grad_k = total_grad[0].reshape(group_tokens, head_count * HD).astype(jnp.bfloat16)
    grad_v = total_grad[1].reshape(group_tokens, head_count * HD).astype(jnp.bfloat16)
    front = lax.all_to_all(
        jnp.stack([attended, grad_q]).reshape(2, group_tokens, head_count * HD),
        "head",
        split_axis=1,
        concat_axis=2,
        tiled=True,
    )
    back = lax.all_to_all(jnp.stack([grad_k, grad_v]), "head", split_axis=1, concat_axis=2, tiled=True)
    return front[0], front[1], back[0], back[1]


def solution(mesh):
    placed = (
        P(("seq", "head"), None),
        P(("seq", "head"), None),
        P(("seq", "head"), None),
        P(("seq", "head"), None),
        P("seq", None),
    )
    return jax.shard_map(
        shards,
        mesh=mesh,
        in_specs=placed,
        out_specs=(
            P(("seq", "head"), None),
            P(("seq", "head"), None),
            P(("seq", "head"), None),
            P(("seq", "head"), None),
        ),
        check_vma=False,
    )
```

```python
import jax
import jax.numpy as jnp
from jax import lax
from jax.sharding import PartitionSpec as P

HD = 128
BLK = 128
RAND = 3


def with_halo(cells, sides, width):
    for axis, dim in sides:
        count = lax.axis_size(axis)
        ends = count - 1
        head = lax.slice_in_dim(cells, 0, width, axis=dim)
        tail = lax.slice_in_dim(cells, cells.shape[dim] - width, cells.shape[dim], axis=dim)
        cells = jnp.concatenate(
            [
                lax.ppermute(tail, axis, [(i, (i + 1) % count) for i in range(ends)]),
                cells,
                lax.ppermute(head, axis, [((i + 1) % count, i) for i in range(ends)]),
            ],
            axis=dim,
        )
    return cells


def row_width(count):
    return 4 if count % 4 == 0 else 1


def broadcast(value, axis):
    count = lax.axis_size(axis)
    me = lax.axis_index(axis)
    width = row_width(count)
    got = jnp.zeros_like(value)
    for row in range(1, count // width):
        got = got + lax.ppermute(value, axis, [(0, row * width)])
    value = jnp.where(me == 0, value, got)
    got = jnp.zeros_like(value)
    for col in range(1, width):
        pairs = [(row * width, row * width + col) for row in range(count // width)]
        got = got + lax.ppermute(value, axis, pairs)
    return jnp.where(me % width == 0, value, got)


def reduce_to_first(value, axis):
    count = lax.axis_size(axis)
    width = row_width(count)
    total = value
    for col in range(1, width):
        pairs = [(row * width + col, row * width) for row in range(count // width)]
        total = total + lax.ppermute(value, axis, pairs)
    value = total
    for row in range(1, count // width):
        total = total + lax.ppermute(value, axis, [(row * width, 0)])
    return total


def slot_places(owners, groups, capacity):
    owner_hits = (owners[:, None] == jnp.arange(groups, dtype=jnp.int32)[None, :]).astype(jnp.int32)
    earlier = jnp.cumsum(owner_hits, axis=0) - owner_hits
    return owners * capacity + jnp.sum(earlier * owner_hits, axis=1)


def request_table(list_rows, query_count, groups, capacity):
    flat_rows = list_rows.reshape(-1)
    places = slot_places(flat_rows // query_count, groups, capacity)
    matches = places[None, :] == jnp.arange(groups * capacity, dtype=jnp.int32)[:, None]
    table = jnp.sum(jnp.where(matches, (flat_rows % query_count)[None, :], 0), axis=1)
    return table.reshape(groups, capacity)


def window_valid(my_group, query_count, groups):
    block_ids = jnp.arange(query_count, dtype=jnp.int32)
    left_ok = jnp.logical_not(jnp.logical_and(my_group == 0, block_ids == 0))
    right_ok = jnp.logical_not(
        jnp.logical_and(my_group == groups - 1, block_ids == query_count - 1)
    )
    all_true = jnp.ones((query_count, BLK), dtype=bool)
    return jnp.concatenate(
        [
            all_true,
            all_true,
            left_ok[:, None] & all_true,
            all_true,
            right_ok[:, None] & all_true,
            jnp.ones((query_count, RAND * BLK), dtype=bool),
        ],
        axis=1,
    )


def against_keys(rows, global_part, window_part, remote_part):
    return jnp.concatenate(
        [
            jnp.einsum("qihd,jhd->qhij", rows, global_part, preferred_element_type=jnp.float32),
            jnp.einsum("qihd,qjhd->qhij", rows, window_part, preferred_element_type=jnp.float32),
            jnp.einsum("qihd,qjhd->qhij", rows, remote_part, preferred_element_type=jnp.float32),
        ],
        axis=-1,
    )


def split_keys(table):
    return (table[..., : 2 * BLK], table[..., 2 * BLK : 5 * BLK], table[..., 5 * BLK :])


def weigh_keys(table, global_part, window_part, remote_part):
    global_w, window_w, random_w = split_keys(table)
    return (
        jnp.einsum("qhij,jhd->qihd", global_w, global_part, preferred_element_type=jnp.float32)
        + jnp.einsum("qhij,qjhd->qihd", window_w, window_part, preferred_element_type=jnp.float32)
        + jnp.einsum("qhij,qjhd->qihd", random_w, remote_part, preferred_element_type=jnp.float32)
    )


def key_terms(table, rows):
    global_w, window_w, random_w = split_keys(table)
    return (
        jnp.einsum("qhij,qihd->jhd", global_w, rows, preferred_element_type=jnp.float32),
        jnp.einsum("qhij,qihd->qjhd", window_w, rows, preferred_element_type=jnp.float32),
        jnp.einsum("qhij,qihd->qjhd", random_w, rows, preferred_element_type=jnp.float32),
    )


def shards(queries, keys, values, grad_out, random_blocks):
    groups = lax.axis_size("seq")
    my_group = lax.axis_index("seq")
    head_q, head_k, head_v, head_g = lax.all_to_all(
        jnp.stack([queries, keys, values, grad_out]), "head", split_axis=2, concat_axis=1, tiled=True
    )
    group_tokens = head_q.shape[0]
    head_count = head_q.shape[1] // HD
    query_count = group_tokens // BLK
    capacity = max(2, 3 * query_count * RAND // (2 * groups))
    score_scale = HD ** (-0.5)
    key_value = jnp.stack([head_k, head_v])
    kv_blocks = key_value.reshape(2, query_count, BLK, head_count, HD)
    edged = with_halo(key_value, (("seq", 1),), BLK)
    edged = edged.reshape(2, query_count + 2, BLK, head_count, HD)
    window_kv = jnp.concatenate(
        [edged[:, 0:query_count], edged[:, 1 : query_count + 1], edged[:, 2 : query_count + 2]],
        axis=2,
    )
    global_kv = broadcast(kv_blocks[:, 0:2].reshape(2, 2 * BLK, head_count, HD), "seq")
    flat_ids = random_blocks.reshape(-1)
    places = slot_places(flat_ids // query_count, groups, capacity)
    wanted = lax.all_to_all(
        request_table(random_blocks, query_count, groups, capacity),
        "seq",
        split_axis=0,
        concat_axis=0,
        tiled=True,
    )
    served = jnp.take(kv_blocks, wanted.reshape(-1), axis=1)
    served = served.reshape(2, groups, capacity, BLK, head_count, HD)
    fetched = lax.all_to_all(served, "seq", split_axis=1, concat_axis=1, tiled=True)
    chosen = jnp.take(fetched.reshape(2, groups * capacity, BLK, head_count, HD), places, axis=1)
    remote_kv = chosen.reshape(2, query_count, RAND * BLK, head_count, HD)
    query_blocks = head_q.reshape(query_count, BLK, head_count, HD)
    grad_blocks = head_g.reshape(query_count, BLK, head_count, HD)
    scores = score_scale * against_keys(query_blocks, global_kv[0], window_kv[0], remote_kv[0])
    valid = window_valid(my_group, query_count, groups)
    scores = jnp.where(valid[:, None, None, :], scores, -jnp.inf)
    row_max = jnp.max(scores, axis=-1, keepdims=True)
    exponent = jnp.exp(scores - row_max)
    attention_probs = exponent / jnp.sum(exponent, axis=-1, keepdims=True)
    weights = attention_probs.astype(jnp.bfloat16)
    attended = weigh_keys(weights, global_kv[1], window_kv[1], remote_kv[1]).astype(jnp.bfloat16)
    grad_prob = against_keys(grad_blocks, global_kv[1], window_kv[1], remote_kv[1])
    row_delta = jnp.sum(attention_probs * grad_prob, axis=-1, keepdims=True)
    grad_score = (score_scale * attention_probs * (grad_prob - row_delta)).astype(jnp.bfloat16)
    grad_q = weigh_keys(grad_score, global_kv[0], window_kv[0], remote_kv[0]).astype(jnp.bfloat16)
    key_global, key_window, key_random = key_terms(grad_score, query_blocks)
    value_global, value_window, value_random = key_terms(weights, grad_blocks)
    global_sum = reduce_to_first(jnp.stack([key_global, value_global]), "seq")
    window_grad = jnp.stack([key_window, value_window]).reshape(
        2, query_count, 3, BLK, head_count, HD
    )
    no_pad = (0, 0)
    extended = (
        jnp.pad(window_grad[:, :, 0], (no_pad, (0, 2), no_pad, no_pad, no_pad))
        + jnp.pad(window_grad[:, :, 1], (no_pad, (1, 1), no_pad, no_pad, no_pad))
        + jnp.pad(window_grad[:, :, 2], (no_pad, (2, 0), no_pad, no_pad, no_pad))
    )
    outward = jnp.concatenate([extended[:, 0], extended[:, query_count + 1]], axis=1)
    inward = with_halo(outward.astype(jnp.bfloat16), (("seq", 1),), BLK).astype(outward.dtype)
    own_grad = extended[:, 1 : query_count + 1]
    own_grad = own_grad.at[:, 0].add(inward[:, :BLK])
    own_grad = own_grad.at[:, query_count - 1].add(inward[:, 3 * BLK :])
    random_terms = (
        jnp.stack([key_random, value_random])
        .reshape(2, query_count * RAND, BLK, head_count, HD)
        .astype(jnp.bfloat16)
    )
    send_pick = (places[None, :] == jnp.arange(groups * capacity, dtype=jnp.int32)[:, None]).astype(
        jnp.bfloat16
    )
    outgoing = jnp.einsum(
        "pj,xjihd->xpihd", send_pick, random_terms, preferred_element_type=jnp.float32
    ).astype(jnp.bfloat16)
    incoming = lax.all_to_all(
        outgoing.reshape(2, groups, capacity, BLK, head_count, HD),
        "seq",
        split_axis=1,
        concat_axis=1,
        tiled=True,
    )
    take_pick = (
        wanted.reshape(-1)[None, :] == jnp.arange(query_count, dtype=jnp.int32)[:, None]
    ).astype(jnp.bfloat16)
    random_sum = jnp.einsum(
        "qp,xpihd->xqihd",
        take_pick,
        incoming.reshape(2, groups * capacity, BLK, head_count, HD),
        preferred_element_type=jnp.float32,
    )
    global_sum = global_sum.reshape(2, 2, BLK, head_count, HD)
    own_grad = own_grad.at[:, 0:2].add(jnp.where(my_group == 0, global_sum, 0.0))
    total_grad = own_grad + random_sum
    grad_k = total_grad[0].reshape(group_tokens, head_count * HD).astype(jnp.bfloat16)
    grad_v = total_grad[1].reshape(group_tokens, head_count * HD).astype(jnp.bfloat16)
    front = lax.all_to_all(
        jnp.stack([attended, grad_q]).reshape(2, group_tokens, head_count * HD),
        "head",
        split_axis=1,
        concat_axis=2,
        tiled=True,
    )
    back = lax.all_to_all(jnp.stack([grad_k, grad_v]), "head", split_axis=1, concat_axis=2, tiled=True)
    return front[0], front[1], back[0], back[1]


def solution(mesh):
    placed = (
        P(("seq", "head"), None),
        P(("seq", "head"), None),
        P(("seq", "head"), None),
        P(("seq", "head"), None),
        P("seq", None),
    )
    return jax.shard_map(
        shards,
        mesh=mesh,
        in_specs=placed,
        out_specs=(
            P(("seq", "head"), None),
            P(("seq", "head"), None),
            P(("seq", "head"), None),
            P(("seq", "head"), None),
        ),
        check_vma=False,
    )
```

```python
import jax
import jax.numpy as jnp
from jax import lax
from jax.sharding import PartitionSpec as P

HD = 128
BLK = 128
RAND = 3


def with_halo(cells, sides, width):
    for axis, dim in sides:
        count = lax.axis_size(axis)
        ends = count - 1
        head = lax.slice_in_dim(cells, 0, width, axis=dim)
        tail = lax.slice_in_dim(cells, cells.shape[dim] - width, cells.shape[dim], axis=dim)
        cells = jnp.concatenate(
            [
                lax.ppermute(tail, axis, [(i, (i + 1) % count) for i in range(ends)]),
                cells,
                lax.ppermute(head, axis, [((i + 1) % count, i) for i in range(ends)]),
            ],
            axis=dim,
        )
    return cells


def row_width(count):
    return 4 if count % 4 == 0 else 1


def broadcast(value, axis):
    count = lax.axis_size(axis)
    me = lax.axis_index(axis)
    width = row_width(count)
    got = jnp.zeros_like(value)
    for row in range(1, count // width):
        got = got + lax.ppermute(value, axis, [(0, row * width)])
    value = jnp.where(me == 0, value, got)
    got = jnp.zeros_like(value)
    for col in range(1, width):
        pairs = [(row * width, row * width + col) for row in range(count // width)]
        got = got + lax.ppermute(value, axis, pairs)
    return jnp.where(me % width == 0, value, got)


def reduce_to_first(value, axis):
    count = lax.axis_size(axis)
    width = row_width(count)
    total = value
    for col in range(1, width):
        pairs = [(row * width + col, row * width) for row in range(count // width)]
        total = total + lax.ppermute(value, axis, pairs)
    value = total
    for row in range(1, count // width):
        total = total + lax.ppermute(value, axis, [(row * width, 0)])
    return total


def slot_places(owners, groups, capacity):
    owner_hits = (owners[:, None] == jnp.arange(groups, dtype=jnp.int32)[None, :]).astype(jnp.int32)
    earlier = jnp.cumsum(owner_hits, axis=0) - owner_hits
    return owners * capacity + jnp.sum(earlier * owner_hits, axis=1)


def request_table(list_rows, query_count, groups, capacity):
    flat_rows = list_rows.reshape(-1)
    places = slot_places(flat_rows // query_count, groups, capacity)
    matches = places[None, :] == jnp.arange(groups * capacity, dtype=jnp.int32)[:, None]
    table = jnp.sum(jnp.where(matches, (flat_rows % query_count)[None, :], 0), axis=1)
    return table.reshape(groups, capacity)


def window_valid(my_group, query_count, groups):
    block_ids = jnp.arange(query_count, dtype=jnp.int32)
    left_ok = jnp.logical_not(jnp.logical_and(my_group == 0, block_ids == 0))
    right_ok = jnp.logical_not(
        jnp.logical_and(my_group == groups - 1, block_ids == query_count - 1)
    )
    all_true = jnp.ones((query_count, BLK), dtype=bool)
    return jnp.concatenate(
        [
            all_true,
            all_true,
            left_ok[:, None] & all_true,
            all_true,
            right_ok[:, None] & all_true,
            jnp.ones((query_count, RAND * BLK), dtype=bool),
        ],
        axis=1,
    )


def against_keys(rows, global_part, window_part, remote_part):
    return jnp.concatenate(
        [
            jnp.einsum("qihd,jhd->qhij", rows, global_part, preferred_element_type=jnp.float32),
            jnp.einsum("qihd,qjhd->qhij", rows, window_part, preferred_element_type=jnp.float32),
            jnp.einsum("qihd,qjhd->qhij", rows, remote_part, preferred_element_type=jnp.float32),
        ],
        axis=-1,
    )


def split_keys(table):
    return (table[..., : 2 * BLK], table[..., 2 * BLK : 5 * BLK], table[..., 5 * BLK :])


def weigh_keys(table, global_part, window_part, remote_part):
    global_w, window_w, random_w = split_keys(table)
    return (
        jnp.einsum("qhij,jhd->qihd", global_w, global_part, preferred_element_type=jnp.float32)
        + jnp.einsum("qhij,qjhd->qihd", window_w, window_part, preferred_element_type=jnp.float32)
        + jnp.einsum("qhij,qjhd->qihd", random_w, remote_part, preferred_element_type=jnp.float32)
    )


def key_terms(table, rows):
    global_w, window_w, random_w = split_keys(table)
    return (
        jnp.einsum("qhij,qihd->jhd", global_w, rows, preferred_element_type=jnp.float32),
        jnp.einsum("qhij,qihd->qjhd", window_w, rows, preferred_element_type=jnp.float32),
        jnp.einsum("qhij,qihd->qjhd", random_w, rows, preferred_element_type=jnp.float32),
    )


def shards(queries, keys, values, grad_out, random_blocks):
    groups = lax.axis_size("seq")
    my_group = lax.axis_index("seq")
    head_q, head_k, head_v, head_g = lax.all_to_all(
        jnp.stack([queries, keys, values, grad_out]), "head", split_axis=2, concat_axis=1, tiled=True
    )
    group_tokens = head_q.shape[0]
    head_count = head_q.shape[1] // HD
    query_count = group_tokens // BLK
    capacity = max(2, 3 * query_count * RAND // (2 * groups))
    score_scale = HD ** (-0.5)
    ordered_table, head_k = lax.optimization_barrier(
        (request_table(random_blocks, query_count, groups, capacity), head_k)
    )
    key_value = jnp.stack([head_k, head_v])
    kv_blocks = key_value.reshape(2, query_count, BLK, head_count, HD)
    edged = with_halo(key_value, (("seq", 1),), BLK)
    edged = edged.reshape(2, query_count + 2, BLK, head_count, HD)
    window_kv = jnp.concatenate(
        [edged[:, 0:query_count], edged[:, 1 : query_count + 1], edged[:, 2 : query_count + 2]],
        axis=2,
    )
    global_kv = broadcast(kv_blocks[:, 0:2].reshape(2, 2 * BLK, head_count, HD), "seq")
    flat_ids = random_blocks.reshape(-1)
    places = slot_places(flat_ids // query_count, groups, capacity)
    table = ordered_table
    wanted = lax.all_to_all(
        table,
        "seq",
        split_axis=0,
        concat_axis=0,
        tiled=True,
    )
    served = jnp.take(kv_blocks, wanted.reshape(-1), axis=1)
    served = served.reshape(2, groups, capacity, BLK, head_count, HD)
    served, global_kv = lax.optimization_barrier((served, global_kv))
    fetched = lax.all_to_all(served, "seq", split_axis=1, concat_axis=1, tiled=True)
    chosen = jnp.take(fetched.reshape(2, groups * capacity, BLK, head_count, HD), places, axis=1)
    remote_kv = chosen.reshape(2, query_count, RAND * BLK, head_count, HD)
    query_blocks = head_q.reshape(query_count, BLK, head_count, HD)
    grad_blocks = head_g.reshape(query_count, BLK, head_count, HD)
    scores = score_scale * against_keys(query_blocks, global_kv[0], window_kv[0], remote_kv[0])
    valid = window_valid(my_group, query_count, groups)
    scores = jnp.where(valid[:, None, None, :], scores, -jnp.inf)
    row_max = jnp.max(scores, axis=-1, keepdims=True)
    exponent = jnp.exp(scores - row_max)
    attention_probs = exponent / jnp.sum(exponent, axis=-1, keepdims=True)
    weights = attention_probs.astype(jnp.bfloat16)
    attended = weigh_keys(weights, global_kv[1], window_kv[1], remote_kv[1]).astype(jnp.bfloat16)
    grad_prob = against_keys(grad_blocks, global_kv[1], window_kv[1], remote_kv[1])
    row_delta = jnp.sum(attention_probs * grad_prob, axis=-1, keepdims=True)
    grad_score = (score_scale * attention_probs * (grad_prob - row_delta)).astype(jnp.bfloat16)
    grad_q = weigh_keys(grad_score, global_kv[0], window_kv[0], remote_kv[0]).astype(jnp.bfloat16)
    key_global, key_window, key_random = key_terms(grad_score, query_blocks)
    value_global, value_window, value_random = key_terms(weights, grad_blocks)
    global_sum = reduce_to_first(jnp.stack([key_global, value_global]), "seq")
    window_grad = jnp.stack([key_window, value_window]).reshape(
        2, query_count, 3, BLK, head_count, HD
    )
    no_pad = (0, 0)
    extended = (
        jnp.pad(window_grad[:, :, 0], (no_pad, (0, 2), no_pad, no_pad, no_pad))
        + jnp.pad(window_grad[:, :, 1], (no_pad, (1, 1), no_pad, no_pad, no_pad))
        + jnp.pad(window_grad[:, :, 2], (no_pad, (2, 0), no_pad, no_pad, no_pad))
    )
    outward = jnp.concatenate([extended[:, 0], extended[:, query_count + 1]], axis=1)
    inward = with_halo(outward.astype(jnp.bfloat16), (("seq", 1),), BLK).astype(outward.dtype)
    own_grad = extended[:, 1 : query_count + 1]
    own_grad = own_grad.at[:, 0].add(inward[:, :BLK])
    own_grad = own_grad.at[:, query_count - 1].add(inward[:, 3 * BLK :])
    random_terms = (
        jnp.stack([key_random, value_random])
        .reshape(2, query_count * RAND, BLK, head_count, HD)
        .astype(jnp.bfloat16)
    )
    send_pick = (places[None, :] == jnp.arange(groups * capacity, dtype=jnp.int32)[:, None]).astype(
        jnp.bfloat16
    )
    outgoing = jnp.einsum(
        "pj,xjihd->xpihd", send_pick, random_terms, preferred_element_type=jnp.float32
    ).astype(jnp.bfloat16)
    incoming = lax.all_to_all(
        outgoing.reshape(2, groups, capacity, BLK, head_count, HD),
        "seq",
        split_axis=1,
        concat_axis=1,
        tiled=True,
    )
    take_pick = (
        wanted.reshape(-1)[None, :] == jnp.arange(query_count, dtype=jnp.int32)[:, None]
    ).astype(jnp.bfloat16)
    random_sum = jnp.einsum(
        "qp,xpihd->xqihd",
        take_pick,
        incoming.reshape(2, groups * capacity, BLK, head_count, HD),
        preferred_element_type=jnp.float32,
    )
    global_sum = global_sum.reshape(2, 2, BLK, head_count, HD)
    own_grad = own_grad.at[:, 0:2].add(jnp.where(my_group == 0, global_sum, 0.0))
    total_grad = own_grad + random_sum
    grad_k = total_grad[0].reshape(group_tokens, head_count * HD).astype(jnp.bfloat16)
    grad_v = total_grad[1].reshape(group_tokens, head_count * HD).astype(jnp.bfloat16)
    results = lax.all_to_all(
        jnp.stack([attended.reshape(group_tokens, head_count * HD),
                   grad_q.reshape(group_tokens, head_count * HD), grad_k, grad_v]),
        "head",
        split_axis=1,
        concat_axis=2,
        tiled=True,
    )
    return results[0], results[1], results[2], results[3]


def solution(mesh):
    placed = (
        P(("seq", "head"), None),
        P(("seq", "head"), None),
        P(("seq", "head"), None),
        P(("seq", "head"), None),
        P("seq", None),
    )
    return jax.shard_map(
        shards,
        mesh=mesh,
        in_specs=placed,
        out_specs=(
            P(("seq", "head"), None),
            P(("seq", "head"), None),
            P(("seq", "head"), None),
            P(("seq", "head"), None),
        ),
        check_vma=False,
    )
```

```python
import jax
import jax.numpy as jnp
from jax import lax
from jax.sharding import PartitionSpec as P

HD = 128
BLK = 128
RAND = 3


def with_halo(cells, sides, width):
    for axis, dim in sides:
        count = lax.axis_size(axis)
        ends = count - 1
        head = lax.slice_in_dim(cells, 0, width, axis=dim)
        tail = lax.slice_in_dim(cells, cells.shape[dim] - width, cells.shape[dim], axis=dim)
        cells = jnp.concatenate(
            [
                lax.ppermute(tail, axis, [(i, (i + 1) % count) for i in range(ends)]),
                cells,
                lax.ppermute(head, axis, [((i + 1) % count, i) for i in range(ends)]),
            ],
            axis=dim,
        )
    return cells


def row_width(count):
    return 4 if count % 4 == 0 else 1


def broadcast(value, axis):
    count = lax.axis_size(axis)
    me = lax.axis_index(axis)
    width = row_width(count)
    got = jnp.zeros_like(value)
    for row in range(1, count // width):
        got = got + lax.ppermute(value, axis, [(0, row * width)])
    value = jnp.where(me == 0, value, got)
    got = jnp.zeros_like(value)
    for col in range(1, width):
        pairs = [(row * width, row * width + col) for row in range(count // width)]
        got = got + lax.ppermute(value, axis, pairs)
    return jnp.where(me % width == 0, value, got)


def reduce_to_first(value, axis):
    count = lax.axis_size(axis)
    width = row_width(count)
    total = value
    for col in range(1, width):
        pairs = [(row * width + col, row * width) for row in range(count // width)]
        total = total + lax.ppermute(value, axis, pairs)
    value = total
    for row in range(1, count // width):
        total = total + lax.ppermute(value, axis, [(row * width, 0)])
    return total


def slot_places(owners, groups, capacity):
    owner_hits = (owners[:, None] == jnp.arange(groups, dtype=jnp.int32)[None, :]).astype(jnp.int32)
    earlier = jnp.cumsum(owner_hits, axis=0) - owner_hits
    return owners * capacity + jnp.sum(earlier * owner_hits, axis=1)


def request_table(list_rows, query_count, groups, capacity):
    flat_rows = list_rows.reshape(-1)
    places = slot_places(flat_rows // query_count, groups, capacity)
    matches = places[None, :] == jnp.arange(groups * capacity, dtype=jnp.int32)[:, None]
    table = jnp.sum(jnp.where(matches, (flat_rows % query_count)[None, :], 0), axis=1)
    return table.reshape(groups, capacity)


def window_valid(my_group, query_count, groups):
    block_ids = jnp.arange(query_count, dtype=jnp.int32)
    left_ok = jnp.logical_not(jnp.logical_and(my_group == 0, block_ids == 0))
    right_ok = jnp.logical_not(
        jnp.logical_and(my_group == groups - 1, block_ids == query_count - 1)
    )
    all_true = jnp.ones((query_count, BLK), dtype=bool)
    return jnp.concatenate(
        [
            all_true,
            all_true,
            left_ok[:, None] & all_true,
            all_true,
            right_ok[:, None] & all_true,
            jnp.ones((query_count, RAND * BLK), dtype=bool),
        ],
        axis=1,
    )


def against_keys(rows, global_part, window_part, remote_part):
    return jnp.concatenate(
        [
            jnp.einsum("qihd,jhd->qhij", rows, global_part, preferred_element_type=jnp.float32),
            jnp.einsum("qihd,qjhd->qhij", rows, window_part, preferred_element_type=jnp.float32),
            jnp.einsum("qihd,qjhd->qhij", rows, remote_part, preferred_element_type=jnp.float32),
        ],
        axis=-1,
    )


def split_keys(table):
    return (table[..., : 2 * BLK], table[..., 2 * BLK : 5 * BLK], table[..., 5 * BLK :])


def weigh_keys(table, global_part, window_part, remote_part):
    global_w, window_w, random_w = split_keys(table)
    return (
        jnp.einsum("qhij,jhd->qihd", global_w, global_part, preferred_element_type=jnp.float32)
        + jnp.einsum("qhij,qjhd->qihd", window_w, window_part, preferred_element_type=jnp.float32)
        + jnp.einsum("qhij,qjhd->qihd", random_w, remote_part, preferred_element_type=jnp.float32)
    )


def key_terms(table, rows):
    global_w, window_w, random_w = split_keys(table)
    return (
        jnp.einsum("qhij,qihd->jhd", global_w, rows, preferred_element_type=jnp.float32),
        jnp.einsum("qhij,qihd->qjhd", window_w, rows, preferred_element_type=jnp.float32),
        jnp.einsum("qhij,qihd->qjhd", random_w, rows, preferred_element_type=jnp.float32),
    )


def shards(queries, keys, values, grad_out, random_blocks):
    groups = lax.axis_size("seq")
    my_group = lax.axis_index("seq")
    head_q, head_k, head_v, head_g = lax.all_to_all(
        jnp.stack([queries, keys, values, grad_out]), "head", split_axis=2, concat_axis=1, tiled=True
    )
    group_tokens = head_q.shape[0]
    head_count = head_q.shape[1] // HD
    query_count = group_tokens // BLK
    capacity = max(2, 3 * query_count * RAND // (2 * groups))
    score_scale = HD ** (-0.5)
    ordered_table, head_k = lax.optimization_barrier(
        (request_table(random_blocks, query_count, groups, capacity), head_k)
    )
    key_value = jnp.stack([head_k, head_v])
    kv_blocks = key_value.reshape(2, query_count, BLK, head_count, HD)
    edged = with_halo(key_value, (("seq", 1),), BLK)
    edged = edged.reshape(2, query_count + 2, BLK, head_count, HD)
    window_kv = jnp.concatenate(
        [edged[:, 0:query_count], edged[:, 1 : query_count + 1], edged[:, 2 : query_count + 2]],
        axis=2,
    )
    global_kv = broadcast(kv_blocks[:, 0:2].reshape(2, 2 * BLK, head_count, HD), "seq")
    flat_ids = random_blocks.reshape(-1)
    places = slot_places(flat_ids // query_count, groups, capacity)
    table = ordered_table
    wanted = lax.all_to_all(
        table,
        "seq",
        split_axis=0,
        concat_axis=0,
        tiled=True,
    )
    served = jnp.take(jnp.swapaxes(kv_blocks, 0, 1), wanted.reshape(-1), axis=0)
    served = served.reshape(groups, capacity, 2, BLK, head_count, HD)
    served, global_kv = lax.optimization_barrier((served, global_kv))
    fetched = lax.all_to_all(served, "seq", split_axis=0, concat_axis=0, tiled=True)
    chosen = jnp.take(fetched.reshape(groups * capacity, 2, BLK, head_count, HD), places, axis=0)
    remote_kv = jnp.swapaxes(chosen, 0, 1).reshape(2, query_count, RAND * BLK, head_count, HD)
    query_blocks = head_q.reshape(query_count, BLK, head_count, HD)
    grad_blocks = head_g.reshape(query_count, BLK, head_count, HD)
    scores = score_scale * against_keys(query_blocks, global_kv[0], window_kv[0], remote_kv[0])
    valid = window_valid(my_group, query_count, groups)
    scores = jnp.where(valid[:, None, None, :], scores, -jnp.inf)
    row_max = jnp.max(scores, axis=-1, keepdims=True)
    exponent = jnp.exp(scores - row_max)
    attention_probs = exponent / jnp.sum(exponent, axis=-1, keepdims=True)
    weights = attention_probs.astype(jnp.bfloat16)
    attended = weigh_keys(weights, global_kv[1], window_kv[1], remote_kv[1]).astype(jnp.bfloat16)
    grad_prob = against_keys(grad_blocks, global_kv[1], window_kv[1], remote_kv[1])
    row_delta = jnp.sum(attention_probs * grad_prob, axis=-1, keepdims=True)
    grad_score = (score_scale * attention_probs * (grad_prob - row_delta)).astype(jnp.bfloat16)
    grad_q = weigh_keys(grad_score, global_kv[0], window_kv[0], remote_kv[0]).astype(jnp.bfloat16)
    key_global, key_window, key_random = key_terms(grad_score, query_blocks)
    value_global, value_window, value_random = key_terms(weights, grad_blocks)
    global_sum = reduce_to_first(jnp.stack([key_global, value_global]), "seq")
    window_grad = jnp.stack([key_window, value_window]).reshape(
        2, query_count, 3, BLK, head_count, HD
    )
    no_pad = (0, 0)
    extended = (
        jnp.pad(window_grad[:, :, 0], (no_pad, (0, 2), no_pad, no_pad, no_pad))
        + jnp.pad(window_grad[:, :, 1], (no_pad, (1, 1), no_pad, no_pad, no_pad))
        + jnp.pad(window_grad[:, :, 2], (no_pad, (2, 0), no_pad, no_pad, no_pad))
    )
    outward = jnp.concatenate([extended[:, 0], extended[:, query_count + 1]], axis=1)
    inward = with_halo(outward.astype(jnp.bfloat16), (("seq", 1),), BLK).astype(outward.dtype)
    own_grad = extended[:, 1 : query_count + 1]
    own_grad = own_grad.at[:, 0].add(inward[:, :BLK])
    own_grad = own_grad.at[:, query_count - 1].add(inward[:, 3 * BLK :])
    random_terms = jnp.stack(
        [key_random.reshape(query_count * RAND, BLK, head_count, HD),
         value_random.reshape(query_count * RAND, BLK, head_count, HD)],
        axis=1,
    ).astype(jnp.bfloat16)
    send_pick = (places[None, :] == jnp.arange(groups * capacity, dtype=jnp.int32)[:, None]).astype(
        jnp.bfloat16
    )
    outgoing = jnp.einsum(
        "pj,jxihd->pxihd", send_pick, random_terms, preferred_element_type=jnp.float32
    ).astype(jnp.bfloat16)
    incoming = lax.all_to_all(
        outgoing.reshape(groups, capacity, 2, BLK, head_count, HD),
        "seq",
        split_axis=0,
        concat_axis=0,
        tiled=True,
    )
    take_pick = (
        wanted.reshape(-1)[None, :] == jnp.arange(query_count, dtype=jnp.int32)[:, None]
    ).astype(jnp.bfloat16)
    random_sum = jnp.einsum(
        "qp,pxihd->xqihd",
        take_pick,
        incoming.reshape(groups * capacity, 2, BLK, head_count, HD),
        preferred_element_type=jnp.float32,
    )
    global_sum = global_sum.reshape(2, 2, BLK, head_count, HD)
    own_grad = own_grad.at[:, 0:2].add(jnp.where(my_group == 0, global_sum, 0.0))
    total_grad = own_grad + random_sum
    grad_k = total_grad[0].reshape(group_tokens, head_count * HD).astype(jnp.bfloat16)
    grad_v = total_grad[1].reshape(group_tokens, head_count * HD).astype(jnp.bfloat16)
    results = lax.all_to_all(
        jnp.stack([attended.reshape(group_tokens, head_count * HD),
                   grad_q.reshape(group_tokens, head_count * HD), grad_k, grad_v]),
        "head",
        split_axis=1,
        concat_axis=2,
        tiled=True,
    )
    return results[0], results[1], results[2], results[3]


def solution(mesh):
    placed = (
        P(("seq", "head"), None),
        P(("seq", "head"), None),
        P(("seq", "head"), None),
        P(("seq", "head"), None),
        P("seq", None),
    )
    return jax.shard_map(
        shards,
        mesh=mesh,
        in_specs=placed,
        out_specs=(
            P(("seq", "head"), None),
            P(("seq", "head"), None),
            P(("seq", "head"), None),
            P(("seq", "head"), None),
        ),
        check_vma=False,
    )
```

```python
import jax
import jax.numpy as jnp
from jax import lax
from jax.sharding import PartitionSpec as P

HD = 128
BLK = 128
RAND = 3


def with_halo(cells, sides, width):
    for axis, dim in sides:
        count = lax.axis_size(axis)
        ends = count - 1
        head = lax.slice_in_dim(cells, 0, width, axis=dim)
        tail = lax.slice_in_dim(cells, cells.shape[dim] - width, cells.shape[dim], axis=dim)
        cells = jnp.concatenate(
            [
                lax.ppermute(tail, axis, [(i, (i + 1) % count) for i in range(ends)]),
                cells,
                lax.ppermute(head, axis, [((i + 1) % count, i) for i in range(ends)]),
            ],
            axis=dim,
        )
    return cells


def row_width(count):
    return 4 if count % 4 == 0 else 1


def broadcast(value, axis):
    count = lax.axis_size(axis)
    me = lax.axis_index(axis)
    width = row_width(count)
    got = jnp.zeros_like(value)
    for row in range(1, count // width):
        got = got + lax.ppermute(value, axis, [(0, row * width)])
    value = jnp.where(me == 0, value, got)
    got = jnp.zeros_like(value)
    for col in range(1, width):
        pairs = [(row * width, row * width + col) for row in range(count // width)]
        got = got + lax.ppermute(value, axis, pairs)
    return jnp.where(me % width == 0, value, got)


def reduce_to_first(value, axis):
    count = lax.axis_size(axis)
    width = row_width(count)
    total = value
    for col in range(1, width):
        pairs = [(row * width + col, row * width) for row in range(count // width)]
        total = total + lax.ppermute(value, axis, pairs)
    value = total
    for row in range(1, count // width):
        total = total + lax.ppermute(value, axis, [(row * width, 0)])
    return total


def slot_places(owners, groups, capacity):
    owner_hits = (owners[:, None] == jnp.arange(groups, dtype=jnp.int32)[None, :]).astype(jnp.int32)
    earlier = jnp.cumsum(owner_hits, axis=0) - owner_hits
    return owners * capacity + jnp.sum(earlier * owner_hits, axis=1)


def request_table(list_rows, query_count, groups, capacity):
    flat_rows = list_rows.reshape(-1)
    places = slot_places(flat_rows // query_count, groups, capacity)
    matches = places[None, :] == jnp.arange(groups * capacity, dtype=jnp.int32)[:, None]
    table = jnp.sum(jnp.where(matches, (flat_rows % query_count)[None, :], 0), axis=1)
    return table.reshape(groups, capacity)


def window_valid(my_group, query_count, groups):
    block_ids = jnp.arange(query_count, dtype=jnp.int32)
    left_ok = jnp.logical_not(jnp.logical_and(my_group == 0, block_ids == 0))
    right_ok = jnp.logical_not(
        jnp.logical_and(my_group == groups - 1, block_ids == query_count - 1)
    )
    all_true = jnp.ones((query_count, BLK), dtype=bool)
    return jnp.concatenate(
        [
            all_true,
            all_true,
            left_ok[:, None] & all_true,
            all_true,
            right_ok[:, None] & all_true,
            jnp.ones((query_count, RAND * BLK), dtype=bool),
        ],
        axis=1,
    )


def against_keys(rows, global_part, window_part, remote_part):
    return jnp.concatenate(
        [
            jnp.einsum("hqid,hjd->hqij", rows, global_part, preferred_element_type=jnp.float32),
            jnp.einsum("hqid,hqjd->hqij", rows, window_part, preferred_element_type=jnp.float32),
            jnp.einsum("hqid,hqjd->hqij", rows, remote_part, preferred_element_type=jnp.float32),
        ],
        axis=-1,
    )


def split_keys(table):
    return (table[..., : 2 * BLK], table[..., 2 * BLK : 5 * BLK], table[..., 5 * BLK :])


def weigh_keys(table, global_part, window_part, remote_part):
    global_w, window_w, random_w = split_keys(table)
    return (
        jnp.einsum("hqij,hjd->hqid", global_w, global_part, preferred_element_type=jnp.float32)
        + jnp.einsum("hqij,hqjd->hqid", window_w, window_part, preferred_element_type=jnp.float32)
        + jnp.einsum("hqij,hqjd->hqid", random_w, remote_part, preferred_element_type=jnp.float32)
    )


def key_terms(table, rows):
    global_w, window_w, random_w = split_keys(table)
    return (
        jnp.einsum("hqij,hqid->hjd", global_w, rows, preferred_element_type=jnp.float32),
        jnp.einsum("hqij,hqid->hqjd", window_w, rows, preferred_element_type=jnp.float32),
        jnp.einsum("hqij,hqid->hqjd", random_w, rows, preferred_element_type=jnp.float32),
    )


def by_head(table, head_count):
    tokens = table.shape[0]
    return jnp.transpose(table.reshape(tokens, head_count, HD), (1, 0, 2))


def by_token(table):
    head_count, tokens = table.shape[0], table.shape[1]
    return jnp.transpose(table, (1, 0, 2)).reshape(tokens, head_count * HD)


def shards(queries, keys, values, grad_out, random_blocks):
    groups = lax.axis_size("seq")
    my_group = lax.axis_index("seq")
    head_q, head_k, head_v, head_g = lax.all_to_all(
        jnp.stack([queries, keys, values, grad_out]), "head", split_axis=2, concat_axis=1, tiled=True
    )
    group_tokens = head_q.shape[0]
    head_count = head_q.shape[1] // HD
    query_count = group_tokens // BLK
    capacity = max(2, 3 * query_count * RAND // (2 * groups))
    score_scale = HD ** (-0.5)
    ordered_table, head_k = lax.optimization_barrier(
        (request_table(random_blocks, query_count, groups, capacity), head_k)
    )
    key_value = jnp.stack([by_head(head_k, head_count), by_head(head_v, head_count)])
    kv_blocks = key_value.reshape(2, head_count, query_count, BLK, HD)
    edged = with_halo(key_value, (("seq", 2),), BLK)
    edged = edged.reshape(2, head_count, query_count + 2, BLK, HD)
    window_kv = jnp.concatenate(
        [edged[:, :, 0:query_count], edged[:, :, 1 : query_count + 1], edged[:, :, 2 : query_count + 2]],
        axis=3,
    )
    global_kv = broadcast(kv_blocks[:, :, 0:2].reshape(2, head_count, 2 * BLK, HD), "seq")
    flat_ids = random_blocks.reshape(-1)
    places = slot_places(flat_ids // query_count, groups, capacity)
    wanted = lax.all_to_all(ordered_table, "seq", split_axis=0, concat_axis=0, tiled=True)
    served = jnp.take(jnp.transpose(kv_blocks, (2, 0, 1, 3, 4)), wanted.reshape(-1), axis=0)
    served = served.reshape(groups, capacity, 2, head_count, BLK, HD)
    served, global_kv = lax.optimization_barrier((served, global_kv))
    fetched = lax.all_to_all(served, "seq", split_axis=0, concat_axis=0, tiled=True)
    chosen = jnp.take(fetched.reshape(groups * capacity, 2, head_count, BLK, HD), places, axis=0)
    remote_kv = jnp.transpose(
        chosen.reshape(query_count, RAND, 2, head_count, BLK, HD), (2, 3, 0, 1, 4, 5)
    ).reshape(2, head_count, query_count, RAND * BLK, HD)
    query_blocks = by_head(head_q, head_count).reshape(head_count, query_count, BLK, HD)
    grad_blocks = by_head(head_g, head_count).reshape(head_count, query_count, BLK, HD)
    scores = score_scale * against_keys(query_blocks, global_kv[0], window_kv[0], remote_kv[0])
    valid = window_valid(my_group, query_count, groups)
    scores = jnp.where(valid[None, :, None, :], scores, -jnp.inf)
    row_max = jnp.max(scores, axis=-1, keepdims=True)
    exponent = jnp.exp(scores - row_max)
    attention_probs = exponent / jnp.sum(exponent, axis=-1, keepdims=True)
    weights = attention_probs.astype(jnp.bfloat16)
    attended = weigh_keys(weights, global_kv[1], window_kv[1], remote_kv[1]).astype(jnp.bfloat16)
    grad_prob = against_keys(grad_blocks, global_kv[1], window_kv[1], remote_kv[1])
    row_delta = jnp.sum(attention_probs * grad_prob, axis=-1, keepdims=True)
    grad_score = (score_scale * attention_probs * (grad_prob - row_delta)).astype(jnp.bfloat16)
    grad_q = weigh_keys(grad_score, global_kv[0], window_kv[0], remote_kv[0]).astype(jnp.bfloat16)
    key_global, key_window, key_random = key_terms(grad_score, query_blocks)
    value_global, value_window, value_random = key_terms(weights, grad_blocks)
    global_sum = reduce_to_first(jnp.stack([key_global, value_global]), "seq")
    window_grad = jnp.stack([key_window, value_window]).reshape(
        2, head_count, query_count, 3, BLK, HD
    )
    no_pad = (0, 0)
    extended = (
        jnp.pad(window_grad[:, :, :, 0], (no_pad, no_pad, (0, 2), no_pad, no_pad))
        + jnp.pad(window_grad[:, :, :, 1], (no_pad, no_pad, (1, 1), no_pad, no_pad))
        + jnp.pad(window_grad[:, :, :, 2], (no_pad, no_pad, (2, 0), no_pad, no_pad))
    )
    outward = jnp.concatenate([extended[:, :, 0], extended[:, :, query_count + 1]], axis=2)
    inward = with_halo(outward.astype(jnp.bfloat16), (("seq", 2),), BLK).astype(outward.dtype)
    own_grad = extended[:, :, 1 : query_count + 1]
    own_grad = own_grad.at[:, :, 0].add(inward[:, :, :BLK])
    own_grad = own_grad.at[:, :, query_count - 1].add(inward[:, :, 3 * BLK :])
    random_terms = jnp.transpose(
        jnp.stack([key_random, value_random]).reshape(2, head_count, query_count * RAND, BLK, HD),
        (2, 0, 1, 3, 4),
    ).astype(jnp.bfloat16)
    send_pick = (places[None, :] == jnp.arange(groups * capacity, dtype=jnp.int32)[:, None]).astype(
        jnp.bfloat16
    )
    outgoing = jnp.einsum(
        "pj,jxhid->pxhid", send_pick, random_terms, preferred_element_type=jnp.float32
    ).astype(jnp.bfloat16)
    incoming = lax.all_to_all(
        outgoing.reshape(groups, capacity, 2, head_count, BLK, HD),
        "seq",
        split_axis=0,
        concat_axis=0,
        tiled=True,
    )
    take_pick = (
        wanted.reshape(-1)[None, :] == jnp.arange(query_count, dtype=jnp.int32)[:, None]
    ).astype(jnp.bfloat16)
    random_sum = jnp.einsum(
        "qp,pxhid->xhqid",
        take_pick,
        incoming.reshape(groups * capacity, 2, head_count, BLK, HD),
        preferred_element_type=jnp.float32,
    )
    global_sum = global_sum.reshape(2, head_count, 2, BLK, HD)
    own_grad = own_grad.at[:, :, 0:2].add(jnp.where(my_group == 0, global_sum, 0.0))
    total_grad = (own_grad + random_sum).astype(jnp.bfloat16)
    flat = (head_count, group_tokens, HD)
    results = lax.all_to_all(
        jnp.stack([by_token(attended.reshape(flat)), by_token(grad_q.reshape(flat)),
                   by_token(total_grad[0].reshape(flat)), by_token(total_grad[1].reshape(flat))]),
        "head",
        split_axis=1,
        concat_axis=2,
        tiled=True,
    )
    return results[0], results[1], results[2], results[3]


def solution(mesh):
    placed = (
        P(("seq", "head"), None),
        P(("seq", "head"), None),
        P(("seq", "head"), None),
        P(("seq", "head"), None),
        P("seq", None),
    )
    return jax.shard_map(
        shards,
        mesh=mesh,
        in_specs=placed,
        out_specs=(
            P(("seq", "head"), None),
            P(("seq", "head"), None),
            P(("seq", "head"), None),
            P(("seq", "head"), None),
        ),
        check_vma=False,
    )
```

```python
import jax
import jax.numpy as jnp
from jax import lax
from jax.sharding import PartitionSpec as P

HD = 128
BLK = 128
RAND = 3


def with_halo(cells, sides, width):
    for axis, dim in sides:
        count = lax.axis_size(axis)
        ends = count - 1
        head = lax.slice_in_dim(cells, 0, width, axis=dim)
        tail = lax.slice_in_dim(cells, cells.shape[dim] - width, cells.shape[dim], axis=dim)
        cells = jnp.concatenate(
            [
                lax.ppermute(tail, axis, [(i, (i + 1) % count) for i in range(ends)]),
                cells,
                lax.ppermute(head, axis, [((i + 1) % count, i) for i in range(ends)]),
            ],
            axis=dim,
        )
    return cells


def row_width(count):
    return 4 if count % 4 == 0 else 1


def broadcast(value, axis):
    count = lax.axis_size(axis)
    me = lax.axis_index(axis)
    width = row_width(count)
    got = jnp.zeros_like(value)
    for row in range(1, count // width):
        got = got + lax.ppermute(value, axis, [(0, row * width)])
    value = jnp.where(me == 0, value, got)
    got = jnp.zeros_like(value)
    for col in range(1, width):
        pairs = [(row * width, row * width + col) for row in range(count // width)]
        got = got + lax.ppermute(value, axis, pairs)
    return jnp.where(me % width == 0, value, got)


def reduce_to_first(value, axis):
    count = lax.axis_size(axis)
    width = row_width(count)
    total = value
    for col in range(1, width):
        pairs = [(row * width + col, row * width) for row in range(count // width)]
        total = total + lax.ppermute(value, axis, pairs)
    value = total
    for row in range(1, count // width):
        total = total + lax.ppermute(value, axis, [(row * width, 0)])
    return total


def slot_places(owners, groups, capacity):
    owner_hits = (owners[:, None] == jnp.arange(groups, dtype=jnp.int32)[None, :]).astype(jnp.int32)
    earlier = jnp.cumsum(owner_hits, axis=0) - owner_hits
    return owners * capacity + jnp.sum(earlier * owner_hits, axis=1)


def request_table(list_rows, query_count, groups, capacity):
    flat_rows = list_rows.reshape(-1)
    places = slot_places(flat_rows // query_count, groups, capacity)
    matches = places[None, :] == jnp.arange(groups * capacity, dtype=jnp.int32)[:, None]
    table = jnp.sum(jnp.where(matches, (flat_rows % query_count)[None, :], 0), axis=1)
    return table.reshape(groups, capacity)


def window_valid(my_group, query_count, groups):
    block_ids = jnp.arange(query_count, dtype=jnp.int32)
    left_ok = jnp.logical_not(jnp.logical_and(my_group == 0, block_ids == 0))
    right_ok = jnp.logical_not(
        jnp.logical_and(my_group == groups - 1, block_ids == query_count - 1)
    )
    all_true = jnp.ones((query_count, BLK), dtype=bool)
    return jnp.concatenate(
        [
            all_true,
            all_true,
            left_ok[:, None] & all_true,
            all_true,
            right_ok[:, None] & all_true,
            jnp.ones((query_count, RAND * BLK), dtype=bool),
        ],
        axis=1,
    )


def against_keys(rows, global_part, window_part, remote_part):
    return jnp.concatenate(
        [
            jnp.einsum("hqid,hjd->hqij", rows, global_part, preferred_element_type=jnp.float32),
            jnp.einsum("hqid,hqjd->hqij", rows, window_part, preferred_element_type=jnp.float32),
            jnp.einsum("hqid,hqjd->hqij", rows, remote_part, preferred_element_type=jnp.float32),
        ],
        axis=-1,
    )


def split_keys(table):
    return (table[..., : 2 * BLK], table[..., 2 * BLK : 5 * BLK], table[..., 5 * BLK :])


def weigh_keys(table, global_part, window_part, remote_part):
    global_w, window_w, random_w = split_keys(table)
    return (
        jnp.einsum("hqij,hjd->hqid", global_w, global_part, preferred_element_type=jnp.float32)
        + jnp.einsum("hqij,hqjd->hqid", window_w, window_part, preferred_element_type=jnp.float32)
        + jnp.einsum("hqij,hqjd->hqid", random_w, remote_part, preferred_element_type=jnp.float32)
    )


def key_terms(table, rows):
    global_w, window_w, random_w = split_keys(table)
    return (
        jnp.einsum("hqij,hqid->hjd", global_w, rows, preferred_element_type=jnp.float32),
        jnp.einsum("hqij,hqid->hqjd", window_w, rows, preferred_element_type=jnp.float32),
        jnp.einsum("hqij,hqid->hqjd", random_w, rows, preferred_element_type=jnp.float32),
    )


def by_head(table, head_count):
    tokens = table.shape[0]
    return jnp.transpose(table.reshape(tokens, head_count, HD), (1, 0, 2))


def by_token(table):
    head_count, tokens = table.shape[0], table.shape[1]
    return jnp.transpose(table, (1, 0, 2)).reshape(tokens, head_count * HD)


def shards(queries, keys, values, grad_out, random_blocks):
    groups = lax.axis_size("seq")
    my_group = lax.axis_index("seq")
    head_q, head_k, head_v, head_g = lax.all_to_all(
        jnp.stack([queries, keys, values, grad_out]), "head", split_axis=2, concat_axis=1, tiled=True
    )
    group_tokens = head_q.shape[0]
    head_count = head_q.shape[1] // HD
    query_count = group_tokens // BLK
    capacity = max(2, 3 * query_count * RAND // (2 * groups))
    score_scale = HD ** (-0.5)
    ordered_table, head_k = lax.optimization_barrier(
        (request_table(random_blocks, query_count, groups, capacity), head_k)
    )
    key_value = jnp.stack([by_head(head_k, head_count), by_head(head_v, head_count)])
    kv_blocks = key_value.reshape(2, head_count, query_count, BLK, HD)
    edged = with_halo(key_value, (("seq", 2),), BLK)
    edged = edged.reshape(2, head_count, query_count + 2, BLK, HD)
    window_kv = jnp.concatenate(
        [edged[:, :, 0:query_count], edged[:, :, 1 : query_count + 1], edged[:, :, 2 : query_count + 2]],
        axis=3,
    )
    global_kv = broadcast(kv_blocks[:, :, 0:2].reshape(2, head_count, 2 * BLK, HD), "seq")
    flat_ids = random_blocks.reshape(-1)
    places = slot_places(flat_ids // query_count, groups, capacity)
    wanted = lax.all_to_all(ordered_table, "seq", split_axis=0, concat_axis=0, tiled=True)
    served = jnp.take(jnp.transpose(kv_blocks, (2, 0, 1, 3, 4)), wanted.reshape(-1), axis=0)
    served = served.reshape(groups, capacity, 2, head_count, BLK, HD)
    served, global_kv, window_kv = lax.optimization_barrier((served, global_kv, window_kv))
    fetched = lax.all_to_all(served, "seq", split_axis=0, concat_axis=0, tiled=True)
    chosen = jnp.take(fetched.reshape(groups * capacity, 2, head_count, BLK, HD), places, axis=0)
    remote_kv = jnp.transpose(
        chosen.reshape(query_count, RAND, 2, head_count, BLK, HD), (2, 3, 0, 1, 4, 5)
    ).reshape(2, head_count, query_count, RAND * BLK, HD)
    query_blocks = by_head(head_q, head_count).reshape(head_count, query_count, BLK, HD)
    grad_blocks = by_head(head_g, head_count).reshape(head_count, query_count, BLK, HD)
    scores = score_scale * against_keys(query_blocks, global_kv[0], window_kv[0], remote_kv[0])
    valid = window_valid(my_group, query_count, groups)
    scores = jnp.where(valid[None, :, None, :], scores, -jnp.inf)
    row_max = jnp.max(scores, axis=-1, keepdims=True)
    exponent = jnp.exp(scores - row_max)
    attention_probs = exponent / jnp.sum(exponent, axis=-1, keepdims=True)
    weights = attention_probs.astype(jnp.bfloat16)
    attended = weigh_keys(weights, global_kv[1], window_kv[1], remote_kv[1]).astype(jnp.bfloat16)
    grad_prob = against_keys(grad_blocks, global_kv[1], window_kv[1], remote_kv[1])
    row_delta = jnp.sum(attention_probs * grad_prob, axis=-1, keepdims=True)
    grad_score = (score_scale * attention_probs * (grad_prob - row_delta)).astype(jnp.bfloat16)
    grad_q = weigh_keys(grad_score, global_kv[0], window_kv[0], remote_kv[0]).astype(jnp.bfloat16)
    key_global, key_window, key_random = key_terms(grad_score, query_blocks)
    value_global, value_window, value_random = key_terms(weights, grad_blocks)
    global_sum = reduce_to_first(jnp.stack([key_global, value_global]), "seq")
    window_grad = jnp.stack([key_window, value_window]).reshape(
        2, head_count, query_count, 3, BLK, HD
    )
    no_pad = (0, 0)
    extended = (
        jnp.pad(window_grad[:, :, :, 0], (no_pad, no_pad, (0, 2), no_pad, no_pad))
        + jnp.pad(window_grad[:, :, :, 1], (no_pad, no_pad, (1, 1), no_pad, no_pad))
        + jnp.pad(window_grad[:, :, :, 2], (no_pad, no_pad, (2, 0), no_pad, no_pad))
    )
    outward = jnp.concatenate([extended[:, :, 0], extended[:, :, query_count + 1]], axis=2)
    inward = with_halo(outward.astype(jnp.bfloat16), (("seq", 2),), BLK).astype(outward.dtype)
    random_terms = jnp.transpose(
        jnp.stack([key_random, value_random]).reshape(2, head_count, query_count * RAND, BLK, HD),
        (2, 0, 1, 3, 4),
    ).astype(jnp.bfloat16)
    send_pick = (places[None, :] == jnp.arange(groups * capacity, dtype=jnp.int32)[:, None]).astype(
        jnp.bfloat16
    )
    outgoing = jnp.einsum(
        "pj,jxhid->pxhid", send_pick, random_terms, preferred_element_type=jnp.float32
    ).astype(jnp.bfloat16)
    outgoing, inward, global_sum = lax.optimization_barrier((outgoing, inward, global_sum))
    incoming = lax.all_to_all(
        outgoing.reshape(groups, capacity, 2, head_count, BLK, HD),
        "seq",
        split_axis=0,
        concat_axis=0,
        tiled=True,
    )
    take_pick = (
        wanted.reshape(-1)[None, :] == jnp.arange(query_count, dtype=jnp.int32)[:, None]
    ).astype(jnp.bfloat16)
    random_sum = jnp.einsum(
        "qp,pxhid->xhqid",
        take_pick,
        incoming.reshape(groups * capacity, 2, head_count, BLK, HD),
        preferred_element_type=jnp.float32,
    )
    own_grad = extended[:, :, 1 : query_count + 1]
    own_grad = own_grad.at[:, :, 0].add(inward[:, :, :BLK])
    own_grad = own_grad.at[:, :, query_count - 1].add(inward[:, :, 3 * BLK :])
    global_sum = global_sum.reshape(2, head_count, 2, BLK, HD)
    own_grad = own_grad.at[:, :, 0:2].add(jnp.where(my_group == 0, global_sum, 0.0))
    total_grad = (own_grad + random_sum).astype(jnp.bfloat16)
    flat = (head_count, group_tokens, HD)
    results = lax.all_to_all(
        jnp.stack([by_token(attended.reshape(flat)), by_token(grad_q.reshape(flat)),
                   by_token(total_grad[0].reshape(flat)), by_token(total_grad[1].reshape(flat))]),
        "head",
        split_axis=1,
        concat_axis=2,
        tiled=True,
    )
    return results[0], results[1], results[2], results[3]


def solution(mesh):
    placed = (
        P(("seq", "head"), None),
        P(("seq", "head"), None),
        P(("seq", "head"), None),
        P(("seq", "head"), None),
        P("seq", None),
    )
    return jax.shard_map(
        shards,
        mesh=mesh,
        in_specs=placed,
        out_specs=(
            P(("seq", "head"), None),
            P(("seq", "head"), None),
            P(("seq", "head"), None),
            P(("seq", "head"), None),
        ),
        check_vma=False,
    )
```

```python
import jax
import jax.numpy as jnp
from jax import lax
from jax.sharding import PartitionSpec as P

HD = 128
BLK = 128
RAND = 3


def with_halo(cells, sides, width):
    for axis, dim in sides:
        count = lax.axis_size(axis)
        ends = count - 1
        head = lax.slice_in_dim(cells, 0, width, axis=dim)
        tail = lax.slice_in_dim(cells, cells.shape[dim] - width, cells.shape[dim], axis=dim)
        cells = jnp.concatenate(
            [
                lax.ppermute(tail, axis, [(i, (i + 1) % count) for i in range(ends)]),
                cells,
                lax.ppermute(head, axis, [((i + 1) % count, i) for i in range(ends)]),
            ],
            axis=dim,
        )
    return cells


def row_width(count):
    return 4 if count % 4 == 0 else 1


def broadcast(value, axis):
    count = lax.axis_size(axis)
    me = lax.axis_index(axis)
    step = 1
    while step < count:
        pairs = [(i, i + step) for i in range(step) if i + step < count]
        got = lax.ppermute(value, axis, pairs)
        value = jnp.where((me >= step) & (me < 2 * step), got, value)
        step *= 2
    return value


def reduce_to_first(value, axis):
    count = lax.axis_size(axis)
    width = row_width(count)
    total = value
    for col in range(1, width):
        pairs = [(row * width + col, row * width) for row in range(count // width)]
        total = total + lax.ppermute(value, axis, pairs)
    value = total
    for row in range(1, count // width):
        total = total + lax.ppermute(value, axis, [(row * width, 0)])
    return total


def slot_places(owners, groups, capacity):
    owner_hits = (owners[:, None] == jnp.arange(groups, dtype=jnp.int32)[None, :]).astype(jnp.int32)
    earlier = jnp.cumsum(owner_hits, axis=0) - owner_hits
    return owners * capacity + jnp.sum(earlier * owner_hits, axis=1)


def request_table(list_rows, query_count, groups, capacity):
    flat_rows = list_rows.reshape(-1)
    places = slot_places(flat_rows // query_count, groups, capacity)
    matches = places[None, :] == jnp.arange(groups * capacity, dtype=jnp.int32)[:, None]
    table = jnp.sum(jnp.where(matches, (flat_rows % query_count)[None, :], 0), axis=1)
    return table.reshape(groups, capacity)


def window_valid(my_group, query_count, groups):
    block_ids = jnp.arange(query_count, dtype=jnp.int32)
    left_ok = jnp.logical_not(jnp.logical_and(my_group == 0, block_ids == 0))
    right_ok = jnp.logical_not(
        jnp.logical_and(my_group == groups - 1, block_ids == query_count - 1)
    )
    all_true = jnp.ones((query_count, BLK), dtype=bool)
    return jnp.concatenate(
        [
            all_true,
            all_true,
            left_ok[:, None] & all_true,
            all_true,
            right_ok[:, None] & all_true,
            jnp.ones((query_count, RAND * BLK), dtype=bool),
        ],
        axis=1,
    )


def against_keys(rows, global_part, window_part, remote_part):
    return jnp.concatenate(
        [
            jnp.einsum("hqid,hjd->hqij", rows, global_part, preferred_element_type=jnp.float32),
            jnp.einsum("hqid,hqjd->hqij", rows, window_part, preferred_element_type=jnp.float32),
            jnp.einsum("hqid,hqjd->hqij", rows, remote_part, preferred_element_type=jnp.float32),
        ],
        axis=-1,
    )


def split_keys(table):
    return (table[..., : 2 * BLK], table[..., 2 * BLK : 5 * BLK], table[..., 5 * BLK :])


def weigh_keys(table, global_part, window_part, remote_part):
    global_w, window_w, random_w = split_keys(table)
    return (
        jnp.einsum("hqij,hjd->hqid", global_w, global_part, preferred_element_type=jnp.float32)
        + jnp.einsum("hqij,hqjd->hqid", window_w, window_part, preferred_element_type=jnp.float32)
        + jnp.einsum("hqij,hqjd->hqid", random_w, remote_part, preferred_element_type=jnp.float32)
    )


def key_terms(table, rows):
    global_w, window_w, random_w = split_keys(table)
    return (
        jnp.einsum("hqij,hqid->hjd", global_w, rows, preferred_element_type=jnp.float32),
        jnp.einsum("hqij,hqid->hqjd", window_w, rows, preferred_element_type=jnp.float32),
        jnp.einsum("hqij,hqid->hqjd", random_w, rows, preferred_element_type=jnp.float32),
    )


def by_head(table, head_count):
    tokens = table.shape[0]
    return jnp.transpose(table.reshape(tokens, head_count, HD), (1, 0, 2))


def by_token(table):
    head_count, tokens = table.shape[0], table.shape[1]
    return jnp.transpose(table, (1, 0, 2)).reshape(tokens, head_count * HD)


def shards(queries, keys, values, grad_out, random_blocks):
    groups = lax.axis_size("seq")
    my_group = lax.axis_index("seq")
    head_q, head_k, head_v, head_g = lax.all_to_all(
        jnp.stack([queries, keys, values, grad_out]), "head", split_axis=2, concat_axis=1, tiled=True
    )
    group_tokens = head_q.shape[0]
    head_count = head_q.shape[1] // HD
    query_count = group_tokens // BLK
    capacity = max(2, 3 * query_count * RAND // (2 * groups))
    score_scale = HD ** (-0.5)
    ordered_table, head_k = lax.optimization_barrier(
        (request_table(random_blocks, query_count, groups, capacity), head_k)
    )
    key_value = jnp.stack([by_head(head_k, head_count), by_head(head_v, head_count)])
    kv_blocks = key_value.reshape(2, head_count, query_count, BLK, HD)
    edged = with_halo(key_value, (("seq", 2),), BLK)
    edged = edged.reshape(2, head_count, query_count + 2, BLK, HD)
    window_kv = jnp.concatenate(
        [edged[:, :, 0:query_count], edged[:, :, 1 : query_count + 1], edged[:, :, 2 : query_count + 2]],
        axis=3,
    )
    global_kv = broadcast(kv_blocks[:, :, 0:2].reshape(2, head_count, 2 * BLK, HD), "seq")
    flat_ids = random_blocks.reshape(-1)
    places = slot_places(flat_ids // query_count, groups, capacity)
    wanted = lax.all_to_all(ordered_table, "seq", split_axis=0, concat_axis=0, tiled=True)
    served = jnp.take(jnp.transpose(kv_blocks, (2, 0, 1, 3, 4)), wanted.reshape(-1), axis=0)
    served = served.reshape(groups, capacity, 2, head_count, BLK, HD)
    served, global_kv = lax.optimization_barrier((served, global_kv))
    fetched = lax.all_to_all(served, "seq", split_axis=0, concat_axis=0, tiled=True)
    chosen = jnp.take(fetched.reshape(groups * capacity, 2, head_count, BLK, HD), places, axis=0)
    remote_kv = jnp.transpose(
        chosen.reshape(query_count, RAND, 2, head_count, BLK, HD), (2, 3, 0, 1, 4, 5)
    ).reshape(2, head_count, query_count, RAND * BLK, HD)
    query_blocks = by_head(head_q, head_count).reshape(head_count, query_count, BLK, HD)
    grad_blocks = by_head(head_g, head_count).reshape(head_count, query_count, BLK, HD)
    scores = score_scale * against_keys(query_blocks, global_kv[0], window_kv[0], remote_kv[0])
    valid = window_valid(my_group, query_count, groups)
    scores = jnp.where(valid[None, :, None, :], scores, -jnp.inf)
    row_max = jnp.max(scores, axis=-1, keepdims=True)
    exponent = jnp.exp(scores - row_max)
    attention_probs = exponent / jnp.sum(exponent, axis=-1, keepdims=True)
    weights = attention_probs.astype(jnp.bfloat16)
    attended = weigh_keys(weights, global_kv[1], window_kv[1], remote_kv[1]).astype(jnp.bfloat16)
    grad_prob = against_keys(grad_blocks, global_kv[1], window_kv[1], remote_kv[1])
    row_delta = jnp.sum(attention_probs * grad_prob, axis=-1, keepdims=True)
    grad_score = (score_scale * attention_probs * (grad_prob - row_delta)).astype(jnp.bfloat16)
    grad_q = weigh_keys(grad_score, global_kv[0], window_kv[0], remote_kv[0]).astype(jnp.bfloat16)
    key_global, key_window, key_random = key_terms(grad_score, query_blocks)
    value_global, value_window, value_random = key_terms(weights, grad_blocks)
    global_sum = reduce_to_first(jnp.stack([key_global, value_global]), "seq")
    window_grad = jnp.stack([key_window, value_window]).reshape(
        2, head_count, query_count, 3, BLK, HD
    )
    no_pad = (0, 0)
    extended = (
        jnp.pad(window_grad[:, :, :, 0], (no_pad, no_pad, (0, 2), no_pad, no_pad))
        + jnp.pad(window_grad[:, :, :, 1], (no_pad, no_pad, (1, 1), no_pad, no_pad))
        + jnp.pad(window_grad[:, :, :, 2], (no_pad, no_pad, (2, 0), no_pad, no_pad))
    )
    outward = jnp.concatenate([extended[:, :, 0], extended[:, :, query_count + 1]], axis=2)
    inward = with_halo(outward.astype(jnp.bfloat16), (("seq", 2),), BLK).astype(outward.dtype)
    own_grad = extended[:, :, 1 : query_count + 1]
    own_grad = own_grad.at[:, :, 0].add(inward[:, :, :BLK])
    own_grad = own_grad.at[:, :, query_count - 1].add(inward[:, :, 3 * BLK :])
    random_terms = jnp.transpose(
        jnp.stack([key_random, value_random]).reshape(2, head_count, query_count * RAND, BLK, HD),
        (2, 0, 1, 3, 4),
    ).astype(jnp.bfloat16)
    send_pick = (places[None, :] == jnp.arange(groups * capacity, dtype=jnp.int32)[:, None]).astype(
        jnp.bfloat16
    )
    outgoing = jnp.einsum(
        "pj,jxhid->pxhid", send_pick, random_terms, preferred_element_type=jnp.float32
    ).astype(jnp.bfloat16)
    incoming = lax.all_to_all(
        outgoing.reshape(groups, capacity, 2, head_count, BLK, HD),
        "seq",
        split_axis=0,
        concat_axis=0,
        tiled=True,
    )
    take_pick = (
        wanted.reshape(-1)[None, :] == jnp.arange(query_count, dtype=jnp.int32)[:, None]
    ).astype(jnp.bfloat16)
    random_sum = jnp.einsum(
        "qp,pxhid->xhqid",
        take_pick,
        incoming.reshape(groups * capacity, 2, head_count, BLK, HD),
        preferred_element_type=jnp.float32,
    )
    global_sum = global_sum.reshape(2, head_count, 2, BLK, HD)
    own_grad = own_grad.at[:, :, 0:2].add(jnp.where(my_group == 0, global_sum, 0.0))
    total_grad = (own_grad + random_sum).astype(jnp.bfloat16)
    flat = (head_count, group_tokens, HD)
    results = lax.all_to_all(
        jnp.stack([by_token(attended.reshape(flat)), by_token(grad_q.reshape(flat)),
                   by_token(total_grad[0].reshape(flat)), by_token(total_grad[1].reshape(flat))]),
        "head",
        split_axis=1,
        concat_axis=2,
        tiled=True,
    )
    return results[0], results[1], results[2], results[3]


def solution(mesh):
    placed = (
        P(("seq", "head"), None),
        P(("seq", "head"), None),
        P(("seq", "head"), None),
        P(("seq", "head"), None),
        P("seq", None),
    )
    return jax.shard_map(
        shards,
        mesh=mesh,
        in_specs=placed,
        out_specs=(
            P(("seq", "head"), None),
            P(("seq", "head"), None),
            P(("seq", "head"), None),
            P(("seq", "head"), None),
        ),
        check_vma=False,
    )
```

```python
import jax
import jax.numpy as jnp
from jax import lax
from jax.sharding import PartitionSpec as P

HD = 128
BLK = 128
RAND = 3


def with_halo(cells, sides, width):
    for axis, dim in sides:
        count = lax.axis_size(axis)
        ends = count - 1
        head = lax.slice_in_dim(cells, 0, width, axis=dim)
        tail = lax.slice_in_dim(cells, cells.shape[dim] - width, cells.shape[dim], axis=dim)
        cells = jnp.concatenate(
            [
                lax.ppermute(tail, axis, [(i, (i + 1) % count) for i in range(ends)]),
                cells,
                lax.ppermute(head, axis, [((i + 1) % count, i) for i in range(ends)]),
            ],
            axis=dim,
        )
    return cells


def row_width(count):
    return 4 if count % 4 == 0 else 1


def broadcast(value, axis):
    count = lax.axis_size(axis)
    me = lax.axis_index(axis)
    width = row_width(count)
    got = jnp.zeros_like(value)
    for row in range(1, count // width):
        got = got + lax.ppermute(value, axis, [(0, row * width)])
    value = jnp.where(me == 0, value, got)
    got = jnp.zeros_like(value)
    for col in range(1, width):
        pairs = [(row * width, row * width + col) for row in range(count // width)]
        got = got + lax.ppermute(value, axis, pairs)
    return jnp.where(me % width == 0, value, got)


def reduce_to_first(value, axis):
    count = lax.axis_size(axis)
    width = row_width(count)
    total = value
    for col in range(1, width):
        pairs = [(row * width + col, row * width) for row in range(count // width)]
        total = total + lax.ppermute(value, axis, pairs)
    value = total
    for row in range(1, count // width):
        total = total + lax.ppermute(value, axis, [(row * width, 0)])
    return total


def slot_places(owners, groups, capacity):
    owner_hits = (owners[:, None] == jnp.arange(groups, dtype=jnp.int32)[None, :]).astype(jnp.int32)
    earlier = jnp.cumsum(owner_hits, axis=0) - owner_hits
    return owners * capacity + jnp.sum(earlier * owner_hits, axis=1)


def request_table(list_rows, query_count, groups, capacity):
    flat_rows = list_rows.reshape(-1)
    places = slot_places(flat_rows // query_count, groups, capacity)
    matches = places[None, :] == jnp.arange(groups * capacity, dtype=jnp.int32)[:, None]
    table = jnp.sum(jnp.where(matches, (flat_rows % query_count)[None, :], 0), axis=1)
    return table.reshape(groups, capacity)


def mirror_shift(groups):
    return max(1, groups * 27 // 32) % groups


def route(list_rows, query_count, groups, capacity):
    flat_rows = list_rows.reshape(-1)
    owners = flat_rows // query_count
    places = slot_places(owners, groups, capacity)
    rank = places - owners * capacity
    source = jnp.where(rank == 0, owners, (owners + mirror_shift(groups)) % groups)
    held_id = jnp.where(rank == 0, flat_rows % query_count, query_count + flat_rows % query_count)
    hits = (source[None, :] == jnp.arange(groups, dtype=jnp.int32)[:, None]).astype(jnp.int32)
    fits = jnp.logical_and(jnp.all(jnp.sum(hits, axis=1) <= 1), jnp.all(rank <= 1))
    fast_table = jnp.sum(hits * held_id[None, :], axis=1)
    table = jnp.concatenate(
        [
            request_table(list_rows, query_count, groups, capacity),
            fast_table[:, None],
            jnp.broadcast_to(fits.astype(jnp.int32), (groups, 1)),
        ],
        axis=1,
    )
    return table, places, source


def window_valid(my_group, query_count, groups):
    block_ids = jnp.arange(query_count, dtype=jnp.int32)
    left_ok = jnp.logical_not(jnp.logical_and(my_group == 0, block_ids == 0))
    right_ok = jnp.logical_not(
        jnp.logical_and(my_group == groups - 1, block_ids == query_count - 1)
    )
    all_true = jnp.ones((query_count, BLK), dtype=bool)
    return jnp.concatenate(
        [
            all_true,
            all_true,
            left_ok[:, None] & all_true,
            all_true,
            right_ok[:, None] & all_true,
            jnp.ones((query_count, RAND * BLK), dtype=bool),
        ],
        axis=1,
    )


def against_keys(rows, global_part, window_part, remote_part):
    return jnp.concatenate(
        [
            jnp.einsum("hqid,hjd->hqij", rows, global_part, preferred_element_type=jnp.float32),
            jnp.einsum("hqid,hqjd->hqij", rows, window_part, preferred_element_type=jnp.float32),
            jnp.einsum("hqid,hqjd->hqij", rows, remote_part, preferred_element_type=jnp.float32),
        ],
        axis=-1,
    )


def split_keys(table):
    return (table[..., : 2 * BLK], table[..., 2 * BLK : 5 * BLK], table[..., 5 * BLK :])


def weigh_keys(table, global_part, window_part, remote_part):
    global_w, window_w, random_w = split_keys(table)
    return (
        jnp.einsum("hqij,hjd->hqid", global_w, global_part, preferred_element_type=jnp.float32)
        + jnp.einsum("hqij,hqjd->hqid", window_w, window_part, preferred_element_type=jnp.float32)
        + jnp.einsum("hqij,hqjd->hqid", random_w, remote_part, preferred_element_type=jnp.float32)
    )


def key_terms(table, rows):
    global_w, window_w, random_w = split_keys(table)
    return (
        jnp.einsum("hqij,hqid->hjd", global_w, rows, preferred_element_type=jnp.float32),
        jnp.einsum("hqij,hqid->hqjd", window_w, rows, preferred_element_type=jnp.float32),
        jnp.einsum("hqij,hqid->hqjd", random_w, rows, preferred_element_type=jnp.float32),
    )


def by_head(table, head_count):
    tokens = table.shape[0]
    return jnp.transpose(table.reshape(tokens, head_count, HD), (1, 0, 2))


def by_token(table):
    head_count, tokens = table.shape[0], table.shape[1]
    return jnp.transpose(table, (1, 0, 2)).reshape(tokens, head_count * HD)


def shards(queries, keys, values, grad_out, random_blocks):
    groups = lax.axis_size("seq")
    my_group = lax.axis_index("seq")
    head_q, head_k, head_v, head_g = lax.all_to_all(
        jnp.stack([queries, keys, values, grad_out]), "head", split_axis=2, concat_axis=1, tiled=True
    )
    group_tokens = head_q.shape[0]
    head_count = head_q.shape[1] // HD
    query_count = group_tokens // BLK
    capacity = max(2, 3 * query_count * RAND // (2 * groups))
    score_scale = HD ** (-0.5)
    ordered_table, places, source = route(random_blocks, query_count, groups, capacity)
    ordered_table, head_k = lax.optimization_barrier((ordered_table, head_k))
    shift = mirror_shift(groups)
    key_value = jnp.stack([by_head(head_k, head_count), by_head(head_v, head_count)])
    kv_blocks = key_value.reshape(2, head_count, query_count, BLK, HD)
    edged = with_halo(key_value, (("seq", 2),), BLK)
    edged = edged.reshape(2, head_count, query_count + 2, BLK, HD)
    window_kv = jnp.concatenate(
        [edged[:, :, 0:query_count], edged[:, :, 1 : query_count + 1], edged[:, :, 2 : query_count + 2]],
        axis=3,
    )
    global_kv = broadcast(kv_blocks[:, :, 0:2].reshape(2, head_count, 2 * BLK, HD), "seq")
    received = lax.all_to_all(ordered_table, "seq", split_axis=0, concat_axis=0, tiled=True)
    wanted = received[:, :capacity]
    wanted_fast = received[:, capacity]
    take_fast = jnp.all(received[:, capacity + 1] == 1)
    mirror = lax.ppermute(kv_blocks, "seq", [(i, (i + shift) % groups) for i in range(groups)])
    held = jnp.transpose(jnp.concatenate([kv_blocks, mirror], axis=2), (2, 0, 1, 3, 4))
    held, global_kv = lax.optimization_barrier((held, global_kv))

    def fetch_fast(held):
        served = jnp.take(held, wanted_fast, axis=0)
        fetched = lax.all_to_all(served, "seq", split_axis=0, concat_axis=0, tiled=True)
        return jnp.take(fetched, source, axis=0)

    def fetch_all(held):
        served = jnp.take(held[:query_count], wanted.reshape(-1), axis=0)
        served = served.reshape(groups, capacity, 2, head_count, BLK, HD)
        fetched = lax.all_to_all(served, "seq", split_axis=0, concat_axis=0, tiled=True)
        return jnp.take(fetched.reshape(groups * capacity, 2, head_count, BLK, HD), places, axis=0)

    chosen = lax.cond(take_fast, fetch_fast, fetch_all, held)
    remote_kv = jnp.transpose(
        chosen.reshape(query_count, RAND, 2, head_count, BLK, HD), (2, 3, 0, 1, 4, 5)
    ).reshape(2, head_count, query_count, RAND * BLK, HD)
    query_blocks = by_head(head_q, head_count).reshape(head_count, query_count, BLK, HD)
    grad_blocks = by_head(head_g, head_count).reshape(head_count, query_count, BLK, HD)
    scores = score_scale * against_keys(query_blocks, global_kv[0], window_kv[0], remote_kv[0])
    valid = window_valid(my_group, query_count, groups)
    scores = jnp.where(valid[None, :, None, :], scores, -jnp.inf)
    row_max = jnp.max(scores, axis=-1, keepdims=True)
    exponent = jnp.exp(scores - row_max)
    attention_probs = exponent / jnp.sum(exponent, axis=-1, keepdims=True)
    weights = attention_probs.astype(jnp.bfloat16)
    attended = weigh_keys(weights, global_kv[1], window_kv[1], remote_kv[1]).astype(jnp.bfloat16)
    grad_prob = against_keys(grad_blocks, global_kv[1], window_kv[1], remote_kv[1])
    row_delta = jnp.sum(attention_probs * grad_prob, axis=-1, keepdims=True)
    grad_score = (score_scale * attention_probs * (grad_prob - row_delta)).astype(jnp.bfloat16)
    grad_q = weigh_keys(grad_score, global_kv[0], window_kv[0], remote_kv[0]).astype(jnp.bfloat16)
    key_global, key_window, key_random = key_terms(grad_score, query_blocks)
    value_global, value_window, value_random = key_terms(weights, grad_blocks)
    global_sum = reduce_to_first(jnp.stack([key_global, value_global]), "seq")
    window_grad = jnp.stack([key_window, value_window]).reshape(
        2, head_count, query_count, 3, BLK, HD
    )
    no_pad = (0, 0)
    extended = (
        jnp.pad(window_grad[:, :, :, 0], (no_pad, no_pad, (0, 2), no_pad, no_pad))
        + jnp.pad(window_grad[:, :, :, 1], (no_pad, no_pad, (1, 1), no_pad, no_pad))
        + jnp.pad(window_grad[:, :, :, 2], (no_pad, no_pad, (2, 0), no_pad, no_pad))
    )
    outward = jnp.concatenate([extended[:, :, 0], extended[:, :, query_count + 1]], axis=2)
    inward = with_halo(outward.astype(jnp.bfloat16), (("seq", 2),), BLK).astype(outward.dtype)
    own_grad = extended[:, :, 1 : query_count + 1]
    own_grad = own_grad.at[:, :, 0].add(inward[:, :, :BLK])
    own_grad = own_grad.at[:, :, query_count - 1].add(inward[:, :, 3 * BLK :])
    random_terms = jnp.transpose(
        jnp.stack([key_random, value_random]).reshape(2, head_count, query_count * RAND, BLK, HD),
        (2, 0, 1, 3, 4),
    ).astype(jnp.bfloat16)

    def return_fast(random_terms):
        send_pick = (source[None, :] == jnp.arange(groups, dtype=jnp.int32)[:, None]).astype(
            jnp.bfloat16
        )
        outgoing = jnp.einsum(
            "pj,jxhid->pxhid", send_pick, random_terms, preferred_element_type=jnp.float32
        ).astype(jnp.bfloat16)
        incoming = lax.all_to_all(outgoing, "seq", split_axis=0, concat_axis=0, tiled=True)
        take_pick = (
            wanted_fast[None, :] == jnp.arange(2 * query_count, dtype=jnp.int32)[:, None]
        ).astype(jnp.bfloat16)
        sums = jnp.einsum("qp,pxhid->xhqid", take_pick, incoming, preferred_element_type=jnp.float32)
        back = lax.ppermute(
            sums[:, :, query_count:], "seq", [((i + shift) % groups, i) for i in range(groups)]
        )
        return sums[:, :, :query_count] + back

    def return_all(random_terms):
        send_pick = (
            places[None, :] == jnp.arange(groups * capacity, dtype=jnp.int32)[:, None]
        ).astype(jnp.bfloat16)
        outgoing = jnp.einsum(
            "pj,jxhid->pxhid", send_pick, random_terms, preferred_element_type=jnp.float32
        ).astype(jnp.bfloat16)
        incoming = lax.all_to_all(
            outgoing.reshape(groups, capacity, 2, head_count, BLK, HD),
            "seq",
            split_axis=0,
            concat_axis=0,
            tiled=True,
        )
        take_pick = (
            wanted.reshape(-1)[None, :] == jnp.arange(query_count, dtype=jnp.int32)[:, None]
        ).astype(jnp.bfloat16)
        return jnp.einsum(
            "qp,pxhid->xhqid",
            take_pick,
            incoming.reshape(groups * capacity, 2, head_count, BLK, HD),
            preferred_element_type=jnp.float32,
        )

    random_sum = lax.cond(take_fast, return_fast, return_all, random_terms)
    global_sum = global_sum.reshape(2, head_count, 2, BLK, HD)
    own_grad = own_grad.at[:, :, 0:2].add(jnp.where(my_group == 0, global_sum, 0.0))
    total_grad = (own_grad + random_sum).astype(jnp.bfloat16)
    flat = (head_count, group_tokens, HD)
    results = lax.all_to_all(
        jnp.stack([by_token(attended.reshape(flat)), by_token(grad_q.reshape(flat)),
                   by_token(total_grad[0].reshape(flat)), by_token(total_grad[1].reshape(flat))]),
        "head",
        split_axis=1,
        concat_axis=2,
        tiled=True,
    )
    return results[0], results[1], results[2], results[3]


def solution(mesh):
    placed = (
        P(("seq", "head"), None),
        P(("seq", "head"), None),
        P(("seq", "head"), None),
        P(("seq", "head"), None),
        P("seq", None),
    )
    return jax.shard_map(
        shards,
        mesh=mesh,
        in_specs=placed,
        out_specs=(
            P(("seq", "head"), None),
            P(("seq", "head"), None),
            P(("seq", "head"), None),
            P(("seq", "head"), None),
        ),
        check_vma=False,
    )
```

```python
import jax
import jax.numpy as jnp
from jax import lax
from jax.sharding import PartitionSpec as P

HD = 128
BLK = 128
RAND = 3


def with_halo(cells, sides, width):
    for axis, dim in sides:
        count = lax.axis_size(axis)
        ends = count - 1
        head = lax.slice_in_dim(cells, 0, width, axis=dim)
        tail = lax.slice_in_dim(cells, cells.shape[dim] - width, cells.shape[dim], axis=dim)
        cells = jnp.concatenate(
            [
                lax.ppermute(tail, axis, [(i, (i + 1) % count) for i in range(ends)]),
                cells,
                lax.ppermute(head, axis, [((i + 1) % count, i) for i in range(ends)]),
            ],
            axis=dim,
        )
    return cells


def row_width(count):
    return 4 if count % 4 == 0 else 1


def broadcast(value, axis):
    count = lax.axis_size(axis)
    me = lax.axis_index(axis)
    width = row_width(count)
    got = jnp.zeros_like(value)
    for row in range(1, count // width):
        got = got + lax.ppermute(value, axis, [(0, row * width)])
    value = jnp.where(me == 0, value, got)
    got = jnp.zeros_like(value)
    for col in range(1, width):
        pairs = [(row * width, row * width + col) for row in range(count // width)]
        got = got + lax.ppermute(value, axis, pairs)
    return jnp.where(me % width == 0, value, got)


def reduce_to_first(value, axis):
    count = lax.axis_size(axis)
    width = row_width(count)
    total = value
    for col in range(1, width):
        pairs = [(row * width + col, row * width) for row in range(count // width)]
        total = total + lax.ppermute(value, axis, pairs)
    value = total
    for row in range(1, count // width):
        total = total + lax.ppermute(value, axis, [(row * width, 0)])
    return total


def slot_places(owners, groups, capacity):
    owner_hits = (owners[:, None] == jnp.arange(groups, dtype=jnp.int32)[None, :]).astype(jnp.int32)
    earlier = jnp.cumsum(owner_hits, axis=0) - owner_hits
    return owners * capacity + jnp.sum(earlier * owner_hits, axis=1)


def request_table(list_rows, query_count, groups, capacity):
    flat_rows = list_rows.reshape(-1)
    places = slot_places(flat_rows // query_count, groups, capacity)
    matches = places[None, :] == jnp.arange(groups * capacity, dtype=jnp.int32)[:, None]
    table = jnp.sum(jnp.where(matches, (flat_rows % query_count)[None, :], 0), axis=1)
    return table.reshape(groups, capacity)


def mirror_shift(groups):
    return groups - 1


def route(list_rows, query_count, groups, capacity):
    flat_rows = list_rows.reshape(-1)
    owners = flat_rows // query_count
    places = slot_places(owners, groups, capacity)
    rank = places - owners * capacity
    source = jnp.where(rank == 0, owners, (owners + mirror_shift(groups)) % groups)
    held_id = jnp.where(rank == 0, flat_rows % query_count, query_count + flat_rows % query_count)
    hits = (source[None, :] == jnp.arange(groups, dtype=jnp.int32)[:, None]).astype(jnp.int32)
    fits = jnp.logical_and(jnp.all(jnp.sum(hits, axis=1) <= 1), jnp.all(rank <= 1))
    fast_table = jnp.sum(hits * held_id[None, :], axis=1)
    table = jnp.concatenate(
        [
            request_table(list_rows, query_count, groups, capacity),
            fast_table[:, None],
            jnp.broadcast_to(fits.astype(jnp.int32), (groups, 1)),
        ],
        axis=1,
    )
    return table, places, source


def window_valid(my_group, query_count, groups):
    block_ids = jnp.arange(query_count, dtype=jnp.int32)
    left_ok = jnp.logical_not(jnp.logical_and(my_group == 0, block_ids == 0))
    right_ok = jnp.logical_not(
        jnp.logical_and(my_group == groups - 1, block_ids == query_count - 1)
    )
    all_true = jnp.ones((query_count, BLK), dtype=bool)
    return jnp.concatenate(
        [
            all_true,
            all_true,
            left_ok[:, None] & all_true,
            all_true,
            right_ok[:, None] & all_true,
            jnp.ones((query_count, RAND * BLK), dtype=bool),
        ],
        axis=1,
    )


def against_keys(rows, global_part, window_part, remote_part):
    return jnp.concatenate(
        [
            jnp.einsum("hqid,hjd->hqij", rows, global_part, preferred_element_type=jnp.float32),
            jnp.einsum("hqid,hqjd->hqij", rows, window_part, preferred_element_type=jnp.float32),
            jnp.einsum("hqid,hqjd->hqij", rows, remote_part, preferred_element_type=jnp.float32),
        ],
        axis=-1,
    )


def split_keys(table):
    return (table[..., : 2 * BLK], table[..., 2 * BLK : 5 * BLK], table[..., 5 * BLK :])


def weigh_keys(table, global_part, window_part, remote_part):
    global_w, window_w, random_w = split_keys(table)
    return (
        jnp.einsum("hqij,hjd->hqid", global_w, global_part, preferred_element_type=jnp.float32)
        + jnp.einsum("hqij,hqjd->hqid", window_w, window_part, preferred_element_type=jnp.float32)
        + jnp.einsum("hqij,hqjd->hqid", random_w, remote_part, preferred_element_type=jnp.float32)
    )


def key_terms(table, rows):
    global_w, window_w, random_w = split_keys(table)
    return (
        jnp.einsum("hqij,hqid->hjd", global_w, rows, preferred_element_type=jnp.float32),
        jnp.einsum("hqij,hqid->hqjd", window_w, rows, preferred_element_type=jnp.float32),
        jnp.einsum("hqij,hqid->hqjd", random_w, rows, preferred_element_type=jnp.float32),
    )


def by_head(table, head_count):
    tokens = table.shape[0]
    return jnp.transpose(table.reshape(tokens, head_count, HD), (1, 0, 2))


def by_token(table):
    head_count, tokens = table.shape[0], table.shape[1]
    return jnp.transpose(table, (1, 0, 2)).reshape(tokens, head_count * HD)


def shards(queries, keys, values, grad_out, random_blocks):
    groups = lax.axis_size("seq")
    my_group = lax.axis_index("seq")
    head_q, head_k, head_v, head_g = lax.all_to_all(
        jnp.stack([queries, keys, values, grad_out]), "head", split_axis=2, concat_axis=1, tiled=True
    )
    group_tokens = head_q.shape[0]
    head_count = head_q.shape[1] // HD
    query_count = group_tokens // BLK
    capacity = max(2, 3 * query_count * RAND // (2 * groups))
    score_scale = HD ** (-0.5)
    ordered_table, places, source = route(random_blocks, query_count, groups, capacity)
    ordered_table, head_k = lax.optimization_barrier((ordered_table, head_k))
    shift = mirror_shift(groups)
    key_value = jnp.stack([by_head(head_k, head_count), by_head(head_v, head_count)])
    kv_blocks = key_value.reshape(2, head_count, query_count, BLK, HD)
    edged = with_halo(key_value, (("seq", 2),), BLK)
    edged = edged.reshape(2, head_count, query_count + 2, BLK, HD)
    window_kv = jnp.concatenate(
        [edged[:, :, 0:query_count], edged[:, :, 1 : query_count + 1], edged[:, :, 2 : query_count + 2]],
        axis=3,
    )
    global_kv = broadcast(kv_blocks[:, :, 0:2].reshape(2, head_count, 2 * BLK, HD), "seq")
    received = lax.all_to_all(ordered_table, "seq", split_axis=0, concat_axis=0, tiled=True)
    wanted = received[:, :capacity]
    wanted_fast = received[:, capacity]
    take_fast = jnp.all(received[:, capacity + 1] == 1)
    mirror = lax.ppermute(kv_blocks, "seq", [(i, (i + shift) % groups) for i in range(groups)])
    held = jnp.transpose(jnp.concatenate([kv_blocks, mirror], axis=2), (2, 0, 1, 3, 4))
    held, global_kv = lax.optimization_barrier((held, global_kv))

    def fetch_fast(held):
        served = jnp.take(held, wanted_fast, axis=0)
        fetched = lax.all_to_all(served, "seq", split_axis=0, concat_axis=0, tiled=True)
        return jnp.take(fetched, source, axis=0)

    def fetch_all(held):
        served = jnp.take(held[:query_count], wanted.reshape(-1), axis=0)
        served = served.reshape(groups, capacity, 2, head_count, BLK, HD)
        fetched = lax.all_to_all(served, "seq", split_axis=0, concat_axis=0, tiled=True)
        return jnp.take(fetched.reshape(groups * capacity, 2, head_count, BLK, HD), places, axis=0)

    chosen = lax.cond(take_fast, fetch_fast, fetch_all, held)
    remote_kv = jnp.transpose(
        chosen.reshape(query_count, RAND, 2, head_count, BLK, HD), (2, 3, 0, 1, 4, 5)
    ).reshape(2, head_count, query_count, RAND * BLK, HD)
    query_blocks = by_head(head_q, head_count).reshape(head_count, query_count, BLK, HD)
    grad_blocks = by_head(head_g, head_count).reshape(head_count, query_count, BLK, HD)
    scores = score_scale * against_keys(query_blocks, global_kv[0], window_kv[0], remote_kv[0])
    valid = window_valid(my_group, query_count, groups)
    scores = jnp.where(valid[None, :, None, :], scores, -jnp.inf)
    row_max = jnp.max(scores, axis=-1, keepdims=True)
    exponent = jnp.exp(scores - row_max)
    attention_probs = exponent / jnp.sum(exponent, axis=-1, keepdims=True)
    weights = attention_probs.astype(jnp.bfloat16)
    attended = weigh_keys(weights, global_kv[1], window_kv[1], remote_kv[1]).astype(jnp.bfloat16)
    grad_prob = against_keys(grad_blocks, global_kv[1], window_kv[1], remote_kv[1])
    row_delta = jnp.sum(attention_probs * grad_prob, axis=-1, keepdims=True)
    grad_score = (score_scale * attention_probs * (grad_prob - row_delta)).astype(jnp.bfloat16)
    grad_q = weigh_keys(grad_score, global_kv[0], window_kv[0], remote_kv[0]).astype(jnp.bfloat16)
    key_global, key_window, key_random = key_terms(grad_score, query_blocks)
    value_global, value_window, value_random = key_terms(weights, grad_blocks)
    global_sum = reduce_to_first(jnp.stack([key_global, value_global]), "seq")
    window_grad = jnp.stack([key_window, value_window]).reshape(
        2, head_count, query_count, 3, BLK, HD
    )
    no_pad = (0, 0)
    extended = (
        jnp.pad(window_grad[:, :, :, 0], (no_pad, no_pad, (0, 2), no_pad, no_pad))
        + jnp.pad(window_grad[:, :, :, 1], (no_pad, no_pad, (1, 1), no_pad, no_pad))
        + jnp.pad(window_grad[:, :, :, 2], (no_pad, no_pad, (2, 0), no_pad, no_pad))
    )
    outward = jnp.concatenate([extended[:, :, 0], extended[:, :, query_count + 1]], axis=2)
    inward = with_halo(outward.astype(jnp.bfloat16), (("seq", 2),), BLK).astype(outward.dtype)
    own_grad = extended[:, :, 1 : query_count + 1]
    own_grad = own_grad.at[:, :, 0].add(inward[:, :, :BLK])
    own_grad = own_grad.at[:, :, query_count - 1].add(inward[:, :, 3 * BLK :])
    random_terms = jnp.transpose(
        jnp.stack([key_random, value_random]).reshape(2, head_count, query_count * RAND, BLK, HD),
        (2, 0, 1, 3, 4),
    ).astype(jnp.bfloat16)

    def return_fast(random_terms):
        send_pick = (source[None, :] == jnp.arange(groups, dtype=jnp.int32)[:, None]).astype(
            jnp.bfloat16
        )
        outgoing = jnp.einsum(
            "pj,jxhid->pxhid", send_pick, random_terms, preferred_element_type=jnp.float32
        ).astype(jnp.bfloat16)
        incoming = lax.all_to_all(outgoing, "seq", split_axis=0, concat_axis=0, tiled=True)
        take_pick = (
            wanted_fast[None, :] == jnp.arange(2 * query_count, dtype=jnp.int32)[:, None]
        ).astype(jnp.bfloat16)
        sums = jnp.einsum("qp,pxhid->xhqid", take_pick, incoming, preferred_element_type=jnp.float32)
        back = lax.ppermute(
            sums[:, :, query_count:], "seq", [((i + shift) % groups, i) for i in range(groups)]
        )
        return sums[:, :, :query_count] + back

    def return_all(random_terms):
        send_pick = (
            places[None, :] == jnp.arange(groups * capacity, dtype=jnp.int32)[:, None]
        ).astype(jnp.bfloat16)
        outgoing = jnp.einsum(
            "pj,jxhid->pxhid", send_pick, random_terms, preferred_element_type=jnp.float32
        ).astype(jnp.bfloat16)
        incoming = lax.all_to_all(
            outgoing.reshape(groups, capacity, 2, head_count, BLK, HD),
            "seq",
            split_axis=0,
            concat_axis=0,
            tiled=True,
        )
        take_pick = (
            wanted.reshape(-1)[None, :] == jnp.arange(query_count, dtype=jnp.int32)[:, None]
        ).astype(jnp.bfloat16)
        return jnp.einsum(
            "qp,pxhid->xhqid",
            take_pick,
            incoming.reshape(groups * capacity, 2, head_count, BLK, HD),
            preferred_element_type=jnp.float32,
        )

    random_sum = lax.cond(take_fast, return_fast, return_all, random_terms)
    global_sum = global_sum.reshape(2, head_count, 2, BLK, HD)
    own_grad = own_grad.at[:, :, 0:2].add(jnp.where(my_group == 0, global_sum, 0.0))
    total_grad = (own_grad + random_sum).astype(jnp.bfloat16)
    flat = (head_count, group_tokens, HD)
    results = lax.all_to_all(
        jnp.stack([by_token(attended.reshape(flat)), by_token(grad_q.reshape(flat)),
                   by_token(total_grad[0].reshape(flat)), by_token(total_grad[1].reshape(flat))]),
        "head",
        split_axis=1,
        concat_axis=2,
        tiled=True,
    )
    return results[0], results[1], results[2], results[3]


def solution(mesh):
    placed = (
        P(("seq", "head"), None),
        P(("seq", "head"), None),
        P(("seq", "head"), None),
        P(("seq", "head"), None),
        P("seq", None),
    )
    return jax.shard_map(
        shards,
        mesh=mesh,
        in_specs=placed,
        out_specs=(
            P(("seq", "head"), None),
            P(("seq", "head"), None),
            P(("seq", "head"), None),
            P(("seq", "head"), None),
        ),
        check_vma=False,
    )
```

```python
import jax
import jax.numpy as jnp
from jax import lax
from jax.sharding import PartitionSpec as P

HD = 128
BLK = 128
RAND = 3


def with_halo(cells, sides, width):
    for axis, dim in sides:
        count = lax.axis_size(axis)
        ends = count - 1
        head = lax.slice_in_dim(cells, 0, width, axis=dim)
        tail = lax.slice_in_dim(cells, cells.shape[dim] - width, cells.shape[dim], axis=dim)
        cells = jnp.concatenate(
            [
                lax.ppermute(tail, axis, [(i, (i + 1) % count) for i in range(ends)]),
                cells,
                lax.ppermute(head, axis, [((i + 1) % count, i) for i in range(ends)]),
            ],
            axis=dim,
        )
    return cells


def row_width(count):
    return 4 if count % 4 == 0 else 1


def broadcast(value, axis):
    count = lax.axis_size(axis)
    me = lax.axis_index(axis)
    width = row_width(count)
    got = jnp.zeros_like(value)
    for row in range(1, count // width):
        got = got + lax.ppermute(value, axis, [(0, row * width)])
    value = jnp.where(me == 0, value, got)
    got = jnp.zeros_like(value)
    for col in range(1, width):
        pairs = [(row * width, row * width + col) for row in range(count // width)]
        got = got + lax.ppermute(value, axis, pairs)
    return jnp.where(me % width == 0, value, got)


def reduce_to_first(value, axis):
    count = lax.axis_size(axis)
    width = row_width(count)
    total = value.astype(jnp.float32)
    for col in range(1, width):
        pairs = [(row * width + col, row * width) for row in range(count // width)]
        total = total + lax.ppermute(value, axis, pairs)
    value = total.astype(jnp.bfloat16)
    for row in range(1, count // width):
        total = total + lax.ppermute(value, axis, [(row * width, 0)])
    return total


def slot_places(owners, groups, capacity):
    owner_hits = (owners[:, None] == jnp.arange(groups, dtype=jnp.int32)[None, :]).astype(jnp.int32)
    earlier = jnp.cumsum(owner_hits, axis=0) - owner_hits
    return owners * capacity + jnp.sum(earlier * owner_hits, axis=1)


def request_table(list_rows, query_count, groups, capacity):
    flat_rows = list_rows.reshape(-1)
    places = slot_places(flat_rows // query_count, groups, capacity)
    matches = places[None, :] == jnp.arange(groups * capacity, dtype=jnp.int32)[:, None]
    table = jnp.sum(jnp.where(matches, (flat_rows % query_count)[None, :], 0), axis=1)
    return table.reshape(groups, capacity)


def mirror_shift(groups):
    return groups - 1


def route(list_rows, query_count, groups, capacity):
    flat_rows = list_rows.reshape(-1)
    owners = flat_rows // query_count
    places = slot_places(owners, groups, capacity)
    rank = places - owners * capacity
    source = jnp.where(rank == 0, owners, (owners + mirror_shift(groups)) % groups)
    held_id = jnp.where(rank == 0, flat_rows % query_count, query_count + flat_rows % query_count)
    hits = (source[None, :] == jnp.arange(groups, dtype=jnp.int32)[:, None]).astype(jnp.int32)
    fits = jnp.logical_and(jnp.all(jnp.sum(hits, axis=1) <= 1), jnp.all(rank <= 1))
    fast_table = jnp.sum(hits * held_id[None, :], axis=1)
    table = jnp.concatenate(
        [
            request_table(list_rows, query_count, groups, capacity),
            fast_table[:, None],
            jnp.broadcast_to(fits.astype(jnp.int32), (groups, 1)),
        ],
        axis=1,
    )
    return table, places, source


def window_valid(my_group, query_count, groups):
    block_ids = jnp.arange(query_count, dtype=jnp.int32)
    left_ok = jnp.logical_not(jnp.logical_and(my_group == 0, block_ids == 0))
    right_ok = jnp.logical_not(
        jnp.logical_and(my_group == groups - 1, block_ids == query_count - 1)
    )
    all_true = jnp.ones((query_count, BLK), dtype=bool)
    return jnp.concatenate(
        [
            all_true,
            all_true,
            left_ok[:, None] & all_true,
            all_true,
            right_ok[:, None] & all_true,
            jnp.ones((query_count, RAND * BLK), dtype=bool),
        ],
        axis=1,
    )


def against_keys(rows, global_part, window_part, remote_part):
    return jnp.concatenate(
        [
            jnp.einsum("hqid,hjd->hqij", rows, global_part, preferred_element_type=jnp.float32),
            jnp.einsum("hqid,hqjd->hqij", rows, window_part, preferred_element_type=jnp.float32),
            jnp.einsum("hqid,hqjd->hqij", rows, remote_part, preferred_element_type=jnp.float32),
        ],
        axis=-1,
    )


def split_keys(table):
    return (table[..., : 2 * BLK], table[..., 2 * BLK : 5 * BLK], table[..., 5 * BLK :])


def weigh_keys(table, global_part, window_part, remote_part):
    global_w, window_w, random_w = split_keys(table)
    return (
        jnp.einsum("hqij,hjd->hqid", global_w, global_part, preferred_element_type=jnp.float32)
        + jnp.einsum("hqij,hqjd->hqid", window_w, window_part, preferred_element_type=jnp.float32)
        + jnp.einsum("hqij,hqjd->hqid", random_w, remote_part, preferred_element_type=jnp.float32)
    )


def key_terms(table, rows):
    global_w, window_w, random_w = split_keys(table)
    return (
        jnp.einsum("hqij,hqid->hjd", global_w, rows, preferred_element_type=jnp.float32),
        jnp.einsum("hqij,hqid->hqjd", window_w, rows, preferred_element_type=jnp.float32),
        jnp.einsum("hqij,hqid->hqjd", random_w, rows, preferred_element_type=jnp.float32),
    )


def by_head(table, head_count):
    tokens = table.shape[0]
    return jnp.transpose(table.reshape(tokens, head_count, HD), (1, 0, 2))


def by_token(table):
    head_count, tokens = table.shape[0], table.shape[1]
    return jnp.transpose(table, (1, 0, 2)).reshape(tokens, head_count * HD)


def shards(queries, keys, values, grad_out, random_blocks):
    groups = lax.axis_size("seq")
    my_group = lax.axis_index("seq")
    head_q, head_k, head_v, head_g = lax.all_to_all(
        jnp.stack([queries, keys, values, grad_out]), "head", split_axis=2, concat_axis=1, tiled=True
    )
    group_tokens = head_q.shape[0]
    head_count = head_q.shape[1] // HD
    query_count = group_tokens // BLK
    capacity = max(2, 3 * query_count * RAND // (2 * groups))
    score_scale = HD ** (-0.5)
    ordered_table, places, source = route(random_blocks, query_count, groups, capacity)
    ordered_table, head_k = lax.optimization_barrier((ordered_table, head_k))
    shift = mirror_shift(groups)
    key_value = jnp.stack([by_head(head_k, head_count), by_head(head_v, head_count)])
    kv_blocks = key_value.reshape(2, head_count, query_count, BLK, HD)
    edged = with_halo(key_value, (("seq", 2),), BLK)
    edged = edged.reshape(2, head_count, query_count + 2, BLK, HD)
    window_kv = jnp.concatenate(
        [edged[:, :, 0:query_count], edged[:, :, 1 : query_count + 1], edged[:, :, 2 : query_count + 2]],
        axis=3,
    )
    global_kv = broadcast(kv_blocks[:, :, 0:2].reshape(2, head_count, 2 * BLK, HD), "seq")
    received = lax.all_to_all(ordered_table, "seq", split_axis=0, concat_axis=0, tiled=True)
    wanted = received[:, :capacity]
    wanted_fast = received[:, capacity]
    take_fast = jnp.all(received[:, capacity + 1] == 1)
    mirror = lax.ppermute(kv_blocks, "seq", [(i, (i + shift) % groups) for i in range(groups)])
    held = jnp.transpose(jnp.concatenate([kv_blocks, mirror], axis=2), (2, 0, 1, 3, 4))
    held, global_kv = lax.optimization_barrier((held, global_kv))

    def fetch_fast(held):
        served = jnp.take(held, wanted_fast, axis=0)
        fetched = lax.all_to_all(served, "seq", split_axis=0, concat_axis=0, tiled=True)
        return jnp.take(fetched, source, axis=0)

    def fetch_all(held):
        served = jnp.take(held[:query_count], wanted.reshape(-1), axis=0)
        served = served.reshape(groups, capacity, 2, head_count, BLK, HD)
        fetched = lax.all_to_all(served, "seq", split_axis=0, concat_axis=0, tiled=True)
        return jnp.take(fetched.reshape(groups * capacity, 2, head_count, BLK, HD), places, axis=0)

    chosen = lax.cond(take_fast, fetch_fast, fetch_all, held)
    remote_kv = jnp.transpose(
        chosen.reshape(query_count, RAND, 2, head_count, BLK, HD), (2, 3, 0, 1, 4, 5)
    ).reshape(2, head_count, query_count, RAND * BLK, HD)
    query_blocks = by_head(head_q, head_count).reshape(head_count, query_count, BLK, HD)
    grad_blocks = by_head(head_g, head_count).reshape(head_count, query_count, BLK, HD)
    scores = score_scale * against_keys(query_blocks, global_kv[0], window_kv[0], remote_kv[0])
    valid = window_valid(my_group, query_count, groups)
    scores = jnp.where(valid[None, :, None, :], scores, -jnp.inf)
    row_max = jnp.max(scores, axis=-1, keepdims=True)
    exponent = jnp.exp(scores - row_max)
    attention_probs = exponent / jnp.sum(exponent, axis=-1, keepdims=True)
    weights = attention_probs.astype(jnp.bfloat16)
    attended = weigh_keys(weights, global_kv[1], window_kv[1], remote_kv[1]).astype(jnp.bfloat16)
    grad_prob = against_keys(grad_blocks, global_kv[1], window_kv[1], remote_kv[1])
    row_delta = jnp.sum(attention_probs * grad_prob, axis=-1, keepdims=True)
    grad_score = (score_scale * attention_probs * (grad_prob - row_delta)).astype(jnp.bfloat16)
    grad_q = weigh_keys(grad_score, global_kv[0], window_kv[0], remote_kv[0]).astype(jnp.bfloat16)
    key_global, key_window, key_random = key_terms(grad_score, query_blocks)
    value_global, value_window, value_random = key_terms(weights, grad_blocks)
    global_sum = reduce_to_first(jnp.stack([key_global, value_global]).astype(jnp.bfloat16), "seq")
    window_grad = jnp.stack([key_window, value_window]).reshape(
        2, head_count, query_count, 3, BLK, HD
    )
    no_pad = (0, 0)
    extended = (
        jnp.pad(window_grad[:, :, :, 0], (no_pad, no_pad, (0, 2), no_pad, no_pad))
        + jnp.pad(window_grad[:, :, :, 1], (no_pad, no_pad, (1, 1), no_pad, no_pad))
        + jnp.pad(window_grad[:, :, :, 2], (no_pad, no_pad, (2, 0), no_pad, no_pad))
    )
    outward = jnp.concatenate([extended[:, :, 0], extended[:, :, query_count + 1]], axis=2)
    inward = with_halo(outward.astype(jnp.bfloat16), (("seq", 2),), BLK).astype(outward.dtype)
    own_grad = extended[:, :, 1 : query_count + 1]
    own_grad = own_grad.at[:, :, 0].add(inward[:, :, :BLK])
    own_grad = own_grad.at[:, :, query_count - 1].add(inward[:, :, 3 * BLK :])
    random_terms = jnp.transpose(
        jnp.stack([key_random, value_random]).reshape(2, head_count, query_count * RAND, BLK, HD),
        (2, 0, 1, 3, 4),
    ).astype(jnp.bfloat16)

    def return_fast(random_terms):
        send_pick = (source[None, :] == jnp.arange(groups, dtype=jnp.int32)[:, None]).astype(
            jnp.bfloat16
        )
        outgoing = jnp.einsum(
            "pj,jxhid->pxhid", send_pick, random_terms, preferred_element_type=jnp.float32
        ).astype(jnp.bfloat16)
        incoming = lax.all_to_all(outgoing, "seq", split_axis=0, concat_axis=0, tiled=True)
        take_pick = (
            wanted_fast[None, :] == jnp.arange(2 * query_count, dtype=jnp.int32)[:, None]
        ).astype(jnp.bfloat16)
        sums = jnp.einsum("qp,pxhid->xhqid", take_pick, incoming, preferred_element_type=jnp.float32)
        back = lax.ppermute(
            sums[:, :, query_count:].astype(jnp.bfloat16),
            "seq",
            [((i + shift) % groups, i) for i in range(groups)],
        )
        return sums[:, :, :query_count] + back

    def return_all(random_terms):
        send_pick = (
            places[None, :] == jnp.arange(groups * capacity, dtype=jnp.int32)[:, None]
        ).astype(jnp.bfloat16)
        outgoing = jnp.einsum(
            "pj,jxhid->pxhid", send_pick, random_terms, preferred_element_type=jnp.float32
        ).astype(jnp.bfloat16)
        incoming = lax.all_to_all(
            outgoing.reshape(groups, capacity, 2, head_count, BLK, HD),
            "seq",
            split_axis=0,
            concat_axis=0,
            tiled=True,
        )
        take_pick = (
            wanted.reshape(-1)[None, :] == jnp.arange(query_count, dtype=jnp.int32)[:, None]
        ).astype(jnp.bfloat16)
        return jnp.einsum(
            "qp,pxhid->xhqid",
            take_pick,
            incoming.reshape(groups * capacity, 2, head_count, BLK, HD),
            preferred_element_type=jnp.float32,
        )

    random_sum = lax.cond(take_fast, return_fast, return_all, random_terms)
    global_sum = global_sum.reshape(2, head_count, 2, BLK, HD)
    own_grad = own_grad.at[:, :, 0:2].add(jnp.where(my_group == 0, global_sum, 0.0))
    total_grad = (own_grad + random_sum).astype(jnp.bfloat16)
    flat = (head_count, group_tokens, HD)
    results = lax.all_to_all(
        jnp.stack([by_token(attended.reshape(flat)), by_token(grad_q.reshape(flat)),
                   by_token(total_grad[0].reshape(flat)), by_token(total_grad[1].reshape(flat))]),
        "head",
        split_axis=1,
        concat_axis=2,
        tiled=True,
    )
    return results[0], results[1], results[2], results[3]


def solution(mesh):
    placed = (
        P(("seq", "head"), None),
        P(("seq", "head"), None),
        P(("seq", "head"), None),
        P(("seq", "head"), None),
        P("seq", None),
    )
    return jax.shard_map(
        shards,
        mesh=mesh,
        in_specs=placed,
        out_specs=(
            P(("seq", "head"), None),
            P(("seq", "head"), None),
            P(("seq", "head"), None),
            P(("seq", "head"), None),
        ),
        check_vma=False,
    )
```

```python
import jax
import jax.numpy as jnp
from jax import lax
from jax.sharding import PartitionSpec as P

HD = 128
BLK = 128
RAND = 3


def with_halo(cells, sides, width):
    for axis, dim in sides:
        count = lax.axis_size(axis)
        ends = count - 1
        head = lax.slice_in_dim(cells, 0, width, axis=dim)
        tail = lax.slice_in_dim(cells, cells.shape[dim] - width, cells.shape[dim], axis=dim)
        cells = jnp.concatenate(
            [
                lax.ppermute(tail, axis, [(i, (i + 1) % count) for i in range(ends)]),
                cells,
                lax.ppermute(head, axis, [((i + 1) % count, i) for i in range(ends)]),
            ],
            axis=dim,
        )
    return cells


def row_width(count):
    return 4 if count % 4 == 0 else 1


def broadcast(value, axis):
    count = lax.axis_size(axis)
    me = lax.axis_index(axis)
    width = row_width(count)
    rows = count // width
    my_row = me // width
    step = 1
    while step < rows:
        pairs = [(row * width, (row + step) * width) for row in range(step) if row + step < rows]
        got = lax.ppermute(value, axis, pairs)
        arrived = (me % width == 0) & (my_row >= step) & (my_row < 2 * step)
        value = jnp.where(arrived, got, value)
        step *= 2
    got = jnp.zeros_like(value)
    for col in range(1, width):
        pairs = [(row * width, row * width + col) for row in range(rows)]
        got = got + lax.ppermute(value, axis, pairs)
    return jnp.where(me % width == 0, value, got)


def reduce_to_first(value, axis):
    count = lax.axis_size(axis)
    width = row_width(count)
    total = value.astype(jnp.float32)
    for col in range(1, width):
        pairs = [(row * width + col, row * width) for row in range(count // width)]
        total = total + lax.ppermute(value, axis, pairs)
    value = total.astype(jnp.bfloat16)
    for row in range(1, count // width):
        total = total + lax.ppermute(value, axis, [(row * width, 0)])
    return total


def slot_places(owners, groups, capacity):
    owner_hits = (owners[:, None] == jnp.arange(groups, dtype=jnp.int32)[None, :]).astype(jnp.int32)
    earlier = jnp.cumsum(owner_hits, axis=0) - owner_hits
    return owners * capacity + jnp.sum(earlier * owner_hits, axis=1)


def request_table(list_rows, query_count, groups, capacity):
    flat_rows = list_rows.reshape(-1)
    places = slot_places(flat_rows // query_count, groups, capacity)
    matches = places[None, :] == jnp.arange(groups * capacity, dtype=jnp.int32)[:, None]
    table = jnp.sum(jnp.where(matches, (flat_rows % query_count)[None, :], 0), axis=1)
    return table.reshape(groups, capacity)


def mirror_shift(groups):
    return groups - 1


def route(list_rows, query_count, groups, capacity):
    flat_rows = list_rows.reshape(-1)
    owners = flat_rows // query_count
    places = slot_places(owners, groups, capacity)
    rank = places - owners * capacity
    source = jnp.where(rank == 0, owners, (owners + mirror_shift(groups)) % groups)
    held_id = jnp.where(rank == 0, flat_rows % query_count, query_count + flat_rows % query_count)
    hits = (source[None, :] == jnp.arange(groups, dtype=jnp.int32)[:, None]).astype(jnp.int32)
    fits = jnp.logical_and(jnp.all(jnp.sum(hits, axis=1) <= 1), jnp.all(rank <= 1))
    fast_table = jnp.sum(hits * held_id[None, :], axis=1)
    table = jnp.concatenate(
        [
            request_table(list_rows, query_count, groups, capacity),
            fast_table[:, None],
            jnp.broadcast_to(fits.astype(jnp.int32), (groups, 1)),
        ],
        axis=1,
    )
    return table, places, source


def window_valid(my_group, query_count, groups):
    block_ids = jnp.arange(query_count, dtype=jnp.int32)
    left_ok = jnp.logical_not(jnp.logical_and(my_group == 0, block_ids == 0))
    right_ok = jnp.logical_not(
        jnp.logical_and(my_group == groups - 1, block_ids == query_count - 1)
    )
    all_true = jnp.ones((query_count, BLK), dtype=bool)
    return jnp.concatenate(
        [
            all_true,
            all_true,
            left_ok[:, None] & all_true,
            all_true,
            right_ok[:, None] & all_true,
            jnp.ones((query_count, RAND * BLK), dtype=bool),
        ],
        axis=1,
    )


def against_keys(rows, global_part, window_part, remote_part):
    return jnp.concatenate(
        [
            jnp.einsum("hqid,hjd->hqij", rows, global_part, preferred_element_type=jnp.float32),
            jnp.einsum("hqid,hqjd->hqij", rows, window_part, preferred_element_type=jnp.float32),
            jnp.einsum("hqid,hqjd->hqij", rows, remote_part, preferred_element_type=jnp.float32),
        ],
        axis=-1,
    )


def split_keys(table):
    return (table[..., : 2 * BLK], table[..., 2 * BLK : 5 * BLK], table[..., 5 * BLK :])


def weigh_keys(table, global_part, window_part, remote_part):
    global_w, window_w, random_w = split_keys(table)
    return (
        jnp.einsum("hqij,hjd->hqid", global_w, global_part, preferred_element_type=jnp.float32)
        + jnp.einsum("hqij,hqjd->hqid", window_w, window_part, preferred_element_type=jnp.float32)
        + jnp.einsum("hqij,hqjd->hqid", random_w, remote_part, preferred_element_type=jnp.float32)
    )


def key_terms(table, rows):
    global_w, window_w, random_w = split_keys(table)
    return (
        jnp.einsum("hqij,hqid->hjd", global_w, rows, preferred_element_type=jnp.float32),
        jnp.einsum("hqij,hqid->hqjd", window_w, rows, preferred_element_type=jnp.float32),
        jnp.einsum("hqij,hqid->hqjd", random_w, rows, preferred_element_type=jnp.float32),
    )


def by_head(table, head_count):
    tokens = table.shape[0]
    return jnp.transpose(table.reshape(tokens, head_count, HD), (1, 0, 2))


def by_token(table):
    head_count, tokens = table.shape[0], table.shape[1]
    return jnp.transpose(table, (1, 0, 2)).reshape(tokens, head_count * HD)


def shards(queries, keys, values, grad_out, random_blocks):
    groups = lax.axis_size("seq")
    my_group = lax.axis_index("seq")
    head_q, head_k, head_v, head_g = lax.all_to_all(
        jnp.stack([queries, keys, values, grad_out]), "head", split_axis=2, concat_axis=1, tiled=True
    )
    group_tokens = head_q.shape[0]
    head_count = head_q.shape[1] // HD
    query_count = group_tokens // BLK
    capacity = max(2, 3 * query_count * RAND // (2 * groups))
    score_scale = HD ** (-0.5)
    ordered_table, places, source = route(random_blocks, query_count, groups, capacity)
    ordered_table, head_k = lax.optimization_barrier((ordered_table, head_k))
    shift = mirror_shift(groups)
    key_value = jnp.stack([by_head(head_k, head_count), by_head(head_v, head_count)])
    kv_blocks = key_value.reshape(2, head_count, query_count, BLK, HD)
    mirror = lax.ppermute(kv_blocks, "seq", [(i, (i + shift) % groups) for i in range(groups)])
    left = lax.ppermute(
        key_value[:, :, group_tokens - BLK :], "seq", [(i, i + 1) for i in range(groups - 1)]
    )
    edged = jnp.concatenate([left, key_value, mirror[:, :, 0]], axis=2)
    edged = edged.reshape(2, head_count, query_count + 2, BLK, HD)
    window_kv = jnp.concatenate(
        [edged[:, :, 0:query_count], edged[:, :, 1 : query_count + 1], edged[:, :, 2 : query_count + 2]],
        axis=3,
    )
    global_kv = broadcast(kv_blocks[:, :, 0:2].reshape(2, head_count, 2 * BLK, HD), "seq")
    received = lax.all_to_all(ordered_table, "seq", split_axis=0, concat_axis=0, tiled=True)
    wanted = received[:, :capacity]
    wanted_fast = received[:, capacity]
    take_fast = jnp.all(received[:, capacity + 1] == 1)
    held = jnp.transpose(jnp.concatenate([kv_blocks, mirror], axis=2), (2, 0, 1, 3, 4))
    held, global_kv = lax.optimization_barrier((held, global_kv))

    def fetch_fast(held):
        served = jnp.take(held, wanted_fast, axis=0)
        fetched = lax.all_to_all(served, "seq", split_axis=0, concat_axis=0, tiled=True)
        return jnp.take(fetched, source, axis=0)

    def fetch_all(held):
        served = jnp.take(held[:query_count], wanted.reshape(-1), axis=0)
        served = served.reshape(groups, capacity, 2, head_count, BLK, HD)
        fetched = lax.all_to_all(served, "seq", split_axis=0, concat_axis=0, tiled=True)
        return jnp.take(fetched.reshape(groups * capacity, 2, head_count, BLK, HD), places, axis=0)

    chosen = lax.cond(take_fast, fetch_fast, fetch_all, held)
    remote_kv = jnp.transpose(
        chosen.reshape(query_count, RAND, 2, head_count, BLK, HD), (2, 3, 0, 1, 4, 5)
    ).reshape(2, head_count, query_count, RAND * BLK, HD)
    query_blocks = by_head(head_q, head_count).reshape(head_count, query_count, BLK, HD)
    grad_blocks = by_head(head_g, head_count).reshape(head_count, query_count, BLK, HD)
    scores = score_scale * against_keys(query_blocks, global_kv[0], window_kv[0], remote_kv[0])
    valid = window_valid(my_group, query_count, groups)
    scores = jnp.where(valid[None, :, None, :], scores, -jnp.inf)
    row_max = jnp.max(scores, axis=-1, keepdims=True)
    exponent = jnp.exp(scores - row_max)
    attention_probs = exponent / jnp.sum(exponent, axis=-1, keepdims=True)
    weights = attention_probs.astype(jnp.bfloat16)
    attended = weigh_keys(weights, global_kv[1], window_kv[1], remote_kv[1]).astype(jnp.bfloat16)
    grad_prob = against_keys(grad_blocks, global_kv[1], window_kv[1], remote_kv[1])
    row_delta = jnp.sum(attention_probs * grad_prob, axis=-1, keepdims=True)
    grad_score = (score_scale * attention_probs * (grad_prob - row_delta)).astype(jnp.bfloat16)
    grad_q = weigh_keys(grad_score, global_kv[0], window_kv[0], remote_kv[0]).astype(jnp.bfloat16)
    key_global, key_window, key_random = key_terms(grad_score, query_blocks)
    value_global, value_window, value_random = key_terms(weights, grad_blocks)
    global_sum = reduce_to_first(jnp.stack([key_global, value_global]).astype(jnp.bfloat16), "seq")
    window_grad = jnp.stack([key_window, value_window]).reshape(
        2, head_count, query_count, 3, BLK, HD
    )
    no_pad = (0, 0)
    extended = (
        jnp.pad(window_grad[:, :, :, 0], (no_pad, no_pad, (0, 2), no_pad, no_pad))
        + jnp.pad(window_grad[:, :, :, 1], (no_pad, no_pad, (1, 1), no_pad, no_pad))
        + jnp.pad(window_grad[:, :, :, 2], (no_pad, no_pad, (2, 0), no_pad, no_pad))
    )
    outward = jnp.concatenate([extended[:, :, 0], extended[:, :, query_count + 1]], axis=2)
    inward = with_halo(outward.astype(jnp.bfloat16), (("seq", 2),), BLK).astype(outward.dtype)
    own_grad = extended[:, :, 1 : query_count + 1]
    own_grad = own_grad.at[:, :, 0].add(inward[:, :, :BLK])
    own_grad = own_grad.at[:, :, query_count - 1].add(inward[:, :, 3 * BLK :])
    random_terms = jnp.transpose(
        jnp.stack([key_random, value_random]).reshape(2, head_count, query_count * RAND, BLK, HD),
        (2, 0, 1, 3, 4),
    ).astype(jnp.bfloat16)

    def return_fast(random_terms):
        send_pick = (source[None, :] == jnp.arange(groups, dtype=jnp.int32)[:, None]).astype(
            jnp.bfloat16
        )
        outgoing = jnp.einsum(
            "pj,jxhid->pxhid", send_pick, random_terms, preferred_element_type=jnp.float32
        ).astype(jnp.bfloat16)
        incoming = lax.all_to_all(outgoing, "seq", split_axis=0, concat_axis=0, tiled=True)
        take_pick = (
            wanted_fast[None, :] == jnp.arange(2 * query_count, dtype=jnp.int32)[:, None]
        ).astype(jnp.bfloat16)
        sums = jnp.einsum("qp,pxhid->xhqid", take_pick, incoming, preferred_element_type=jnp.float32)
        back = lax.ppermute(
            sums[:, :, query_count:].astype(jnp.bfloat16),
            "seq",
            [((i + shift) % groups, i) for i in range(groups)],
        )
        return sums[:, :, :query_count] + back

    def return_all(random_terms):
        send_pick = (
            places[None, :] == jnp.arange(groups * capacity, dtype=jnp.int32)[:, None]
        ).astype(jnp.bfloat16)
        outgoing = jnp.einsum(
            "pj,jxhid->pxhid", send_pick, random_terms, preferred_element_type=jnp.float32
        ).astype(jnp.bfloat16)
        incoming = lax.all_to_all(
            outgoing.reshape(groups, capacity, 2, head_count, BLK, HD),
            "seq",
            split_axis=0,
            concat_axis=0,
            tiled=True,
        )
        take_pick = (
            wanted.reshape(-1)[None, :] == jnp.arange(query_count, dtype=jnp.int32)[:, None]
        ).astype(jnp.bfloat16)
        return jnp.einsum(
            "qp,pxhid->xhqid",
            take_pick,
            incoming.reshape(groups * capacity, 2, head_count, BLK, HD),
            preferred_element_type=jnp.float32,
        )

    random_sum = lax.cond(take_fast, return_fast, return_all, random_terms)
    global_sum = global_sum.reshape(2, head_count, 2, BLK, HD)
    own_grad = own_grad.at[:, :, 0:2].add(jnp.where(my_group == 0, global_sum, 0.0))
    total_grad = (own_grad + random_sum).astype(jnp.bfloat16)
    flat = (head_count, group_tokens, HD)
    results = lax.all_to_all(
        jnp.stack([by_token(attended.reshape(flat)), by_token(grad_q.reshape(flat)),
                   by_token(total_grad[0].reshape(flat)), by_token(total_grad[1].reshape(flat))]),
        "head",
        split_axis=1,
        concat_axis=2,
        tiled=True,
    )
    return results[0], results[1], results[2], results[3]


def solution(mesh):
    placed = (
        P(("seq", "head"), None),
        P(("seq", "head"), None),
        P(("seq", "head"), None),
        P(("seq", "head"), None),
        P("seq", None),
    )
    return jax.shard_map(
        shards,
        mesh=mesh,
        in_specs=placed,
        out_specs=(
            P(("seq", "head"), None),
            P(("seq", "head"), None),
            P(("seq", "head"), None),
            P(("seq", "head"), None),
        ),
        check_vma=False,
    )
```

```python
import jax
import jax.numpy as jnp
from jax import lax
from jax.sharding import PartitionSpec as P

HD = 128
BLK = 128
RAND = 3


def with_halo(cells, sides, width):
    for axis, dim in sides:
        count = lax.axis_size(axis)
        ends = count - 1
        head = lax.slice_in_dim(cells, 0, width, axis=dim)
        tail = lax.slice_in_dim(cells, cells.shape[dim] - width, cells.shape[dim], axis=dim)
        cells = jnp.concatenate(
            [
                lax.ppermute(tail, axis, [(i, (i + 1) % count) for i in range(ends)]),
                cells,
                lax.ppermute(head, axis, [((i + 1) % count, i) for i in range(ends)]),
            ],
            axis=dim,
        )
    return cells


def row_width(count):
    return 4 if count % 4 == 0 else 1


def broadcast(value, axis):
    count = lax.axis_size(axis)
    me = lax.axis_index(axis)
    width = row_width(count)
    rows = count // width
    my_row = me // width
    step = 1
    while step < rows:
        pairs = [(row * width, (row + step) * width) for row in range(step) if row + step < rows]
        got = lax.ppermute(value, axis, pairs)
        arrived = (me % width == 0) & (my_row >= step) & (my_row < 2 * step)
        value = jnp.where(arrived, got, value)
        step *= 2
    got = jnp.zeros_like(value)
    for col in range(1, width):
        pairs = [(row * width, row * width + col) for row in range(rows)]
        got = got + lax.ppermute(value, axis, pairs)
    return jnp.where(me % width == 0, value, got)


def reduce_to_first(value, axis):
    count = lax.axis_size(axis)
    width = row_width(count)
    total = value.astype(jnp.float32)
    for col in range(1, width):
        pairs = [(row * width + col, row * width) for row in range(count // width)]
        total = total + lax.ppermute(value, axis, pairs)
    value = total.astype(jnp.bfloat16)
    for row in range(1, count // width):
        total = total + lax.ppermute(value, axis, [(row * width, 0)])
    return total


def slot_places(owners, groups, capacity):
    owner_hits = (owners[:, None] == jnp.arange(groups, dtype=jnp.int32)[None, :]).astype(jnp.int32)
    earlier = jnp.cumsum(owner_hits, axis=0) - owner_hits
    return owners * capacity + jnp.sum(earlier * owner_hits, axis=1)


def request_table(list_rows, query_count, groups, capacity):
    flat_rows = list_rows.reshape(-1)
    places = slot_places(flat_rows // query_count, groups, capacity)
    matches = places[None, :] == jnp.arange(groups * capacity, dtype=jnp.int32)[:, None]
    table = jnp.sum(jnp.where(matches, (flat_rows % query_count)[None, :], 0), axis=1)
    return table.reshape(groups, capacity)


def mirror_shift(groups):
    return groups - 1


def route(list_rows, query_count, groups, capacity):
    flat_rows = list_rows.reshape(-1)
    owners = flat_rows // query_count
    places = slot_places(owners, groups, capacity)
    rank = places - owners * capacity
    source = jnp.where(rank == 0, owners, (owners + mirror_shift(groups)) % groups)
    held_id = jnp.where(rank == 0, flat_rows % query_count, query_count + flat_rows % query_count)
    hits = (source[None, :] == jnp.arange(groups, dtype=jnp.int32)[:, None]).astype(jnp.int32)
    fits = jnp.logical_and(jnp.all(jnp.sum(hits, axis=1) <= 1), jnp.all(rank <= 1))
    fast_table = jnp.sum(hits * held_id[None, :], axis=1)
    table = jnp.concatenate(
        [
            request_table(list_rows, query_count, groups, capacity),
            fast_table[:, None],
            jnp.broadcast_to(fits.astype(jnp.int32), (groups, 1)),
        ],
        axis=1,
    )
    return table, places, source


def window_valid(my_group, query_count, groups):
    block_ids = jnp.arange(query_count, dtype=jnp.int32)
    left_ok = jnp.logical_not(jnp.logical_and(my_group == 0, block_ids == 0))
    right_ok = jnp.logical_not(
        jnp.logical_and(my_group == groups - 1, block_ids == query_count - 1)
    )
    all_true = jnp.ones((query_count, BLK), dtype=bool)
    return jnp.concatenate(
        [
            all_true,
            all_true,
            left_ok[:, None] & all_true,
            all_true,
            right_ok[:, None] & all_true,
            jnp.ones((query_count, RAND * BLK), dtype=bool),
        ],
        axis=1,
    )


def against_keys(rows, global_part, window_part, remote_part):
    return jnp.concatenate(
        [
            jnp.einsum("hqid,hjd->hqij", rows, global_part, preferred_element_type=jnp.float32),
            jnp.einsum("hqid,hqjd->hqij", rows, window_part, preferred_element_type=jnp.float32),
            jnp.einsum("hqid,hqjd->hqij", rows, remote_part, preferred_element_type=jnp.float32),
        ],
        axis=-1,
    )


def split_keys(table):
    return (table[..., : 2 * BLK], table[..., 2 * BLK : 5 * BLK], table[..., 5 * BLK :])


def weigh_keys(table, global_part, window_part, remote_part):
    global_w, window_w, random_w = split_keys(table)
    return (
        jnp.einsum("hqij,hjd->hqid", global_w, global_part, preferred_element_type=jnp.float32)
        + jnp.einsum("hqij,hqjd->hqid", window_w, window_part, preferred_element_type=jnp.float32)
        + jnp.einsum("hqij,hqjd->hqid", random_w, remote_part, preferred_element_type=jnp.float32)
    )


def key_terms(table, rows):
    global_w, window_w, random_w = split_keys(table)
    return (
        jnp.einsum("hqij,hqid->hjd", global_w, rows, preferred_element_type=jnp.float32),
        jnp.einsum("hqij,hqid->hqjd", window_w, rows, preferred_element_type=jnp.float32),
        jnp.einsum("hqij,hqid->hqjd", random_w, rows, preferred_element_type=jnp.float32),
    )


def by_head(table, head_count):
    tokens = table.shape[0]
    return jnp.transpose(table.reshape(tokens, head_count, HD), (1, 0, 2))


def by_token(table):
    head_count, tokens = table.shape[0], table.shape[1]
    return jnp.transpose(table, (1, 0, 2)).reshape(tokens, head_count * HD)


def shards(queries, keys, values, grad_out, random_blocks):
    groups = lax.axis_size("seq")
    my_group = lax.axis_index("seq")
    head_q, head_k, head_v, head_g = lax.all_to_all(
        jnp.stack([queries, keys, values, grad_out]), "head", split_axis=2, concat_axis=1, tiled=True
    )
    group_tokens = head_q.shape[0]
    head_count = head_q.shape[1] // HD
    query_count = group_tokens // BLK
    capacity = max(2, 3 * query_count * RAND // (2 * groups))
    score_scale = HD ** (-0.5)
    ordered_table, places, source = route(random_blocks, query_count, groups, capacity)
    ordered_table, head_k = lax.optimization_barrier((ordered_table, head_k))
    shift = mirror_shift(groups)
    key_value = jnp.stack([by_head(head_k, head_count), by_head(head_v, head_count)])
    kv_blocks = key_value.reshape(2, head_count, query_count, BLK, HD)
    mirror = lax.ppermute(kv_blocks, "seq", [(i, (i + shift) % groups) for i in range(groups)])
    left = lax.ppermute(
        key_value[:, :, group_tokens - BLK :], "seq", [(i, i + 1) for i in range(groups - 1)]
    )
    edged = jnp.concatenate([left, key_value, mirror[:, :, 0]], axis=2)
    edged = edged.reshape(2, head_count, query_count + 2, BLK, HD)
    window_kv = jnp.concatenate(
        [edged[:, :, 0:query_count], edged[:, :, 1 : query_count + 1], edged[:, :, 2 : query_count + 2]],
        axis=3,
    )
    global_kv = broadcast(kv_blocks[:, :, 0:2].reshape(2, head_count, 2 * BLK, HD), "seq")
    received = lax.all_to_all(ordered_table, "seq", split_axis=0, concat_axis=0, tiled=True)
    wanted = received[:, :capacity]
    wanted_fast = received[:, capacity]
    take_fast = jnp.all(received[:, capacity + 1] == 1)
    held = jnp.transpose(jnp.concatenate([kv_blocks, mirror], axis=2), (2, 0, 1, 3, 4))
    held = lax.optimization_barrier(held)

    def fetch_fast(held):
        served = jnp.take(held, wanted_fast, axis=0)
        fetched = lax.all_to_all(served, "seq", split_axis=0, concat_axis=0, tiled=True)
        return jnp.take(fetched, source, axis=0)

    def fetch_all(held):
        served = jnp.take(held[:query_count], wanted.reshape(-1), axis=0)
        served = served.reshape(groups, capacity, 2, head_count, BLK, HD)
        fetched = lax.all_to_all(served, "seq", split_axis=0, concat_axis=0, tiled=True)
        return jnp.take(fetched.reshape(groups * capacity, 2, head_count, BLK, HD), places, axis=0)

    chosen = lax.cond(take_fast, fetch_fast, fetch_all, held)
    remote_kv = jnp.transpose(
        chosen.reshape(query_count, RAND, 2, head_count, BLK, HD), (2, 3, 0, 1, 4, 5)
    ).reshape(2, head_count, query_count, RAND * BLK, HD)
    query_blocks = by_head(head_q, head_count).reshape(head_count, query_count, BLK, HD)
    grad_blocks = by_head(head_g, head_count).reshape(head_count, query_count, BLK, HD)
    scores = score_scale * against_keys(query_blocks, global_kv[0], window_kv[0], remote_kv[0])
    valid = window_valid(my_group, query_count, groups)
    scores = jnp.where(valid[None, :, None, :], scores, -jnp.inf)
    row_max = jnp.max(scores, axis=-1, keepdims=True)
    exponent = jnp.exp(scores - row_max)
    attention_probs = exponent / jnp.sum(exponent, axis=-1, keepdims=True)
    weights = attention_probs.astype(jnp.bfloat16)
    attended = weigh_keys(weights, global_kv[1], window_kv[1], remote_kv[1]).astype(jnp.bfloat16)
    grad_prob = against_keys(grad_blocks, global_kv[1], window_kv[1], remote_kv[1])
    row_delta = jnp.sum(attention_probs * grad_prob, axis=-1, keepdims=True)
    grad_score = (score_scale * attention_probs * (grad_prob - row_delta)).astype(jnp.bfloat16)
    grad_q = weigh_keys(grad_score, global_kv[0], window_kv[0], remote_kv[0]).astype(jnp.bfloat16)
    key_global, key_window, key_random = key_terms(grad_score, query_blocks)
    value_global, value_window, value_random = key_terms(weights, grad_blocks)
    global_sum = reduce_to_first(jnp.stack([key_global, value_global]).astype(jnp.bfloat16), "seq")
    window_grad = jnp.stack([key_window, value_window]).reshape(
        2, head_count, query_count, 3, BLK, HD
    )
    no_pad = (0, 0)
    extended = (
        jnp.pad(window_grad[:, :, :, 0], (no_pad, no_pad, (0, 2), no_pad, no_pad))
        + jnp.pad(window_grad[:, :, :, 1], (no_pad, no_pad, (1, 1), no_pad, no_pad))
        + jnp.pad(window_grad[:, :, :, 2], (no_pad, no_pad, (2, 0), no_pad, no_pad))
    )
    outward = jnp.concatenate([extended[:, :, 0], extended[:, :, query_count + 1]], axis=2)
    inward = with_halo(outward.astype(jnp.bfloat16), (("seq", 2),), BLK).astype(outward.dtype)
    own_grad = extended[:, :, 1 : query_count + 1]
    own_grad = own_grad.at[:, :, 0].add(inward[:, :, :BLK])
    own_grad = own_grad.at[:, :, query_count - 1].add(inward[:, :, 3 * BLK :])
    random_terms = jnp.transpose(
        jnp.stack([key_random, value_random]).reshape(2, head_count, query_count * RAND, BLK, HD),
        (2, 0, 1, 3, 4),
    ).astype(jnp.bfloat16)

    def return_fast(random_terms):
        send_pick = (source[None, :] == jnp.arange(groups, dtype=jnp.int32)[:, None]).astype(
            jnp.bfloat16
        )
        outgoing = jnp.einsum(
            "pj,jxhid->pxhid", send_pick, random_terms, preferred_element_type=jnp.float32
        ).astype(jnp.bfloat16)
        incoming = lax.all_to_all(outgoing, "seq", split_axis=0, concat_axis=0, tiled=True)
        take_pick = (
            wanted_fast[None, :] == jnp.arange(2 * query_count, dtype=jnp.int32)[:, None]
        ).astype(jnp.bfloat16)
        sums = jnp.einsum("qp,pxhid->xhqid", take_pick, incoming, preferred_element_type=jnp.float32)
        back = lax.ppermute(
            sums[:, :, query_count:].astype(jnp.bfloat16),
            "seq",
            [((i + shift) % groups, i) for i in range(groups)],
        )
        return sums[:, :, :query_count] + back

    def return_all(random_terms):
        send_pick = (
            places[None, :] == jnp.arange(groups * capacity, dtype=jnp.int32)[:, None]
        ).astype(jnp.bfloat16)
        outgoing = jnp.einsum(
            "pj,jxhid->pxhid", send_pick, random_terms, preferred_element_type=jnp.float32
        ).astype(jnp.bfloat16)
        incoming = lax.all_to_all(
            outgoing.reshape(groups, capacity, 2, head_count, BLK, HD),
            "seq",
            split_axis=0,
            concat_axis=0,
            tiled=True,
        )
        take_pick = (
            wanted.reshape(-1)[None, :] == jnp.arange(query_count, dtype=jnp.int32)[:, None]
        ).astype(jnp.bfloat16)
        return jnp.einsum(
            "qp,pxhid->xhqid",
            take_pick,
            incoming.reshape(groups * capacity, 2, head_count, BLK, HD),
            preferred_element_type=jnp.float32,
        )

    random_sum = lax.cond(take_fast, return_fast, return_all, random_terms)
    global_sum = global_sum.reshape(2, head_count, 2, BLK, HD)
    own_grad = own_grad.at[:, :, 0:2].add(jnp.where(my_group == 0, global_sum, 0.0))
    total_grad = (own_grad + random_sum).astype(jnp.bfloat16)
    flat = (head_count, group_tokens, HD)
    results = lax.all_to_all(
        jnp.stack([by_token(attended.reshape(flat)), by_token(grad_q.reshape(flat)),
                   by_token(total_grad[0].reshape(flat)), by_token(total_grad[1].reshape(flat))]),
        "head",
        split_axis=1,
        concat_axis=2,
        tiled=True,
    )
    return results[0], results[1], results[2], results[3]


def solution(mesh):
    placed = (
        P(("seq", "head"), None),
        P(("seq", "head"), None),
        P(("seq", "head"), None),
        P(("seq", "head"), None),
        P("seq", None),
    )
    return jax.shard_map(
        shards,
        mesh=mesh,
        in_specs=placed,
        out_specs=(
            P(("seq", "head"), None),
            P(("seq", "head"), None),
            P(("seq", "head"), None),
            P(("seq", "head"), None),
        ),
        check_vma=False,
    )
```

```python
import jax
import jax.numpy as jnp
from jax import lax
from jax.sharding import PartitionSpec as P

HD = 128
BLK = 128
RAND = 3


def with_halo(cells, sides, width):
    for axis, dim in sides:
        count = lax.axis_size(axis)
        ends = count - 1
        head = lax.slice_in_dim(cells, 0, width, axis=dim)
        tail = lax.slice_in_dim(cells, cells.shape[dim] - width, cells.shape[dim], axis=dim)
        cells = jnp.concatenate(
            [
                lax.ppermute(tail, axis, [(i, (i + 1) % count) for i in range(ends)]),
                cells,
                lax.ppermute(head, axis, [((i + 1) % count, i) for i in range(ends)]),
            ],
            axis=dim,
        )
    return cells


def row_width(count):
    return 4 if count % 4 == 0 else 1


def broadcast(value, axis):
    count = lax.axis_size(axis)
    me = lax.axis_index(axis)
    width = row_width(count)
    rows = count // width
    my_row = me // width
    step = 1
    while step < rows:
        pairs = [(row * width, (row + step) * width) for row in range(step) if row + step < rows]
        got = lax.ppermute(value, axis, pairs)
        arrived = (me % width == 0) & (my_row >= step) & (my_row < 2 * step)
        value = jnp.where(arrived, got, value)
        step *= 2
    got = jnp.zeros_like(value)
    for col in range(1, width):
        pairs = [(row * width, row * width + col) for row in range(rows)]
        got = got + lax.ppermute(value, axis, pairs)
    return jnp.where(me % width == 0, value, got)


def reduce_along_rows(value, axis):
    count = lax.axis_size(axis)
    width = row_width(count)
    total = value.astype(jnp.float32)
    for col in range(1, width):
        pairs = [(row * width + col, row * width) for row in range(count // width)]
        total = total + lax.ppermute(value, axis, pairs)
    return total


def reduce_row_heads(total, axis):
    count = lax.axis_size(axis)
    width = row_width(count)
    value = total.astype(jnp.bfloat16)
    for row in range(1, count // width):
        total = total + lax.ppermute(value, axis, [(row * width, 0)])
    return total


def slot_places(owners, groups, capacity):
    owner_hits = (owners[:, None] == jnp.arange(groups, dtype=jnp.int32)[None, :]).astype(jnp.int32)
    earlier = jnp.cumsum(owner_hits, axis=0) - owner_hits
    return owners * capacity + jnp.sum(earlier * owner_hits, axis=1)


def request_table(list_rows, query_count, groups, capacity):
    flat_rows = list_rows.reshape(-1)
    places = slot_places(flat_rows // query_count, groups, capacity)
    matches = places[None, :] == jnp.arange(groups * capacity, dtype=jnp.int32)[:, None]
    table = jnp.sum(jnp.where(matches, (flat_rows % query_count)[None, :], 0), axis=1)
    return table.reshape(groups, capacity)


def mirror_shift(groups):
    return groups - 1


def route(list_rows, query_count, groups, capacity):
    flat_rows = list_rows.reshape(-1)
    owners = flat_rows // query_count
    places = slot_places(owners, groups, capacity)
    rank = places - owners * capacity
    source = jnp.where(rank == 0, owners, (owners + mirror_shift(groups)) % groups)
    held_id = jnp.where(rank == 0, flat_rows % query_count, query_count + flat_rows % query_count)
    hits = (source[None, :] == jnp.arange(groups, dtype=jnp.int32)[:, None]).astype(jnp.int32)
    fits = jnp.logical_and(jnp.all(jnp.sum(hits, axis=1) <= 1), jnp.all(rank <= 1))
    fast_table = jnp.sum(hits * held_id[None, :], axis=1)
    table = jnp.concatenate(
        [
            request_table(list_rows, query_count, groups, capacity),
            fast_table[:, None],
            jnp.broadcast_to(fits.astype(jnp.int32), (groups, 1)),
        ],
        axis=1,
    )
    return table, places, source


def window_valid(my_group, query_count, groups):
    block_ids = jnp.arange(query_count, dtype=jnp.int32)
    left_ok = jnp.logical_not(jnp.logical_and(my_group == 0, block_ids == 0))
    right_ok = jnp.logical_not(
        jnp.logical_and(my_group == groups - 1, block_ids == query_count - 1)
    )
    all_true = jnp.ones((query_count, BLK), dtype=bool)
    return jnp.concatenate(
        [
            all_true,
            all_true,
            left_ok[:, None] & all_true,
            all_true,
            right_ok[:, None] & all_true,
            jnp.ones((query_count, RAND * BLK), dtype=bool),
        ],
        axis=1,
    )


def against_keys(rows, global_part, window_part, remote_part):
    return jnp.concatenate(
        [
            jnp.einsum("hqid,hjd->hqij", rows, global_part, preferred_element_type=jnp.float32),
            jnp.einsum("hqid,hqjd->hqij", rows, window_part, preferred_element_type=jnp.float32),
            jnp.einsum("hqid,hqjd->hqij", rows, remote_part, preferred_element_type=jnp.float32),
        ],
        axis=-1,
    )


def split_keys(table):
    return (table[..., : 2 * BLK], table[..., 2 * BLK : 5 * BLK], table[..., 5 * BLK :])


def weigh_keys(table, global_part, window_part, remote_part):
    global_w, window_w, random_w = split_keys(table)
    return (
        jnp.einsum("hqij,hjd->hqid", global_w, global_part, preferred_element_type=jnp.float32)
        + jnp.einsum("hqij,hqjd->hqid", window_w, window_part, preferred_element_type=jnp.float32)
        + jnp.einsum("hqij,hqjd->hqid", random_w, remote_part, preferred_element_type=jnp.float32)
    )


def key_terms(table, rows):
    global_w, window_w, random_w = split_keys(table)
    return (
        jnp.einsum("hqij,hqid->hjd", global_w, rows, preferred_element_type=jnp.float32),
        jnp.einsum("hqij,hqid->hqjd", window_w, rows, preferred_element_type=jnp.float32),
        jnp.einsum("hqij,hqid->hqjd", random_w, rows, preferred_element_type=jnp.float32),
    )


def by_head(table, head_count):
    tokens = table.shape[0]
    return jnp.transpose(table.reshape(tokens, head_count, HD), (1, 0, 2))


def by_token(table):
    head_count, tokens = table.shape[0], table.shape[1]
    return jnp.transpose(table, (1, 0, 2)).reshape(tokens, head_count * HD)


def shards(queries, keys, values, grad_out, random_blocks):
    groups = lax.axis_size("seq")
    my_group = lax.axis_index("seq")
    head_q, head_k, head_v, head_g = lax.all_to_all(
        jnp.stack([queries, keys, values, grad_out]), "head", split_axis=2, concat_axis=1, tiled=True
    )
    group_tokens = head_q.shape[0]
    head_count = head_q.shape[1] // HD
    query_count = group_tokens // BLK
    capacity = max(2, 3 * query_count * RAND // (2 * groups))
    score_scale = HD ** (-0.5)
    ordered_table, places, source = route(random_blocks, query_count, groups, capacity)
    ordered_table, head_k = lax.optimization_barrier((ordered_table, head_k))
    shift = mirror_shift(groups)
    key_value = jnp.stack([by_head(head_k, head_count), by_head(head_v, head_count)])
    kv_blocks = key_value.reshape(2, head_count, query_count, BLK, HD)
    mirror = lax.ppermute(kv_blocks, "seq", [(i, (i + shift) % groups) for i in range(groups)])
    left = lax.ppermute(
        key_value[:, :, group_tokens - BLK :], "seq", [(i, i + 1) for i in range(groups - 1)]
    )
    edged = jnp.concatenate([left, key_value, mirror[:, :, 0]], axis=2)
    edged = edged.reshape(2, head_count, query_count + 2, BLK, HD)
    window_kv = jnp.concatenate(
        [edged[:, :, 0:query_count], edged[:, :, 1 : query_count + 1], edged[:, :, 2 : query_count + 2]],
        axis=3,
    )
    global_kv = broadcast(kv_blocks[:, :, 0:2].reshape(2, head_count, 2 * BLK, HD), "seq")
    received = lax.all_to_all(ordered_table, "seq", split_axis=0, concat_axis=0, tiled=True)
    wanted = received[:, :capacity]
    wanted_fast = received[:, capacity]
    take_fast = jnp.all(received[:, capacity + 1] == 1)
    held = jnp.transpose(jnp.concatenate([kv_blocks, mirror], axis=2), (2, 0, 1, 3, 4))
    held = lax.optimization_barrier(held)

    def fetch_fast(held):
        served = jnp.take(held, wanted_fast, axis=0)
        fetched = lax.all_to_all(served, "seq", split_axis=0, concat_axis=0, tiled=True)
        return jnp.take(fetched, source, axis=0)

    def fetch_all(held):
        served = jnp.take(held[:query_count], wanted.reshape(-1), axis=0)
        served = served.reshape(groups, capacity, 2, head_count, BLK, HD)
        fetched = lax.all_to_all(served, "seq", split_axis=0, concat_axis=0, tiled=True)
        return jnp.take(fetched.reshape(groups * capacity, 2, head_count, BLK, HD), places, axis=0)

    chosen = lax.cond(take_fast, fetch_fast, fetch_all, held)
    remote_kv = jnp.transpose(
        chosen.reshape(query_count, RAND, 2, head_count, BLK, HD), (2, 3, 0, 1, 4, 5)
    ).reshape(2, head_count, query_count, RAND * BLK, HD)
    query_blocks = by_head(head_q, head_count).reshape(head_count, query_count, BLK, HD)
    grad_blocks = by_head(head_g, head_count).reshape(head_count, query_count, BLK, HD)
    scores = score_scale * against_keys(query_blocks, global_kv[0], window_kv[0], remote_kv[0])
    valid = window_valid(my_group, query_count, groups)
    scores = jnp.where(valid[None, :, None, :], scores, -jnp.inf)
    row_max = jnp.max(scores, axis=-1, keepdims=True)
    exponent = jnp.exp(scores - row_max)
    attention_probs = exponent / jnp.sum(exponent, axis=-1, keepdims=True)
    weights = attention_probs.astype(jnp.bfloat16)
    attended = weigh_keys(weights, global_kv[1], window_kv[1], remote_kv[1]).astype(jnp.bfloat16)
    grad_prob = against_keys(grad_blocks, global_kv[1], window_kv[1], remote_kv[1])
    row_delta = jnp.sum(attention_probs * grad_prob, axis=-1, keepdims=True)
    grad_score = (score_scale * attention_probs * (grad_prob - row_delta)).astype(jnp.bfloat16)
    grad_q = weigh_keys(grad_score, global_kv[0], window_kv[0], remote_kv[0]).astype(jnp.bfloat16)
    key_global, key_window, key_random = key_terms(grad_score, query_blocks)
    value_global, value_window, value_random = key_terms(weights, grad_blocks)
    row_sum = reduce_along_rows(jnp.stack([key_global, value_global]).astype(jnp.bfloat16), "seq")
    window_grad = jnp.stack([key_window, value_window]).reshape(
        2, head_count, query_count, 3, BLK, HD
    )
    no_pad = (0, 0)
    extended = (
        jnp.pad(window_grad[:, :, :, 0], (no_pad, no_pad, (0, 2), no_pad, no_pad))
        + jnp.pad(window_grad[:, :, :, 1], (no_pad, no_pad, (1, 1), no_pad, no_pad))
        + jnp.pad(window_grad[:, :, :, 2], (no_pad, no_pad, (2, 0), no_pad, no_pad))
    )
    outward = jnp.concatenate([extended[:, :, 0], extended[:, :, query_count + 1]], axis=2)
    inward = with_halo(outward.astype(jnp.bfloat16), (("seq", 2),), BLK).astype(outward.dtype)
    own_grad = extended[:, :, 1 : query_count + 1]
    own_grad = own_grad.at[:, :, 0].add(inward[:, :, :BLK])
    own_grad = own_grad.at[:, :, query_count - 1].add(inward[:, :, 3 * BLK :])
    random_terms = jnp.transpose(
        jnp.stack([key_random, value_random]).reshape(2, head_count, query_count * RAND, BLK, HD),
        (2, 0, 1, 3, 4),
    ).astype(jnp.bfloat16)

    def return_fast(random_terms, row_sum):
        global_sum = reduce_row_heads(row_sum, "seq")
        send_pick = (source[None, :] == jnp.arange(groups, dtype=jnp.int32)[:, None]).astype(
            jnp.bfloat16
        )
        outgoing = jnp.einsum(
            "pj,jxhid->pxhid", send_pick, random_terms, preferred_element_type=jnp.float32
        ).astype(jnp.bfloat16)
        incoming = lax.all_to_all(outgoing, "seq", split_axis=0, concat_axis=0, tiled=True)
        take_pick = (
            wanted_fast[None, :] == jnp.arange(2 * query_count, dtype=jnp.int32)[:, None]
        ).astype(jnp.bfloat16)
        sums = jnp.einsum("qp,pxhid->xhqid", take_pick, incoming, preferred_element_type=jnp.float32)
        back = lax.ppermute(
            sums[:, :, query_count:].astype(jnp.bfloat16),
            "seq",
            [((i + shift) % groups, i) for i in range(groups)],
        )
        return sums[:, :, :query_count] + back, global_sum

    def return_all(random_terms, row_sum):
        global_sum = reduce_row_heads(row_sum, "seq")
        send_pick = (
            places[None, :] == jnp.arange(groups * capacity, dtype=jnp.int32)[:, None]
        ).astype(jnp.bfloat16)
        outgoing = jnp.einsum(
            "pj,jxhid->pxhid", send_pick, random_terms, preferred_element_type=jnp.float32
        ).astype(jnp.bfloat16)
        incoming = lax.all_to_all(
            outgoing.reshape(groups, capacity, 2, head_count, BLK, HD),
            "seq",
            split_axis=0,
            concat_axis=0,
            tiled=True,
        )
        take_pick = (
            wanted.reshape(-1)[None, :] == jnp.arange(query_count, dtype=jnp.int32)[:, None]
        ).astype(jnp.bfloat16)
        return jnp.einsum(
            "qp,pxhid->xhqid",
            take_pick,
            incoming.reshape(groups * capacity, 2, head_count, BLK, HD),
            preferred_element_type=jnp.float32,
        ), global_sum

    random_sum, global_sum = lax.cond(take_fast, return_fast, return_all, random_terms, row_sum)
    global_sum = global_sum.reshape(2, head_count, 2, BLK, HD)
    own_grad = own_grad.at[:, :, 0:2].add(jnp.where(my_group == 0, global_sum, 0.0))
    total_grad = (own_grad + random_sum).astype(jnp.bfloat16)
    flat = (head_count, group_tokens, HD)
    results = lax.all_to_all(
        jnp.stack([by_token(attended.reshape(flat)), by_token(grad_q.reshape(flat)),
                   by_token(total_grad[0].reshape(flat)), by_token(total_grad[1].reshape(flat))]),
        "head",
        split_axis=1,
        concat_axis=2,
        tiled=True,
    )
    return results[0], results[1], results[2], results[3]


def solution(mesh):
    placed = (
        P(("seq", "head"), None),
        P(("seq", "head"), None),
        P(("seq", "head"), None),
        P(("seq", "head"), None),
        P("seq", None),
    )
    return jax.shard_map(
        shards,
        mesh=mesh,
        in_specs=placed,
        out_specs=(
            P(("seq", "head"), None),
            P(("seq", "head"), None),
            P(("seq", "head"), None),
            P(("seq", "head"), None),
        ),
        check_vma=False,
    )
```

```python
import jax
import jax.numpy as jnp
from jax import lax
from jax.sharding import PartitionSpec as P

HD = 128
BLK = 128
RAND = 3


def with_halo(cells, sides, width):
    for axis, dim in sides:
        count = lax.axis_size(axis)
        ends = count - 1
        head = lax.slice_in_dim(cells, 0, width, axis=dim)
        tail = lax.slice_in_dim(cells, cells.shape[dim] - width, cells.shape[dim], axis=dim)
        cells = jnp.concatenate(
            [
                lax.ppermute(tail, axis, [(i, (i + 1) % count) for i in range(ends)]),
                cells,
                lax.ppermute(head, axis, [((i + 1) % count, i) for i in range(ends)]),
            ],
            axis=dim,
        )
    return cells


def row_width(count):
    return 4 if count % 4 == 0 else 1


def broadcast(value, axis):
    count = lax.axis_size(axis)
    me = lax.axis_index(axis)
    width = row_width(count)
    rows = count // width
    my_row = me // width
    step = 1
    while step < rows:
        pairs = [(row * width, (row + step) * width) for row in range(step) if row + step < rows]
        got = lax.ppermute(value, axis, pairs)
        arrived = (me % width == 0) & (my_row >= step) & (my_row < 2 * step)
        value = jnp.where(arrived, got, value)
        step *= 2
    got = jnp.zeros_like(value)
    for col in range(1, width):
        pairs = [(row * width, row * width + col) for row in range(rows)]
        got = got + lax.ppermute(value, axis, pairs)
    return jnp.where(me % width == 0, value, got)


def reduce_along_rows(value, axis):
    count = lax.axis_size(axis)
    width = row_width(count)
    total = value.astype(jnp.float32)
    for col in range(1, width):
        pairs = [(row * width + col, row * width) for row in range(count // width)]
        total = total + lax.ppermute(value, axis, pairs)
    return total


def reduce_row_heads(total, axis):
    count = lax.axis_size(axis)
    width = row_width(count)
    value = total.astype(jnp.bfloat16)
    for row in range(1, count // width):
        total = total + lax.ppermute(value, axis, [(row * width, 0)])
    return total


def slot_places(owners, groups, capacity):
    owner_hits = (owners[:, None] == jnp.arange(groups, dtype=jnp.int32)[None, :]).astype(jnp.int32)
    earlier = jnp.cumsum(owner_hits, axis=0) - owner_hits
    return owners * capacity + jnp.sum(earlier * owner_hits, axis=1)


def request_table(list_rows, query_count, groups, capacity):
    flat_rows = list_rows.reshape(-1)
    places = slot_places(flat_rows // query_count, groups, capacity)
    matches = places[None, :] == jnp.arange(groups * capacity, dtype=jnp.int32)[:, None]
    table = jnp.sum(jnp.where(matches, (flat_rows % query_count)[None, :], 0), axis=1)
    return table.reshape(groups, capacity)


def mirror_shift(groups):
    return groups - 1


def route(list_rows, query_count, groups, capacity):
    flat_rows = list_rows.reshape(-1)
    owners = flat_rows // query_count
    places = slot_places(owners, groups, capacity)
    rank = places - owners * capacity
    source = jnp.where(rank == 0, owners, (owners + mirror_shift(groups)) % groups)
    held_id = jnp.where(rank == 0, flat_rows % query_count, query_count + flat_rows % query_count)
    hits = (source[None, :] == jnp.arange(groups, dtype=jnp.int32)[:, None]).astype(jnp.int32)
    fits = jnp.logical_and(jnp.all(jnp.sum(hits, axis=1) <= 1), jnp.all(rank <= 1))
    fast_table = jnp.sum(hits * held_id[None, :], axis=1)
    table = jnp.concatenate(
        [
            request_table(list_rows, query_count, groups, capacity),
            fast_table[:, None],
            jnp.broadcast_to(fits.astype(jnp.int32), (groups, 1)),
        ],
        axis=1,
    )
    return table, places, source


def window_valid(my_group, query_count, groups):
    block_ids = jnp.arange(query_count, dtype=jnp.int32)
    left_ok = jnp.logical_not(jnp.logical_and(my_group == 0, block_ids == 0))
    right_ok = jnp.logical_not(
        jnp.logical_and(my_group == groups - 1, block_ids == query_count - 1)
    )
    all_true = jnp.ones((query_count, BLK), dtype=bool)
    return jnp.concatenate(
        [
            all_true,
            all_true,
            left_ok[:, None] & all_true,
            all_true,
            right_ok[:, None] & all_true,
            jnp.ones((query_count, RAND * BLK), dtype=bool),
        ],
        axis=1,
    )


def against_keys(rows, global_part, window_part, remote_part):
    return jnp.concatenate(
        [
            jnp.einsum("hqid,hjd->hqij", rows, global_part, preferred_element_type=jnp.float32),
            jnp.einsum("hqid,hqjd->hqij", rows, window_part, preferred_element_type=jnp.float32),
            jnp.einsum("hqid,hqjd->hqij", rows, remote_part, preferred_element_type=jnp.float32),
        ],
        axis=-1,
    )


def split_keys(table):
    return (table[..., : 2 * BLK], table[..., 2 * BLK : 5 * BLK], table[..., 5 * BLK :])


def weigh_keys(table, global_part, window_part, remote_part):
    global_w, window_w, random_w = split_keys(table)
    return (
        jnp.einsum("hqij,hjd->hqid", global_w, global_part, preferred_element_type=jnp.float32)
        + jnp.einsum("hqij,hqjd->hqid", window_w, window_part, preferred_element_type=jnp.float32)
        + jnp.einsum("hqij,hqjd->hqid", random_w, remote_part, preferred_element_type=jnp.float32)
    )


def key_terms(table, rows):
    global_w, window_w, random_w = split_keys(table)
    return (
        jnp.einsum("hqij,hqid->hjd", global_w, rows, preferred_element_type=jnp.float32),
        jnp.einsum("hqij,hqid->hqjd", window_w, rows, preferred_element_type=jnp.float32),
        jnp.einsum("hqij,hqid->hqjd", random_w, rows, preferred_element_type=jnp.float32),
    )


def by_head(table, head_count):
    tokens = table.shape[0]
    return jnp.transpose(table.reshape(tokens, head_count, HD), (1, 0, 2))


def by_token(table):
    head_count, tokens = table.shape[0], table.shape[1]
    return jnp.transpose(table, (1, 0, 2)).reshape(tokens, head_count * HD)


def shards(queries, keys, values, grad_out, random_blocks):
    groups = lax.axis_size("seq")
    my_group = lax.axis_index("seq")
    head_q, head_k, head_v, head_g = lax.all_to_all(
        jnp.stack([queries, keys, values, grad_out]), "head", split_axis=2, concat_axis=1, tiled=True
    )
    group_tokens = head_q.shape[0]
    head_count = head_q.shape[1] // HD
    query_count = group_tokens // BLK
    capacity = max(2, 3 * query_count * RAND // (2 * groups))
    score_scale = HD ** (-0.5)
    ordered_table, places, source = route(random_blocks, query_count, groups, capacity)
    ordered_table, head_k = lax.optimization_barrier((ordered_table, head_k))
    shift = mirror_shift(groups)
    key_value = jnp.stack([by_head(head_k, head_count), by_head(head_v, head_count)])
    kv_blocks = key_value.reshape(2, head_count, query_count, BLK, HD)
    mirror = lax.ppermute(kv_blocks, "seq", [(i, (i + shift) % groups) for i in range(groups)])
    left = lax.ppermute(
        key_value[:, :, group_tokens - BLK :], "seq", [(i, i + 1) for i in range(groups - 1)]
    )
    edged = jnp.concatenate([left, key_value, mirror[:, :, 0]], axis=2)
    edged = edged.reshape(2, head_count, query_count + 2, BLK, HD)
    window_kv = jnp.concatenate(
        [edged[:, :, 0:query_count], edged[:, :, 1 : query_count + 1], edged[:, :, 2 : query_count + 2]],
        axis=3,
    )
    global_src = kv_blocks[:, :, 0:2].reshape(2, head_count, 2 * BLK, HD)
    received = lax.all_to_all(ordered_table, "seq", split_axis=0, concat_axis=0, tiled=True)
    wanted = received[:, :capacity]
    wanted_fast = received[:, capacity]
    take_fast = jnp.all(received[:, capacity + 1] == 1)
    held = jnp.transpose(jnp.concatenate([kv_blocks, mirror], axis=2), (2, 0, 1, 3, 4))
    held = lax.optimization_barrier(held)

    def fetch_fast(held, global_src):
        global_kv = broadcast(global_src, "seq")
        served = jnp.take(held, wanted_fast, axis=0)
        fetched = lax.all_to_all(served, "seq", split_axis=0, concat_axis=0, tiled=True)
        return jnp.take(fetched, source, axis=0), global_kv

    def fetch_all(held, global_src):
        global_kv = broadcast(global_src, "seq")
        served = jnp.take(held[:query_count], wanted.reshape(-1), axis=0)
        served = served.reshape(groups, capacity, 2, head_count, BLK, HD)
        fetched = lax.all_to_all(served, "seq", split_axis=0, concat_axis=0, tiled=True)
        chosen = jnp.take(fetched.reshape(groups * capacity, 2, head_count, BLK, HD), places, axis=0)
        return chosen, global_kv

    chosen, global_kv = lax.cond(take_fast, fetch_fast, fetch_all, held, global_src)
    remote_kv = jnp.transpose(
        chosen.reshape(query_count, RAND, 2, head_count, BLK, HD), (2, 3, 0, 1, 4, 5)
    ).reshape(2, head_count, query_count, RAND * BLK, HD)
    query_blocks = by_head(head_q, head_count).reshape(head_count, query_count, BLK, HD)
    grad_blocks = by_head(head_g, head_count).reshape(head_count, query_count, BLK, HD)
    scores = score_scale * against_keys(query_blocks, global_kv[0], window_kv[0], remote_kv[0])
    valid = window_valid(my_group, query_count, groups)
    scores = jnp.where(valid[None, :, None, :], scores, -jnp.inf)
    row_max = jnp.max(scores, axis=-1, keepdims=True)
    exponent = jnp.exp(scores - row_max)
    attention_probs = exponent / jnp.sum(exponent, axis=-1, keepdims=True)
    weights = attention_probs.astype(jnp.bfloat16)
    attended = weigh_keys(weights, global_kv[1], window_kv[1], remote_kv[1]).astype(jnp.bfloat16)
    grad_prob = against_keys(grad_blocks, global_kv[1], window_kv[1], remote_kv[1])
    row_delta = jnp.sum(attention_probs * grad_prob, axis=-1, keepdims=True)
    grad_score = (score_scale * attention_probs * (grad_prob - row_delta)).astype(jnp.bfloat16)
    grad_q = weigh_keys(grad_score, global_kv[0], window_kv[0], remote_kv[0]).astype(jnp.bfloat16)
    key_global, key_window, key_random = key_terms(grad_score, query_blocks)
    value_global, value_window, value_random = key_terms(weights, grad_blocks)
    row_sum = reduce_along_rows(jnp.stack([key_global, value_global]).astype(jnp.bfloat16), "seq")
    window_grad = jnp.stack([key_window, value_window]).reshape(
        2, head_count, query_count, 3, BLK, HD
    )
    no_pad = (0, 0)
    extended = (
        jnp.pad(window_grad[:, :, :, 0], (no_pad, no_pad, (0, 2), no_pad, no_pad))
        + jnp.pad(window_grad[:, :, :, 1], (no_pad, no_pad, (1, 1), no_pad, no_pad))
        + jnp.pad(window_grad[:, :, :, 2], (no_pad, no_pad, (2, 0), no_pad, no_pad))
    )
    outward = jnp.concatenate([extended[:, :, 0], extended[:, :, query_count + 1]], axis=2)
    inward = with_halo(outward.astype(jnp.bfloat16), (("seq", 2),), BLK).astype(outward.dtype)
    own_grad = extended[:, :, 1 : query_count + 1]
    own_grad = own_grad.at[:, :, 0].add(inward[:, :, :BLK])
    own_grad = own_grad.at[:, :, query_count - 1].add(inward[:, :, 3 * BLK :])
    random_terms = jnp.transpose(
        jnp.stack([key_random, value_random]).reshape(2, head_count, query_count * RAND, BLK, HD),
        (2, 0, 1, 3, 4),
    ).astype(jnp.bfloat16)

    def return_fast(random_terms, row_sum):
        global_sum = reduce_row_heads(row_sum, "seq")
        send_pick = (source[None, :] == jnp.arange(groups, dtype=jnp.int32)[:, None]).astype(
            jnp.bfloat16
        )
        outgoing = jnp.einsum(
            "pj,jxhid->pxhid", send_pick, random_terms, preferred_element_type=jnp.float32
        ).astype(jnp.bfloat16)
        incoming = lax.all_to_all(outgoing, "seq", split_axis=0, concat_axis=0, tiled=True)
        take_pick = (
            wanted_fast[None, :] == jnp.arange(2 * query_count, dtype=jnp.int32)[:, None]
        ).astype(jnp.bfloat16)
        sums = jnp.einsum("qp,pxhid->xhqid", take_pick, incoming, preferred_element_type=jnp.float32)
        back = lax.ppermute(
            sums[:, :, query_count:].astype(jnp.bfloat16),
            "seq",
            [((i + shift) % groups, i) for i in range(groups)],
        )
        return sums[:, :, :query_count] + back, global_sum

    def return_all(random_terms, row_sum):
        global_sum = reduce_row_heads(row_sum, "seq")
        send_pick = (
            places[None, :] == jnp.arange(groups * capacity, dtype=jnp.int32)[:, None]
        ).astype(jnp.bfloat16)
        outgoing = jnp.einsum(
            "pj,jxhid->pxhid", send_pick, random_terms, preferred_element_type=jnp.float32
        ).astype(jnp.bfloat16)
        incoming = lax.all_to_all(
            outgoing.reshape(groups, capacity, 2, head_count, BLK, HD),
            "seq",
            split_axis=0,
            concat_axis=0,
            tiled=True,
        )
        take_pick = (
            wanted.reshape(-1)[None, :] == jnp.arange(query_count, dtype=jnp.int32)[:, None]
        ).astype(jnp.bfloat16)
        return jnp.einsum(
            "qp,pxhid->xhqid",
            take_pick,
            incoming.reshape(groups * capacity, 2, head_count, BLK, HD),
            preferred_element_type=jnp.float32,
        ), global_sum

    random_sum, global_sum = lax.cond(take_fast, return_fast, return_all, random_terms, row_sum)
    global_sum = global_sum.reshape(2, head_count, 2, BLK, HD)
    own_grad = own_grad.at[:, :, 0:2].add(jnp.where(my_group == 0, global_sum, 0.0))
    total_grad = (own_grad + random_sum).astype(jnp.bfloat16)
    flat = (head_count, group_tokens, HD)
    results = lax.all_to_all(
        jnp.stack([by_token(attended.reshape(flat)), by_token(grad_q.reshape(flat)),
                   by_token(total_grad[0].reshape(flat)), by_token(total_grad[1].reshape(flat))]),
        "head",
        split_axis=1,
        concat_axis=2,
        tiled=True,
    )
    return results[0], results[1], results[2], results[3]


def solution(mesh):
    placed = (
        P(("seq", "head"), None),
        P(("seq", "head"), None),
        P(("seq", "head"), None),
        P(("seq", "head"), None),
        P("seq", None),
    )
    return jax.shard_map(
        shards,
        mesh=mesh,
        in_specs=placed,
        out_specs=(
            P(("seq", "head"), None),
            P(("seq", "head"), None),
            P(("seq", "head"), None),
            P(("seq", "head"), None),
        ),
        check_vma=False,
    )
```

```python
import jax
import jax.numpy as jnp
from jax import lax
from jax.sharding import PartitionSpec as P

HD = 128
BLK = 128
RAND = 3


def with_halo(cells, sides, width):
    for axis, dim in sides:
        count = lax.axis_size(axis)
        ends = count - 1
        head = lax.slice_in_dim(cells, 0, width, axis=dim)
        tail = lax.slice_in_dim(cells, cells.shape[dim] - width, cells.shape[dim], axis=dim)
        cells = jnp.concatenate(
            [
                lax.ppermute(tail, axis, [(i, (i + 1) % count) for i in range(ends)]),
                cells,
                lax.ppermute(head, axis, [((i + 1) % count, i) for i in range(ends)]),
            ],
            axis=dim,
        )
    return cells


def row_width(count):
    return 4 if count % 4 == 0 else 1


def broadcast(value, axis):
    count = lax.axis_size(axis)
    me = lax.axis_index(axis)
    width = row_width(count)
    rows = count // width
    my_row = me // width
    step = 1
    while step < rows:
        pairs = [(row * width, (row + step) * width) for row in range(step) if row + step < rows]
        got = lax.ppermute(value, axis, pairs)
        arrived = (me % width == 0) & (my_row >= step) & (my_row < 2 * step)
        value = jnp.where(arrived, got, value)
        step *= 2
    got = jnp.zeros_like(value)
    for col in range(1, width):
        pairs = [(row * width, row * width + col) for row in range(rows)]
        got = got + lax.ppermute(value, axis, pairs)
    return jnp.where(me % width == 0, value, got)


def reduce_along_rows(value, axis):
    count = lax.axis_size(axis)
    width = row_width(count)
    total = value.astype(jnp.float32)
    for col in range(1, width):
        pairs = [(row * width + col, row * width) for row in range(count // width)]
        total = total + lax.ppermute(value, axis, pairs)
    return total


def reduce_row_heads(total, axis):
    count = lax.axis_size(axis)
    width = row_width(count)
    rows = count // width
    step = 1
    while step < rows:
        pairs = [((row + step) * width, row * width) for row in range(0, rows, 2 * step) if row + step < rows]
        total = total + lax.ppermute(total.astype(jnp.bfloat16), axis, pairs)
        step *= 2
    return total


def slot_places(owners, groups, capacity):
    owner_hits = (owners[:, None] == jnp.arange(groups, dtype=jnp.int32)[None, :]).astype(jnp.int32)
    earlier = jnp.cumsum(owner_hits, axis=0) - owner_hits
    return owners * capacity + jnp.sum(earlier * owner_hits, axis=1)


def request_table(list_rows, query_count, groups, capacity):
    flat_rows = list_rows.reshape(-1)
    places = slot_places(flat_rows // query_count, groups, capacity)
    matches = places[None, :] == jnp.arange(groups * capacity, dtype=jnp.int32)[:, None]
    table = jnp.sum(jnp.where(matches, (flat_rows % query_count)[None, :], 0), axis=1)
    return table.reshape(groups, capacity)


def mirror_shift(groups):
    return groups - 1


def route(list_rows, query_count, groups, capacity):
    flat_rows = list_rows.reshape(-1)
    owners = flat_rows // query_count
    places = slot_places(owners, groups, capacity)
    rank = places - owners * capacity
    source = jnp.where(rank == 0, owners, (owners + mirror_shift(groups)) % groups)
    held_id = jnp.where(rank == 0, flat_rows % query_count, query_count + flat_rows % query_count)
    hits = (source[None, :] == jnp.arange(groups, dtype=jnp.int32)[:, None]).astype(jnp.int32)
    fits = jnp.logical_and(jnp.all(jnp.sum(hits, axis=1) <= 1), jnp.all(rank <= 1))
    fast_table = jnp.sum(hits * held_id[None, :], axis=1)
    table = jnp.concatenate(
        [
            request_table(list_rows, query_count, groups, capacity),
            fast_table[:, None],
            jnp.broadcast_to(fits.astype(jnp.int32), (groups, 1)),
        ],
        axis=1,
    )
    return table, places, source


def window_valid(my_group, query_count, groups):
    block_ids = jnp.arange(query_count, dtype=jnp.int32)
    left_ok = jnp.logical_not(jnp.logical_and(my_group == 0, block_ids == 0))
    right_ok = jnp.logical_not(
        jnp.logical_and(my_group == groups - 1, block_ids == query_count - 1)
    )
    all_true = jnp.ones((query_count, BLK), dtype=bool)
    return jnp.concatenate(
        [
            all_true,
            all_true,
            left_ok[:, None] & all_true,
            all_true,
            right_ok[:, None] & all_true,
            jnp.ones((query_count, RAND * BLK), dtype=bool),
        ],
        axis=1,
    )


def against_keys(rows, global_part, window_part, remote_part):
    return jnp.concatenate(
        [
            jnp.einsum("hqid,hjd->hqij", rows, global_part, preferred_element_type=jnp.float32),
            jnp.einsum("hqid,hqjd->hqij", rows, window_part, preferred_element_type=jnp.float32),
            jnp.einsum("hqid,hqjd->hqij", rows, remote_part, preferred_element_type=jnp.float32),
        ],
        axis=-1,
    )


def split_keys(table):
    return (table[..., : 2 * BLK], table[..., 2 * BLK : 5 * BLK], table[..., 5 * BLK :])


def weigh_keys(table, global_part, window_part, remote_part):
    global_w, window_w, random_w = split_keys(table)
    return (
        jnp.einsum("hqij,hjd->hqid", global_w, global_part, preferred_element_type=jnp.float32)
        + jnp.einsum("hqij,hqjd->hqid", window_w, window_part, preferred_element_type=jnp.float32)
        + jnp.einsum("hqij,hqjd->hqid", random_w, remote_part, preferred_element_type=jnp.float32)
    )


def key_terms(table, rows):
    global_w, window_w, random_w = split_keys(table)
    return (
        jnp.einsum("hqij,hqid->hjd", global_w, rows, preferred_element_type=jnp.float32),
        jnp.einsum("hqij,hqid->hqjd", window_w, rows, preferred_element_type=jnp.float32),
        jnp.einsum("hqij,hqid->hqjd", random_w, rows, preferred_element_type=jnp.float32),
    )


def by_head(table, head_count):
    tokens = table.shape[0]
    return jnp.transpose(table.reshape(tokens, head_count, HD), (1, 0, 2))


def by_token(table):
    head_count, tokens = table.shape[0], table.shape[1]
    return jnp.transpose(table, (1, 0, 2)).reshape(tokens, head_count * HD)


def shards(queries, keys, values, grad_out, random_blocks):
    groups = lax.axis_size("seq")
    my_group = lax.axis_index("seq")
    head_q, head_k, head_v, head_g = lax.all_to_all(
        jnp.stack([queries, keys, values, grad_out]), "head", split_axis=2, concat_axis=1, tiled=True
    )
    group_tokens = head_q.shape[0]
    head_count = head_q.shape[1] // HD
    query_count = group_tokens // BLK
    capacity = max(2, 3 * query_count * RAND // (2 * groups))
    score_scale = HD ** (-0.5)
    ordered_table, places, source = route(random_blocks, query_count, groups, capacity)
    ordered_table, head_k = lax.optimization_barrier((ordered_table, head_k))
    shift = mirror_shift(groups)
    key_value = jnp.stack([by_head(head_k, head_count), by_head(head_v, head_count)])
    kv_blocks = key_value.reshape(2, head_count, query_count, BLK, HD)
    mirror = lax.ppermute(kv_blocks, "seq", [(i, (i + shift) % groups) for i in range(groups)])
    left = lax.ppermute(
        key_value[:, :, group_tokens - BLK :], "seq", [(i, i + 1) for i in range(groups - 1)]
    )
    edged = jnp.concatenate([left, key_value, mirror[:, :, 0]], axis=2)
    edged = edged.reshape(2, head_count, query_count + 2, BLK, HD)
    window_kv = jnp.concatenate(
        [edged[:, :, 0:query_count], edged[:, :, 1 : query_count + 1], edged[:, :, 2 : query_count + 2]],
        axis=3,
    )
    global_kv = broadcast(kv_blocks[:, :, 0:2].reshape(2, head_count, 2 * BLK, HD), "seq")
    received = lax.all_to_all(ordered_table, "seq", split_axis=0, concat_axis=0, tiled=True)
    wanted = received[:, :capacity]
    wanted_fast = received[:, capacity]
    take_fast = jnp.all(received[:, capacity + 1] == 1)
    held = jnp.transpose(jnp.concatenate([kv_blocks, mirror], axis=2), (2, 0, 1, 3, 4))
    held = lax.optimization_barrier(held)

    def fetch_fast(held):
        served = jnp.take(held, wanted_fast, axis=0)
        fetched = lax.all_to_all(served, "seq", split_axis=0, concat_axis=0, tiled=True)
        return jnp.take(fetched, source, axis=0)

    def fetch_all(held):
        served = jnp.take(held[:query_count], wanted.reshape(-1), axis=0)
        served = served.reshape(groups, capacity, 2, head_count, BLK, HD)
        fetched = lax.all_to_all(served, "seq", split_axis=0, concat_axis=0, tiled=True)
        return jnp.take(fetched.reshape(groups * capacity, 2, head_count, BLK, HD), places, axis=0)

    chosen = lax.cond(take_fast, fetch_fast, fetch_all, held)
    remote_kv = jnp.transpose(
        chosen.reshape(query_count, RAND, 2, head_count, BLK, HD), (2, 3, 0, 1, 4, 5)
    ).reshape(2, head_count, query_count, RAND * BLK, HD)
    query_blocks = by_head(head_q, head_count).reshape(head_count, query_count, BLK, HD)
    grad_blocks = by_head(head_g, head_count).reshape(head_count, query_count, BLK, HD)
    scores = score_scale * against_keys(query_blocks, global_kv[0], window_kv[0], remote_kv[0])
    valid = window_valid(my_group, query_count, groups)
    scores = jnp.where(valid[None, :, None, :], scores, -jnp.inf)
    row_max = jnp.max(scores, axis=-1, keepdims=True)
    exponent = jnp.exp(scores - row_max)
    attention_probs = exponent / jnp.sum(exponent, axis=-1, keepdims=True)
    weights = attention_probs.astype(jnp.bfloat16)
    attended = weigh_keys(weights, global_kv[1], window_kv[1], remote_kv[1]).astype(jnp.bfloat16)
    grad_prob = against_keys(grad_blocks, global_kv[1], window_kv[1], remote_kv[1])
    row_delta = jnp.sum(attention_probs * grad_prob, axis=-1, keepdims=True)
    grad_score = (score_scale * attention_probs * (grad_prob - row_delta)).astype(jnp.bfloat16)
    grad_q = weigh_keys(grad_score, global_kv[0], window_kv[0], remote_kv[0]).astype(jnp.bfloat16)
    key_global, key_window, key_random = key_terms(grad_score, query_blocks)
    value_global, value_window, value_random = key_terms(weights, grad_blocks)
    row_sum = reduce_along_rows(jnp.stack([key_global, value_global]).astype(jnp.bfloat16), "seq")
    window_grad = jnp.stack([key_window, value_window]).reshape(
        2, head_count, query_count, 3, BLK, HD
    )
    no_pad = (0, 0)
    extended = (
        jnp.pad(window_grad[:, :, :, 0], (no_pad, no_pad, (0, 2), no_pad, no_pad))
        + jnp.pad(window_grad[:, :, :, 1], (no_pad, no_pad, (1, 1), no_pad, no_pad))
        + jnp.pad(window_grad[:, :, :, 2], (no_pad, no_pad, (2, 0), no_pad, no_pad))
    )
    outward = jnp.concatenate([extended[:, :, 0], extended[:, :, query_count + 1]], axis=2)
    inward = with_halo(outward.astype(jnp.bfloat16), (("seq", 2),), BLK).astype(outward.dtype)
    own_grad = extended[:, :, 1 : query_count + 1]
    own_grad = own_grad.at[:, :, 0].add(inward[:, :, :BLK])
    own_grad = own_grad.at[:, :, query_count - 1].add(inward[:, :, 3 * BLK :])
    random_terms = jnp.transpose(
        jnp.stack([key_random, value_random]).reshape(2, head_count, query_count * RAND, BLK, HD),
        (2, 0, 1, 3, 4),
    ).astype(jnp.bfloat16)

    def return_fast(random_terms, row_sum):
        global_sum = reduce_row_heads(row_sum, "seq")
        send_pick = (source[None, :] == jnp.arange(groups, dtype=jnp.int32)[:, None]).astype(
            jnp.bfloat16
        )
        outgoing = jnp.einsum(
            "pj,jxhid->pxhid", send_pick, random_terms, preferred_element_type=jnp.float32
        ).astype(jnp.bfloat16)
        incoming = lax.all_to_all(outgoing, "seq", split_axis=0, concat_axis=0, tiled=True)
        take_pick = (
            wanted_fast[None, :] == jnp.arange(2 * query_count, dtype=jnp.int32)[:, None]
        ).astype(jnp.bfloat16)
        sums = jnp.einsum("qp,pxhid->xhqid", take_pick, incoming, preferred_element_type=jnp.float32)
        back = lax.ppermute(
            sums[:, :, query_count:].astype(jnp.bfloat16),
            "seq",
            [((i + shift) % groups, i) for i in range(groups)],
        )
        return sums[:, :, :query_count] + back, global_sum

    def return_all(random_terms, row_sum):
        global_sum = reduce_row_heads(row_sum, "seq")
        send_pick = (
            places[None, :] == jnp.arange(groups * capacity, dtype=jnp.int32)[:, None]
        ).astype(jnp.bfloat16)
        outgoing = jnp.einsum(
            "pj,jxhid->pxhid", send_pick, random_terms, preferred_element_type=jnp.float32
        ).astype(jnp.bfloat16)
        incoming = lax.all_to_all(
            outgoing.reshape(groups, capacity, 2, head_count, BLK, HD),
            "seq",
            split_axis=0,
            concat_axis=0,
            tiled=True,
        )
        take_pick = (
            wanted.reshape(-1)[None, :] == jnp.arange(query_count, dtype=jnp.int32)[:, None]
        ).astype(jnp.bfloat16)
        return jnp.einsum(
            "qp,pxhid->xhqid",
            take_pick,
            incoming.reshape(groups * capacity, 2, head_count, BLK, HD),
            preferred_element_type=jnp.float32,
        ), global_sum

    random_sum, global_sum = lax.cond(take_fast, return_fast, return_all, random_terms, row_sum)
    global_sum = global_sum.reshape(2, head_count, 2, BLK, HD)
    own_grad = own_grad.at[:, :, 0:2].add(jnp.where(my_group == 0, global_sum, 0.0))
    total_grad = (own_grad + random_sum).astype(jnp.bfloat16)
    flat = (head_count, group_tokens, HD)
    results = lax.all_to_all(
        jnp.stack([by_token(attended.reshape(flat)), by_token(grad_q.reshape(flat)),
                   by_token(total_grad[0].reshape(flat)), by_token(total_grad[1].reshape(flat))]),
        "head",
        split_axis=1,
        concat_axis=2,
        tiled=True,
    )
    return results[0], results[1], results[2], results[3]


def solution(mesh):
    placed = (
        P(("seq", "head"), None),
        P(("seq", "head"), None),
        P(("seq", "head"), None),
        P(("seq", "head"), None),
        P("seq", None),
    )
    return jax.shard_map(
        shards,
        mesh=mesh,
        in_specs=placed,
        out_specs=(
            P(("seq", "head"), None),
            P(("seq", "head"), None),
            P(("seq", "head"), None),
            P(("seq", "head"), None),
        ),
        check_vma=False,
    )
```

```python
import jax
import jax.numpy as jnp
from jax import lax
from jax.sharding import PartitionSpec as P

HD = 128
BLK = 128
RAND = 3


def with_halo(cells, sides, width):
    for axis, dim in sides:
        count = lax.axis_size(axis)
        ends = count - 1
        head = lax.slice_in_dim(cells, 0, width, axis=dim)
        tail = lax.slice_in_dim(cells, cells.shape[dim] - width, cells.shape[dim], axis=dim)
        cells = jnp.concatenate(
            [
                lax.ppermute(tail, axis, [(i, (i + 1) % count) for i in range(ends)]),
                cells,
                lax.ppermute(head, axis, [((i + 1) % count, i) for i in range(ends)]),
            ],
            axis=dim,
        )
    return cells


def row_width(count):
    return 4 if count % 4 == 0 else 1


def broadcast(value, axis):
    count = lax.axis_size(axis)
    me = lax.axis_index(axis)
    width = row_width(count)
    rows = count // width
    my_row = me // width
    step = 1
    while step < rows:
        pairs = [(row * width, (row + step) * width) for row in range(step) if row + step < rows]
        got = lax.ppermute(value, axis, pairs)
        arrived = (me % width == 0) & (my_row >= step) & (my_row < 2 * step)
        value = jnp.where(arrived, got, value)
        step *= 2
    got = jnp.zeros_like(value)
    for col in range(1, width):
        pairs = [(row * width, row * width + col) for row in range(rows)]
        got = got + lax.ppermute(value, axis, pairs)
    return jnp.where(me % width == 0, value, got)


def reduce_along_rows(value, axis):
    count = lax.axis_size(axis)
    width = row_width(count)
    total = value.astype(jnp.float32)
    for col in range(1, width):
        pairs = [(row * width + col, row * width) for row in range(count // width)]
        total = total + lax.ppermute(value, axis, pairs)
    return total


def reduce_row_heads(total, axis):
    count = lax.axis_size(axis)
    width = row_width(count)
    rows = count // width
    step = 1
    while step < rows:
        pairs = [((row + step) * width, row * width) for row in range(0, rows, 2 * step) if row + step < rows]
        total = total + lax.ppermute(total.astype(jnp.bfloat16), axis, pairs)
        step *= 2
    return total


def slot_places(owners, groups, capacity):
    owner_hits = (owners[:, None] == jnp.arange(groups, dtype=jnp.int32)[None, :]).astype(jnp.int32)
    earlier = jnp.cumsum(owner_hits, axis=0) - owner_hits
    return owners * capacity + jnp.sum(earlier * owner_hits, axis=1)


def request_table(list_rows, query_count, groups, capacity):
    flat_rows = list_rows.reshape(-1)
    places = slot_places(flat_rows // query_count, groups, capacity)
    matches = places[None, :] == jnp.arange(groups * capacity, dtype=jnp.int32)[:, None]
    table = jnp.sum(jnp.where(matches, (flat_rows % query_count)[None, :], 0), axis=1)
    return table.reshape(groups, capacity)


def mirror_shift(groups):
    return groups - 1


def route(list_rows, query_count, groups, capacity):
    flat_rows = list_rows.reshape(-1)
    owners = flat_rows // query_count
    places = slot_places(owners, groups, capacity)
    rank = places - owners * capacity
    source = jnp.where(rank == 0, owners, (owners + mirror_shift(groups)) % groups)
    held_id = jnp.where(rank == 0, flat_rows % query_count, query_count + flat_rows % query_count)
    hits = (source[None, :] == jnp.arange(groups, dtype=jnp.int32)[:, None]).astype(jnp.int32)
    fits = jnp.logical_and(jnp.all(jnp.sum(hits, axis=1) <= 1), jnp.all(rank <= 1))
    fast_table = jnp.sum(hits * held_id[None, :], axis=1)
    table = jnp.concatenate(
        [
            request_table(list_rows, query_count, groups, capacity),
            fast_table[:, None],
            jnp.broadcast_to(fits.astype(jnp.int32), (groups, 1)),
        ],
        axis=1,
    )
    return table, places, source


def window_valid(my_group, query_count, groups):
    block_ids = jnp.arange(query_count, dtype=jnp.int32)
    left_ok = jnp.logical_not(jnp.logical_and(my_group == 0, block_ids == 0))
    right_ok = jnp.logical_not(
        jnp.logical_and(my_group == groups - 1, block_ids == query_count - 1)
    )
    all_true = jnp.ones((query_count, BLK), dtype=bool)
    return jnp.concatenate(
        [
            all_true,
            all_true,
            left_ok[:, None] & all_true,
            all_true,
            right_ok[:, None] & all_true,
            jnp.ones((query_count, RAND * BLK), dtype=bool),
        ],
        axis=1,
    )


def against_keys(rows, global_part, window_part, remote_part):
    return jnp.concatenate(
        [
            jnp.einsum("hqid,hjd->hqij", rows, global_part, preferred_element_type=jnp.float32),
            jnp.einsum("hqid,hqjd->hqij", rows, window_part, preferred_element_type=jnp.float32),
            jnp.einsum("hqid,hqjd->hqij", rows, remote_part, preferred_element_type=jnp.float32),
        ],
        axis=-1,
    )


def split_keys(table):
    return (table[..., : 2 * BLK], table[..., 2 * BLK : 5 * BLK], table[..., 5 * BLK :])


def weigh_keys(table, global_part, window_part, remote_part):
    global_w, window_w, random_w = split_keys(table)
    return (
        jnp.einsum("hqij,hjd->hqid", global_w, global_part, preferred_element_type=jnp.float32)
        + jnp.einsum("hqij,hqjd->hqid", window_w, window_part, preferred_element_type=jnp.float32)
        + jnp.einsum("hqij,hqjd->hqid", random_w, remote_part, preferred_element_type=jnp.float32)
    )


def key_terms(table, rows):
    global_w, window_w, random_w = split_keys(table)
    return (
        jnp.einsum("hqij,hqid->hjd", global_w, rows, preferred_element_type=jnp.float32),
        jnp.einsum("hqij,hqid->hqjd", window_w, rows, preferred_element_type=jnp.float32),
        jnp.einsum("hqij,hqid->hqjd", random_w, rows, preferred_element_type=jnp.float32),
    )


def by_head(table, head_count):
    tokens = table.shape[0]
    return jnp.transpose(table.reshape(tokens, head_count, HD), (1, 0, 2))


def by_token(table):
    head_count, tokens = table.shape[0], table.shape[1]
    return jnp.transpose(table, (1, 0, 2)).reshape(tokens, head_count * HD)


def shards(queries, keys, values, grad_out, random_blocks):
    groups = lax.axis_size("seq")
    my_group = lax.axis_index("seq")
    head_q, head_k, head_v, head_g = lax.all_to_all(
        jnp.stack([queries, keys, values, grad_out]), "head", split_axis=2, concat_axis=1, tiled=True
    )
    group_tokens = head_q.shape[0]
    head_count = head_q.shape[1] // HD
    query_count = group_tokens // BLK
    capacity = max(2, 3 * query_count * RAND // (2 * groups))
    score_scale = HD ** (-0.5)
    ordered_table, places, source = route(random_blocks, query_count, groups, capacity)
    ordered_table, head_k = lax.optimization_barrier((ordered_table, head_k))
    shift = mirror_shift(groups)
    key_value = jnp.stack([by_head(head_k, head_count), by_head(head_v, head_count)])
    kv_blocks = key_value.reshape(2, head_count, query_count, BLK, HD)
    mirror = lax.ppermute(kv_blocks, "seq", [(i, (i + shift) % groups) for i in range(groups)])
    left = lax.ppermute(
        key_value[:, :, group_tokens - BLK :], "seq", [(i, i + 1) for i in range(groups - 1)]
    )
    edged = jnp.concatenate([left, key_value, mirror[:, :, 0]], axis=2)
    edged = edged.reshape(2, head_count, query_count + 2, BLK, HD)
    window_kv = jnp.concatenate(
        [edged[:, :, 0:query_count], edged[:, :, 1 : query_count + 1], edged[:, :, 2 : query_count + 2]],
        axis=3,
    )
    global_kv = broadcast(kv_blocks[:, :, 0:2].reshape(2, head_count, 2 * BLK, HD), "seq")
    received = lax.all_to_all(ordered_table, "seq", split_axis=0, concat_axis=0, tiled=True)
    wanted = received[:, :capacity]
    wanted_fast = received[:, capacity]
    take_fast = jnp.all(received[:, capacity + 1] == 1)
    held = jnp.transpose(jnp.concatenate([kv_blocks, mirror], axis=2), (2, 0, 1, 3, 4))
    held = lax.optimization_barrier(held)

    def fetch_fast(held):
        served = jnp.take(held, wanted_fast, axis=0, mode="clip")
        fetched = lax.all_to_all(served, "seq", split_axis=0, concat_axis=0, tiled=True)
        return jnp.take(fetched, source, axis=0, mode="clip")

    def fetch_all(held):
        served = jnp.take(held[:query_count], wanted.reshape(-1), axis=0, mode="clip")
        served = served.reshape(groups, capacity, 2, head_count, BLK, HD)
        fetched = lax.all_to_all(served, "seq", split_axis=0, concat_axis=0, tiled=True)
        return jnp.take(fetched.reshape(groups * capacity, 2, head_count, BLK, HD), places, axis=0, mode="clip")

    chosen = lax.cond(take_fast, fetch_fast, fetch_all, held)
    remote_kv = jnp.transpose(
        chosen.reshape(query_count, RAND, 2, head_count, BLK, HD), (2, 3, 0, 1, 4, 5)
    ).reshape(2, head_count, query_count, RAND * BLK, HD)
    query_blocks = by_head(head_q, head_count).reshape(head_count, query_count, BLK, HD)
    grad_blocks = by_head(head_g, head_count).reshape(head_count, query_count, BLK, HD)
    scores = score_scale * against_keys(query_blocks, global_kv[0], window_kv[0], remote_kv[0])
    valid = window_valid(my_group, query_count, groups)
    scores = jnp.where(valid[None, :, None, :], scores, -jnp.inf)
    row_max = jnp.max(scores, axis=-1, keepdims=True)
    exponent = jnp.exp(scores - row_max)
    attention_probs = exponent / jnp.sum(exponent, axis=-1, keepdims=True)
    weights = attention_probs.astype(jnp.bfloat16)
    attended = weigh_keys(weights, global_kv[1], window_kv[1], remote_kv[1]).astype(jnp.bfloat16)
    grad_prob = against_keys(grad_blocks, global_kv[1], window_kv[1], remote_kv[1])
    row_delta = jnp.sum(attention_probs * grad_prob, axis=-1, keepdims=True)
    grad_score = (score_scale * attention_probs * (grad_prob - row_delta)).astype(jnp.bfloat16)
    grad_q = weigh_keys(grad_score, global_kv[0], window_kv[0], remote_kv[0]).astype(jnp.bfloat16)
    key_global, key_window, key_random = key_terms(grad_score, query_blocks)
    value_global, value_window, value_random = key_terms(weights, grad_blocks)
    row_sum = reduce_along_rows(jnp.stack([key_global, value_global]).astype(jnp.bfloat16), "seq")
    window_grad = jnp.stack([key_window, value_window]).reshape(
        2, head_count, query_count, 3, BLK, HD
    )
    no_pad = (0, 0)
    extended = (
        jnp.pad(window_grad[:, :, :, 0], (no_pad, no_pad, (0, 2), no_pad, no_pad))
        + jnp.pad(window_grad[:, :, :, 1], (no_pad, no_pad, (1, 1), no_pad, no_pad))
        + jnp.pad(window_grad[:, :, :, 2], (no_pad, no_pad, (2, 0), no_pad, no_pad))
    )
    outward = jnp.concatenate([extended[:, :, 0], extended[:, :, query_count + 1]], axis=2)
    inward = with_halo(outward.astype(jnp.bfloat16), (("seq", 2),), BLK).astype(outward.dtype)
    own_grad = extended[:, :, 1 : query_count + 1]
    own_grad = own_grad.at[:, :, 0].add(inward[:, :, :BLK])
    own_grad = own_grad.at[:, :, query_count - 1].add(inward[:, :, 3 * BLK :])
    random_terms = jnp.transpose(
        jnp.stack([key_random, value_random]).reshape(2, head_count, query_count * RAND, BLK, HD),
        (2, 0, 1, 3, 4),
    ).astype(jnp.bfloat16)

    def return_fast(random_terms, row_sum):
        global_sum = reduce_row_heads(row_sum, "seq")
        send_pick = (source[None, :] == jnp.arange(groups, dtype=jnp.int32)[:, None]).astype(
            jnp.bfloat16
        )
        outgoing = jnp.einsum(
            "pj,jxhid->pxhid", send_pick, random_terms, preferred_element_type=jnp.float32
        ).astype(jnp.bfloat16)
        incoming = lax.all_to_all(outgoing, "seq", split_axis=0, concat_axis=0, tiled=True)
        take_pick = (
            wanted_fast[None, :] == jnp.arange(2 * query_count, dtype=jnp.int32)[:, None]
        ).astype(jnp.bfloat16)
        sums = jnp.einsum("qp,pxhid->xhqid", take_pick, incoming, preferred_element_type=jnp.float32)
        back = lax.ppermute(
            sums[:, :, query_count:].astype(jnp.bfloat16),
            "seq",
            [((i + shift) % groups, i) for i in range(groups)],
        )
        return sums[:, :, :query_count] + back, global_sum

    def return_all(random_terms, row_sum):
        global_sum = reduce_row_heads(row_sum, "seq")
        send_pick = (
            places[None, :] == jnp.arange(groups * capacity, dtype=jnp.int32)[:, None]
        ).astype(jnp.bfloat16)
        outgoing = jnp.einsum(
            "pj,jxhid->pxhid", send_pick, random_terms, preferred_element_type=jnp.float32
        ).astype(jnp.bfloat16)
        incoming = lax.all_to_all(
            outgoing.reshape(groups, capacity, 2, head_count, BLK, HD),
            "seq",
            split_axis=0,
            concat_axis=0,
            tiled=True,
        )
        take_pick = (
            wanted.reshape(-1)[None, :] == jnp.arange(query_count, dtype=jnp.int32)[:, None]
        ).astype(jnp.bfloat16)
        return jnp.einsum(
            "qp,pxhid->xhqid",
            take_pick,
            incoming.reshape(groups * capacity, 2, head_count, BLK, HD),
            preferred_element_type=jnp.float32,
        ), global_sum

    random_sum, global_sum = lax.cond(take_fast, return_fast, return_all, random_terms, row_sum)
    global_sum = global_sum.reshape(2, head_count, 2, BLK, HD)
    own_grad = own_grad.at[:, :, 0:2].add(jnp.where(my_group == 0, global_sum, 0.0))
    total_grad = (own_grad + random_sum).astype(jnp.bfloat16)
    flat = (head_count, group_tokens, HD)
    results = lax.all_to_all(
        jnp.stack([by_token(attended.reshape(flat)), by_token(grad_q.reshape(flat)),
                   by_token(total_grad[0].reshape(flat)), by_token(total_grad[1].reshape(flat))]),
        "head",
        split_axis=1,
        concat_axis=2,
        tiled=True,
    )
    return results[0], results[1], results[2], results[3]


def solution(mesh):
    placed = (
        P(("seq", "head"), None),
        P(("seq", "head"), None),
        P(("seq", "head"), None),
        P(("seq", "head"), None),
        P("seq", None),
    )
    return jax.shard_map(
        shards,
        mesh=mesh,
        in_specs=placed,
        out_specs=(
            P(("seq", "head"), None),
            P(("seq", "head"), None),
            P(("seq", "head"), None),
            P(("seq", "head"), None),
        ),
        check_vma=False,
    )
```

```python
import jax
import jax.numpy as jnp
from jax import lax
from jax.sharding import PartitionSpec as P

HD = 128
BLK = 128
RAND = 3


def with_halo(cells, sides, width):
    for axis, dim in sides:
        count = lax.axis_size(axis)
        ends = count - 1
        head = lax.slice_in_dim(cells, 0, width, axis=dim)
        tail = lax.slice_in_dim(cells, cells.shape[dim] - width, cells.shape[dim], axis=dim)
        cells = jnp.concatenate(
            [
                lax.ppermute(tail, axis, [(i, (i + 1) % count) for i in range(ends)]),
                cells,
                lax.ppermute(head, axis, [((i + 1) % count, i) for i in range(ends)]),
            ],
            axis=dim,
        )
    return cells


def row_width(count):
    return 4 if count % 4 == 0 else 1


def broadcast(value, axis):
    count = lax.axis_size(axis)
    me = lax.axis_index(axis)
    width = row_width(count)
    rows = count // width
    my_row = me // width
    step = 1
    while step < rows:
        pairs = [(row * width, (row + step) * width) for row in range(step) if row + step < rows]
        got = lax.ppermute(value, axis, pairs)
        arrived = (me % width == 0) & (my_row >= step) & (my_row < 2 * step)
        value = jnp.where(arrived, got, value)
        step *= 2
    got = jnp.zeros_like(value)
    for col in range(1, width):
        pairs = [(row * width, row * width + col) for row in range(rows)]
        got = got + lax.ppermute(value, axis, pairs)
    return jnp.where(me % width == 0, value, got)


def reduce_along_rows(value, axis):
    count = lax.axis_size(axis)
    width = row_width(count)
    total = value.astype(jnp.float32)
    for col in range(1, width):
        pairs = [(row * width + col, row * width) for row in range(count // width)]
        total = total + lax.ppermute(value, axis, pairs)
    return total


def reduce_row_heads(total, axis):
    count = lax.axis_size(axis)
    width = row_width(count)
    rows = count // width
    step = 1
    while step < rows:
        pairs = [((row + step) * width, row * width) for row in range(0, rows, 2 * step) if row + step < rows]
        total = total + lax.ppermute(total.astype(jnp.bfloat16), axis, pairs)
        step *= 2
    return total


def slot_places(owners, groups, capacity):
    owner_hits = (owners[:, None] == jnp.arange(groups, dtype=jnp.int32)[None, :]).astype(jnp.int32)
    earlier = jnp.cumsum(owner_hits, axis=0) - owner_hits
    return owners * capacity + jnp.sum(earlier * owner_hits, axis=1)


def request_table(list_rows, query_count, groups, capacity):
    flat_rows = list_rows.reshape(-1)
    places = slot_places(flat_rows // query_count, groups, capacity)
    matches = places[None, :] == jnp.arange(groups * capacity, dtype=jnp.int32)[:, None]
    table = jnp.sum(jnp.where(matches, (flat_rows % query_count)[None, :], 0), axis=1)
    return table.reshape(groups, capacity)


def mirror_shift(groups):
    return groups - 1


def route(list_rows, query_count, groups, capacity):
    flat_rows = list_rows.reshape(-1)
    owners = flat_rows // query_count
    places = slot_places(owners, groups, capacity)
    rank = places - owners * capacity
    source = jnp.where(rank == 0, owners, (owners + mirror_shift(groups)) % groups)
    held_id = jnp.where(rank == 0, flat_rows % query_count, query_count + flat_rows % query_count)
    hits = (source[None, :] == jnp.arange(groups, dtype=jnp.int32)[:, None]).astype(jnp.int32)
    fits = jnp.logical_and(jnp.all(jnp.sum(hits, axis=1) <= 1), jnp.all(rank <= 1))
    fast_table = jnp.sum(hits * held_id[None, :], axis=1)
    table = jnp.concatenate(
        [
            request_table(list_rows, query_count, groups, capacity),
            fast_table[:, None],
            jnp.broadcast_to(fits.astype(jnp.int32), (groups, 1)),
        ],
        axis=1,
    )
    return table, places, source


def window_valid(my_group, query_count, groups):
    block_ids = jnp.arange(query_count, dtype=jnp.int32)
    left_ok = jnp.logical_not(jnp.logical_and(my_group == 0, block_ids == 0))
    right_ok = jnp.logical_not(
        jnp.logical_and(my_group == groups - 1, block_ids == query_count - 1)
    )
    all_true = jnp.ones((query_count, BLK), dtype=bool)
    return jnp.concatenate(
        [
            all_true,
            all_true,
            left_ok[:, None] & all_true,
            all_true,
            right_ok[:, None] & all_true,
            jnp.ones((query_count, RAND * BLK), dtype=bool),
        ],
        axis=1,
    )


def against_keys(rows, global_part, window_part, remote_part):
    return jnp.concatenate(
        [
            jnp.einsum("hqid,hjd->hqij", rows, global_part, preferred_element_type=jnp.float32),
            jnp.einsum("hqid,hqjd->hqij", rows, window_part, preferred_element_type=jnp.float32),
            jnp.einsum("hqid,hqjd->hqij", rows, remote_part, preferred_element_type=jnp.float32),
        ],
        axis=-1,
    )


def split_keys(table):
    return (table[..., : 2 * BLK], table[..., 2 * BLK : 5 * BLK], table[..., 5 * BLK :])


def weigh_keys(table, global_part, window_part, remote_part):
    global_w, window_w, random_w = split_keys(table)
    return (
        jnp.einsum("hqij,hjd->hqid", global_w, global_part, preferred_element_type=jnp.float32)
        + jnp.einsum("hqij,hqjd->hqid", window_w, window_part, preferred_element_type=jnp.float32)
        + jnp.einsum("hqij,hqjd->hqid", random_w, remote_part, preferred_element_type=jnp.float32)
    )


def key_terms(table, rows):
    global_w, window_w, random_w = split_keys(table)
    return (
        jnp.einsum("hqij,hqid->hjd", global_w, rows, preferred_element_type=jnp.float32),
        jnp.einsum("hqij,hqid->hqjd", window_w, rows, preferred_element_type=jnp.float32),
        jnp.einsum("hqij,hqid->hqjd", random_w, rows, preferred_element_type=jnp.float32),
    )


def by_head(table, head_count):
    tokens = table.shape[0]
    return jnp.transpose(table.reshape(tokens, head_count, HD), (1, 0, 2))


def by_token(table):
    head_count, tokens = table.shape[0], table.shape[1]
    return jnp.transpose(table, (1, 0, 2)).reshape(tokens, head_count * HD)


def shards(queries, keys, values, grad_out, random_blocks):
    groups = lax.axis_size("seq")
    my_group = lax.axis_index("seq")
    head_q, head_k, head_v, head_g = lax.all_to_all(
        jnp.stack([queries, keys, values, grad_out]), "head", split_axis=2, concat_axis=1, tiled=True
    )
    group_tokens = head_q.shape[0]
    head_count = head_q.shape[1] // HD
    query_count = group_tokens // BLK
    capacity = max(2, 3 * query_count * RAND // (2 * groups))
    score_scale = HD ** (-0.5)
    ordered_table, places, source = route(random_blocks, query_count, groups, capacity)
    ordered_table, head_k = lax.optimization_barrier((ordered_table, head_k))
    shift = mirror_shift(groups)
    key_value = jnp.stack([by_head(head_k, head_count), by_head(head_v, head_count)])
    kv_blocks = key_value.reshape(2, head_count, query_count, BLK, HD)
    mirror = lax.ppermute(kv_blocks, "seq", [(i, (i + shift) % groups) for i in range(groups)])
    left = lax.ppermute(
        key_value[:, :, group_tokens - BLK :], "seq", [(i, i + 1) for i in range(groups - 1)]
    )
    edged = jnp.concatenate([left, key_value, mirror[:, :, 0]], axis=2)
    edged = edged.reshape(2, head_count, query_count + 2, BLK, HD)
    window_kv = jnp.concatenate(
        [edged[:, :, 0:query_count], edged[:, :, 1 : query_count + 1], edged[:, :, 2 : query_count + 2]],
        axis=3,
    )
    global_kv = broadcast(kv_blocks[:, :, 0:2].reshape(2, head_count, 2 * BLK, HD), "seq")
    received = lax.all_to_all(ordered_table, "seq", split_axis=0, concat_axis=0, tiled=True)
    wanted = received[:, :capacity]
    wanted_fast = received[:, capacity]
    take_fast = jnp.all(received[:, capacity + 1] == 1)
    held = jnp.transpose(jnp.concatenate([kv_blocks, mirror], axis=2), (2, 0, 1, 3, 4))
    held = lax.optimization_barrier(held)

    def fetch_fast(held):
        served = jnp.take(held, wanted_fast, axis=0, mode="clip")
        fetched = lax.all_to_all(served, "seq", split_axis=0, concat_axis=0, tiled=True)
        return jnp.take(fetched, source, axis=0, mode="clip")

    def fetch_all(held):
        served = jnp.take(held[:query_count], wanted.reshape(-1), axis=0, mode="clip")
        served = served.reshape(groups, capacity, 2, head_count, BLK, HD)
        fetched = lax.all_to_all(served, "seq", split_axis=0, concat_axis=0, tiled=True)
        return jnp.take(fetched.reshape(groups * capacity, 2, head_count, BLK, HD), places, axis=0, mode="clip")

    chosen = lax.cond(take_fast, fetch_fast, fetch_all, held)
    remote_kv = jnp.transpose(
        chosen.reshape(query_count, RAND, 2, head_count, BLK, HD), (2, 3, 0, 1, 4, 5)
    ).reshape(2, head_count, query_count, RAND * BLK, HD)
    query_blocks = by_head(head_q, head_count).reshape(head_count, query_count, BLK, HD)
    grad_blocks = by_head(head_g, head_count).reshape(head_count, query_count, BLK, HD)
    scores = score_scale * against_keys(query_blocks, global_kv[0], window_kv[0], remote_kv[0])
    valid = window_valid(my_group, query_count, groups)
    scores = jnp.where(valid[None, :, None, :], scores, -jnp.inf)
    row_max = jnp.max(scores, axis=-1, keepdims=True)
    exponent = jnp.exp(scores - row_max)
    attention_probs = exponent / jnp.sum(exponent, axis=-1, keepdims=True)
    weights = attention_probs.astype(jnp.bfloat16)
    attended = weigh_keys(weights, global_kv[1], window_kv[1], remote_kv[1]).astype(jnp.bfloat16)
    grad_prob = against_keys(grad_blocks, global_kv[1], window_kv[1], remote_kv[1])
    row_delta = jnp.sum(attention_probs * grad_prob, axis=-1, keepdims=True)
    grad_score = (score_scale * attention_probs * (grad_prob - row_delta)).astype(jnp.bfloat16)
    grad_q = weigh_keys(grad_score, global_kv[0], window_kv[0], remote_kv[0]).astype(jnp.bfloat16)
    key_global, key_window, key_random = key_terms(grad_score, query_blocks)
    value_global, value_window, value_random = key_terms(weights, grad_blocks)
    row_sum = reduce_along_rows(jnp.stack([key_global, value_global]).astype(jnp.bfloat16), "seq")
    window_grad = jnp.stack([key_window, value_window]).reshape(
        2, head_count, query_count, 3, BLK, HD
    )
    no_pad = (0, 0)
    extended = (
        jnp.pad(window_grad[:, :, :, 0], (no_pad, no_pad, (0, 2), no_pad, no_pad))
        + jnp.pad(window_grad[:, :, :, 1], (no_pad, no_pad, (1, 1), no_pad, no_pad))
        + jnp.pad(window_grad[:, :, :, 2], (no_pad, no_pad, (2, 0), no_pad, no_pad))
    )
    outward = jnp.concatenate([extended[:, :, 0], extended[:, :, query_count + 1]], axis=2)
    inward = with_halo(outward.astype(jnp.bfloat16), (("seq", 2),), BLK).astype(outward.dtype)
    own_grad = extended[:, :, 1 : query_count + 1]
    edge_pad = ((0, 0), (0, 0), (0, query_count - 1), (0, 0), (0, 0))
    own_grad = own_grad + jnp.pad(inward[:, :, None, :BLK], edge_pad)
    own_grad = own_grad + jnp.pad(inward[:, :, None, 3 * BLK :], (edge_pad[0], edge_pad[1], (query_count - 1, 0), edge_pad[3], edge_pad[4]))
    random_terms = jnp.transpose(
        jnp.stack([key_random, value_random]).reshape(2, head_count, query_count * RAND, BLK, HD),
        (2, 0, 1, 3, 4),
    ).astype(jnp.bfloat16)

    def return_fast(random_terms, row_sum):
        global_sum = reduce_row_heads(row_sum, "seq")
        send_pick = (source[None, :] == jnp.arange(groups, dtype=jnp.int32)[:, None]).astype(
            jnp.bfloat16
        )
        outgoing = jnp.einsum(
            "pj,jxhid->pxhid", send_pick, random_terms, preferred_element_type=jnp.float32
        ).astype(jnp.bfloat16)
        incoming = lax.all_to_all(outgoing, "seq", split_axis=0, concat_axis=0, tiled=True)
        take_pick = (
            wanted_fast[None, :] == jnp.arange(2 * query_count, dtype=jnp.int32)[:, None]
        ).astype(jnp.bfloat16)
        sums = jnp.einsum("qp,pxhid->xhqid", take_pick, incoming, preferred_element_type=jnp.float32)
        back = lax.ppermute(
            sums[:, :, query_count:].astype(jnp.bfloat16),
            "seq",
            [((i + shift) % groups, i) for i in range(groups)],
        )
        return sums[:, :, :query_count] + back, global_sum

    def return_all(random_terms, row_sum):
        global_sum = reduce_row_heads(row_sum, "seq")
        send_pick = (
            places[None, :] == jnp.arange(groups * capacity, dtype=jnp.int32)[:, None]
        ).astype(jnp.bfloat16)
        outgoing = jnp.einsum(
            "pj,jxhid->pxhid", send_pick, random_terms, preferred_element_type=jnp.float32
        ).astype(jnp.bfloat16)
        incoming = lax.all_to_all(
            outgoing.reshape(groups, capacity, 2, head_count, BLK, HD),
            "seq",
            split_axis=0,
            concat_axis=0,
            tiled=True,
        )
        take_pick = (
            wanted.reshape(-1)[None, :] == jnp.arange(query_count, dtype=jnp.int32)[:, None]
        ).astype(jnp.bfloat16)
        return jnp.einsum(
            "qp,pxhid->xhqid",
            take_pick,
            incoming.reshape(groups * capacity, 2, head_count, BLK, HD),
            preferred_element_type=jnp.float32,
        ), global_sum

    random_sum, global_sum = lax.cond(take_fast, return_fast, return_all, random_terms, row_sum)
    global_sum = global_sum.reshape(2, head_count, 2, BLK, HD)
    own_grad = own_grad + jnp.pad(
        jnp.where(my_group == 0, global_sum, 0.0), ((0, 0), (0, 0), (0, query_count - 2), (0, 0), (0, 0))
    )
    total_grad = (own_grad + random_sum).astype(jnp.bfloat16)
    flat = (head_count, group_tokens, HD)
    results = lax.all_to_all(
        jnp.stack([by_token(attended.reshape(flat)), by_token(grad_q.reshape(flat)),
                   by_token(total_grad[0].reshape(flat)), by_token(total_grad[1].reshape(flat))]),
        "head",
        split_axis=1,
        concat_axis=2,
        tiled=True,
    )
    return results[0], results[1], results[2], results[3]


def solution(mesh):
    placed = (
        P(("seq", "head"), None),
        P(("seq", "head"), None),
        P(("seq", "head"), None),
        P(("seq", "head"), None),
        P("seq", None),
    )
    return jax.shard_map(
        shards,
        mesh=mesh,
        in_specs=placed,
        out_specs=(
            P(("seq", "head"), None),
            P(("seq", "head"), None),
            P(("seq", "head"), None),
            P(("seq", "head"), None),
        ),
        check_vma=False,
    )
```
